32 devices in a mesh: depth: 4 (over y, core), tile: 2 (over x), angle: 4 (over z).
Axes of the slice: x: 2, y: 2, z: 4, core: 2. Of those that a mesh axis runs over, the one named last changes fastest.
Arguments:
- probe: bfloat16 [2, 512, 256], P(None, 'tile'), may hold values from -5 to 5
- phase: float32 [4, 1, 512, 256], P('depth', None, 'tile'), may hold values from -1.5 to 1.5
- forward_in: float32 [4, 4, 2, 512, 256], P('depth', 'angle', None, 'tile'), may hold values from -5 to 5
- adjoint_in: float32 [4, 4, 2, 512, 256], P('depth', 'angle', None, 'tile'), may hold values from -5 to 5
- held_waves: bfloat16 [4, 2, 4, 2, 512, 256], P('depth', None, 'angle', None, 'tile'), may hold values from -5 to 5
- measured: float32 [4, 512, 256], P('angle', 'tile'), may hold values from 0.1 to 2
- tilt_index: int32 [4], P('angle'), may hold values from 0 to 60
- positions: int32 [4, 2], P('angle'), may hold values from -8 to 8
Outputs:
- forward_out: float32 [4, 4, 2, 512, 256], P('depth', 'angle', None, 'tile')
- adjoint_out: float32 [4, 4, 2, 512, 256], P('depth', 'angle', None, 'tile')
- gradient: float32 [4, 1, 2, 512, 256], P('depth', None, None, 'tile')
The draws below stay inside these ranges and needn't reach their ends.
All inputs are finite; a program needn't handle non-finite values.
Results may differ from the reference program's by a relative error of at most 0.0012.
Values sent between devices are 32-bit elements; how exact they have to be, the bound alone decides.
No kernel may reach another device: no remote copies, remote signals or barrier semaphores. Data moves between devices by JAX's collectives and lax.ppermute only.
A program may use at most 64 MiB of HBM per device.

```python
import math
import jax
import jax.numpy as jnp
from jax import lax

SLICES = 1
TILE = 256
MARGIN = 32
TILTS = 61
POSMAX = 8
PADDED = 320
FIELD_ROWS = 512
ANGLES = 4
DEPTHS = 4
N_TILE = 2


def touch_ends(entries, key, smallest, largest):
    longest = entries.shape.index(max(entries.shape))
    spots = []
    for shift in (0, 1):
        where = [jax.random.randint(jax.random.fold_in(key, axis), (), 0, length) for axis, length in enumerate(entries.shape)]
        where[longest] = (where[longest] + shift) % entries.shape[longest]
        spots.append(tuple(where))
    return entries.at[spots[0]].set(smallest).at[spots[1]].set(largest)


def levels(rng, extent, pieces, least, top_value):
    def one(dim, shards_of):
        steps = jax.random.uniform(jax.random.fold_in(jax.random.fold_in(rng, 6), dim), (shards_of,), jnp.float32, least / len(pieces), top_value / len(pieces))
        return jnp.repeat(jnp.exp(steps), extent[dim] // shards_of).reshape((-1,) + (1,) * (len(extent) - dim - 1))

    level = one(*pieces[0])
    for cut in pieces[1:]:
        level = level * one(*cut)
    return level


def gaussian(own_key, dims, scale, most, shards=(), kind=jnp.bfloat16):
    entries = scale * jax.random.normal(own_key, dims, jnp.float32)
    if shards:
        entries = entries * levels(own_key, dims, shards, -0.22, 0.18)
    return jnp.clip(entries, -most, most).astype(kind)


def setup_inputs(seed: int = 0) -> dict:
    splits = jax.random.split(jax.random.key(seed), 9)
    probe = gaussian(splits[0], (2, FIELD_ROWS, TILE), 0.7, 5.0, ((1, 2),))
    phase = jnp.clip(jax.random.uniform(splits[1], (DEPTHS, SLICES, FIELD_ROWS, TILE), jnp.float32, -1.5, 1.5) * levels(splits[1], (DEPTHS, SLICES, FIELD_ROWS, TILE), ((0, 4), (2, 2)), -0.4, 0.0), -1.5, 1.5)
    forward_in = gaussian(splits[2], (DEPTHS, ANGLES, 2, FIELD_ROWS, TILE), 0.7, 5.0, ((0, 4), (1, 4), (3, 2)), jnp.float32)
    adjoint_in = gaussian(splits[3], (DEPTHS, ANGLES, 2, FIELD_ROWS, TILE), 0.7, 5.0, ((0, 4), (1, 4), (3, 2)), jnp.float32)
    held_waves = gaussian(splits[4], (DEPTHS, SLICES + 1, ANGLES, 2, FIELD_ROWS, TILE), 0.7, 5.0, ((0, 4), (2, 4), (4, 2)))
    measured = jnp.clip(jnp.exp(math.log(2.0) - 2.9957323 * jax.random.uniform(splits[5], (ANGLES, FIELD_ROWS, TILE), jnp.float32) ** levels(splits[5], (ANGLES, FIELD_ROWS, TILE), ((0, 4), (1, 2)), -0.2, 0.2)), 0.1, 2.0)
    tilt_index = touch_ends(jax.random.randint(splits[6], (ANGLES,), 0, TILTS), jax.random.fold_in(splits[6], 1), 0, TILTS - 1).astype(jnp.int32)
    positions = touch_ends(jax.random.randint(splits[7], (ANGLES, 2), -POSMAX, POSMAX + 1), jax.random.fold_in(splits[7], 1), -POSMAX, POSMAX).astype(jnp.int32)
    return dict(probe=probe, phase=phase, forward_in=forward_in, adjoint_in=adjoint_in, held_waves=held_waves, measured=measured, tilt_index=tilt_index, positions=positions)


fresnel = 24.0
slice_step = 6.0
tilt_step = math.pi / 90.0


def to_complex(pair_arrays):
    pair_arrays = pair_arrays.astype(jnp.float32)
    return lax.complex(pair_arrays[0], pair_arrays[1]).reshape(N_TILE, TILE, TILE)


def to_pair(tile_field):
    flattened = tile_field.reshape(N_TILE * TILE, TILE)
    return jnp.stack([jnp.real(flattened), jnp.imag(flattened)]).astype(jnp.float32)


def windows(tile_field):
    image_plane = tile_field.transpose(1, 0, 2).reshape(TILE, N_TILE * TILE)
    padded = jnp.pad(image_plane, MARGIN, mode="wrap")

    def cut_window(tile_id):
        return lax.dynamic_slice(padded, (jnp.int32(0), tile_id * TILE), (PADDED, PADDED))

    return jax.vmap(cut_window)(jnp.arange(N_TILE, dtype=jnp.int32))


def propagate(tile_field, phase_plane):
    kernel = lax.complex(jnp.cos(phase_plane), jnp.sin(phase_plane))
    spectrum = jnp.fft.fft2(windows(tile_field)) * kernel[None]
    return jnp.fft.ifft2(spectrum)[:, MARGIN:MARGIN + TILE, MARGIN:MARGIN + TILE]


def spectral_phase(tilt_value, shift_pair, shifted):
    frequency = jnp.fft.fftfreq(PADDED).astype(jnp.float32)
    base_phase = -math.pi * fresnel * frequency * frequency
    tilt_angle = (tilt_value.astype(jnp.float32) - (TILTS - 1) / 2.0) * tilt_step
    lateral_drift = slice_step * jnp.tan(tilt_angle)
    shift_rows = shift_pair[0].astype(jnp.float32) * shifted
    shift_cols = lateral_drift + shift_pair[1].astype(jnp.float32) * shifted
    row_phase = base_phase - 2.0 * math.pi * frequency * shift_rows
    col_phase = base_phase - 2.0 * math.pi * frequency * shift_cols
    return row_phase[:, None] + col_phase[None, :]


def one_angle(section, wave_pair, back_pair, held_set, phase_set, tilt_value, shift_pair):
    wavefield = to_complex(wave_pair)
    transmissions = []
    for level_at in range(SLICES):
        plane_phase = phase_set[level_at].reshape(N_TILE, TILE, TILE)
        transmissions.append(lax.complex(jnp.cos(plane_phase), jnp.sin(plane_phase)))
    for level_at in range(SLICES):
        shifted = 1.0 if (section == 0 and level_at == 0) else 0.0
        wavefield = propagate(transmissions[level_at] * wavefield, spectral_phase(tilt_value, shift_pair, shifted))
    returning = to_complex(back_pair)
    gradients = [None] * SLICES
    for level_at in reversed(range(SLICES)):
        shifted = 1.0 if (section == 0 and level_at == 0) else 0.0
        spread = propagate(returning, -spectral_phase(tilt_value, shift_pair, shifted))
        held_field = to_complex(held_set[level_at])
        gradients[level_at] = to_pair(spread * jnp.conj(held_field))
        returning = jnp.conj(transmissions[level_at]) * spread
    return to_pair(wavefield), to_pair(returning), jnp.stack(gradients)


def reference(probe, phase, forward_in, adjoint_in, held_waves, measured, tilt_index, positions):
    forward_list = []
    adjoint_list = []
    gradient_list = []
    for section in range(DEPTHS):
        if section == 0:
            incoming = jnp.broadcast_to(probe.astype(jnp.float32)[None], (ANGLES, 2, N_TILE * TILE, TILE))
        else:
            incoming = forward_in[section - 1]
        if section == DEPTHS - 1:
            exit_wave = held_waves[section, SLICES].astype(jnp.float32)
            intensity = exit_wave[:, 0] * exit_wave[:, 0] + exit_wave[:, 1] * exit_wave[:, 1]
            returning = (intensity - measured)[:, None] * exit_wave
        else:
            returning = adjoint_in[section + 1]
        held_set = jnp.transpose(held_waves[section, :SLICES], (1, 0, 2, 3, 4))

        def run_angle(wave_pair, back_pair, held_one, tilt_value, shift_pair):
            return one_angle(section, wave_pair, back_pair, held_one, phase[section], tilt_value, shift_pair)

        leaving, arriving, terms = jax.vmap(run_angle)(incoming, returning, held_set, tilt_index, positions)
        forward_list.append(leaving)
        adjoint_list.append(arriving)
        gradient_list.append(jnp.sum(terms, axis=0))
    return jnp.stack(forward_list), jnp.stack(adjoint_list), jnp.stack(gradient_list)
```

```python
import math

import jax
import jax.numpy as jnp
from jax import lax
from jax.experimental import pallas as pl
from jax.experimental.pallas import tpu as pltpu
from jax.sharding import PartitionSpec as P

MARGIN = 32
TILTS = 61


fresnel = 24.0
slice_step = 6.0
tilt_step = math.pi / 90.0
highest = lax.Precision.HIGHEST
wave_precision = lax.Precision.HIGH


def padded_2(block, sides, width, periodic):
    for axis, dim in sides:
        count = lax.axis_size(axis)
        forward = [(i, i + 1) for i in range(count - 1)]
        if periodic:
            forward.append((count - 1, 0))
        backward = [(target, source) for source, target in forward]
        low = lax.ppermute(
            lax.slice_in_dim(block, block.shape[dim] - width, None, axis=dim), axis, forward
        )
        high = lax.ppermute(lax.slice_in_dim(block, 0, width, axis=dim), axis, backward)
        block = jnp.concatenate([low, block, high], axis=dim)
    return block


def contract(form, left, right):
    return jnp.einsum(form, left, right, precision=wave_precision)


def signed_freqs(length):
    ordinal = lax.iota(jnp.int32, length)
    signed = jnp.where(ordinal >= length // 2, ordinal - length, ordinal)
    return signed.astype(jnp.float32) / length


def kernel_lines(lines, length):
    ids = lax.iota(jnp.int32, length)
    angle = 2.0 * math.pi / length * (ids[:, None] * ids[None, :] % length).astype(jnp.float32)
    cos_grid = jnp.cos(angle)
    sin_grid = jnp.sin(angle)
    cos_line = jnp.cos(lines)
    sin_line = jnp.sin(lines)
    dot = lambda x, y: jnp.einsum("...f,nf->...n", x, y, precision=highest)
    real = (dot(cos_line, cos_grid) - dot(sin_line, sin_grid)) / length
    imag = (dot(sin_line, cos_grid) + dot(cos_line, sin_grid)) / length
    return real, imag


def toeplitz_kernel(q_ref, o_ref):
    count = q_ref.shape[0]
    rows, length = o_ref.shape[1], o_ref.shape[2]
    for t in range(count):
        line = jnp.broadcast_to(q_ref[t : t + 1, :], (rows, q_ref.shape[1]))
        rolled = pltpu.roll(line, MARGIN, 1, stride=1, stride_axis=0)
        o_ref[t] = rolled[:, :length]


def toeplitz(h, rows):
    count, length = h.shape
    flipped = jnp.roll(h[:, ::-1], 1, axis=-1)
    width = ((2 * length + 127) // 128) * 128
    reps = -(-width // length)
    doubled = jnp.concatenate([flipped] * reps, axis=-1)[:, :width]
    return pl.pallas_call(
        toeplitz_kernel,
        out_shape=jax.ShapeDtypeStruct((count, rows, length), jnp.float32),
    )(doubled)


def fold_rows(table, core_size):
    inner = table[..., MARGIN : MARGIN + core_size]
    top = table[..., :MARGIN]
    bottom = table[..., MARGIN + core_size :]
    zeros = jnp.zeros(inner.shape[:-1] + (core_size - MARGIN,), inner.dtype)
    return (
        inner
        + jnp.concatenate([zeros, top], axis=-1)
        + jnp.concatenate([bottom, zeros], axis=-1)
    )


def apply_operator(wave, padded_cols, row_table, col_table):
    wave_real = wave[:, 0]
    wave_imag = wave[:, 1]
    row_real = row_table[:, 0]
    row_imag = row_table[:, 1]
    first = contract("ajl,alk->ajk", row_real + row_imag, wave_real)
    second = contract("ajl,alk->ajk", row_real, wave_imag - wave_real)
    third = contract("ajl,alk->ajk", row_imag, wave_real + wave_imag)
    half = jnp.stack([first - third, first + second], axis=1)
    half = padded_cols(half)
    half_real = half[:, 0]
    half_imag = half[:, 1]
    col_real = col_table[:, 0]
    col_imag = col_table[:, 1]
    first = contract("ajk,aik->aji", half_real + half_imag, col_real)
    second = contract("ajk,aik->aji", half_real, col_imag - col_real)
    third = contract("ajk,aik->aji", half_imag, col_real + col_imag)
    return jnp.stack([first - third, first + second], axis=1)


def body(probe, phase, forward_in, adjoint_in, held_waves, measured, tilt_index, positions):
    core_size = phase.shape[-1]
    length = core_size + 2 * MARGIN
    angle_count = forward_in.shape[1]
    section = lax.axis_index("depth")
    sections = lax.axis_size("depth")
    is_first = section == 0
    frequency = signed_freqs(length)
    base_phase = -math.pi * fresnel * frequency * frequency

    tilt_angle = (tilt_index.astype(jnp.float32) - (TILTS - 1) / 2.0) * tilt_step
    lateral_drift = slice_step * jnp.tan(tilt_angle)
    shift_rows = jnp.where(is_first, positions[:, 0].astype(jnp.float32), 0.0)
    shift_cols = lateral_drift + jnp.where(is_first, positions[:, 1].astype(jnp.float32), 0.0)
    row_line = base_phase[None, :] - 2.0 * math.pi * frequency[None, :] * shift_rows[:, None]
    col_line = base_phase[None, :] - 2.0 * math.pi * frequency[None, :] * shift_cols[:, None]
    lines = jnp.stack([row_line, -row_line, col_line, -col_line], axis=1)
    h_real, h_imag = kernel_lines(lines, length)
    h_all = jnp.stack([h_real, h_imag], axis=2).reshape(angle_count * 8, length)
    tables = toeplitz(h_all, core_size).reshape(angle_count, 4, 2, core_size, length)
    rows_fwd = fold_rows(tables[:, 0], core_size)
    rows_back = fold_rows(tables[:, 1], core_size)
    cols_fwd = tables[:, 2]
    cols_back = tables[:, 3]

    cosine = jnp.cos(phase[0, 0])
    sine_part = jnp.sin(phase[0, 0])
    outgoing = jnp.concatenate([adjoint_in, forward_in], axis=0)
    received = padded_2(outgoing, (("depth", 0),), 1, False)
    probe_wave = probe.astype(jnp.float32)[None]
    wavefield = jnp.where(is_first, probe_wave, received[0])
    exit_wave = held_waves[0, 1].astype(jnp.float32)
    intensity = exit_wave[:, 0] * exit_wave[:, 0] + exit_wave[:, 1] * exit_wave[:, 1]
    residual = (intensity - measured)[:, None] * exit_wave
    returning = jnp.where(section == sections - 1, residual, received[3])
    transmitted = jnp.stack(
        [
            cosine * wavefield[:, 0] - sine_part * wavefield[:, 1],
            cosine * wavefield[:, 1] + sine_part * wavefield[:, 0],
        ],
        axis=1,
    )

    def side_halo(field):
        return padded_2(field, (("tile", 3),), MARGIN, True)

    spread = apply_operator(returning, side_halo, rows_back, cols_back)
    held_field = held_waves[0, 0].astype(jnp.float32)
    grad_real = spread[:, 0] * held_field[:, 0] + spread[:, 1] * held_field[:, 1]
    grad_imag = spread[:, 1] * held_field[:, 0] - spread[:, 0] * held_field[:, 1]
    gradient_term = jnp.stack([jnp.sum(grad_real, axis=0), jnp.sum(grad_imag, axis=0)])
    summed = lax.psum(gradient_term, "angle")
    returning = jnp.stack(
        [
            cosine * spread[:, 0] + sine_part * spread[:, 1],
            cosine * spread[:, 1] - sine_part * spread[:, 0],
        ],
        axis=1,
    )
    wavefield = apply_operator(transmitted, side_halo, rows_fwd, cols_fwd)
    return (wavefield[None], returning[None], summed[None, None])


def solution(mesh):
    in_specs = (
        P(None, "tile", None),
        P("depth", None, "tile", None),
        P("depth", "angle", None, "tile", None),
        P("depth", "angle", None, "tile", None),
        P("depth", None, "angle", None, "tile", None),
        P("angle", "tile", None),
        P("angle"),
        P("angle", None),
    )
    out_specs = (
        P("depth", "angle", None, "tile", None),
        P("depth", "angle", None, "tile", None),
        P("depth", None, None, "tile", None),
    )
    return jax.shard_map(body, mesh=mesh, in_specs=in_specs, out_specs=out_specs, check_vma=False)
```

```python
import math

import jax
import numpy as np
import jax.numpy as jnp
from jax import lax
from jax.experimental import pallas as pl
from jax.experimental.pallas import tpu as pltpu
from jax.sharding import PartitionSpec as P

MARGIN = 32
TILTS = 61


fresnel = 24.0
slice_step = 6.0
tilt_step = math.pi / 90.0
highest = lax.Precision.HIGHEST
wave_precision = lax.Precision.HIGH


def padded_2(block, sides, width, periodic):
    for axis, dim in sides:
        count = lax.axis_size(axis)
        forward = [(i, i + 1) for i in range(count - 1)]
        if periodic:
            forward.append((count - 1, 0))
        backward = [(target, source) for source, target in forward]
        low = lax.ppermute(
            lax.slice_in_dim(block, block.shape[dim] - width, None, axis=dim), axis, forward
        )
        high = lax.ppermute(lax.slice_in_dim(block, 0, width, axis=dim), axis, backward)
        block = jnp.concatenate([low, block, high], axis=dim)
    return block


def contract(form, left, right):
    return jnp.einsum(form, left, right, precision=wave_precision)


def signed_freqs(length):
    ordinal = lax.iota(jnp.int32, length)
    signed = jnp.where(ordinal >= length // 2, ordinal - length, ordinal)
    return signed.astype(jnp.float32) / length


def kernel_lines(lines, length):
    ids = np.arange(length)
    angle = 2.0 * np.pi / length * (ids[None, :] * ids[:, None] % length)
    grids = jnp.asarray(np.concatenate([np.cos(angle), np.sin(angle)], axis=1), jnp.float32)
    both = jnp.concatenate([jnp.cos(lines), jnp.sin(lines)], axis=-2)
    product = jnp.einsum("...f,fn->...n", both, grids, precision=highest)
    count = lines.shape[-2]
    cos_cos = product[..., :count, :length]
    cos_sin = product[..., :count, length:]
    sin_cos = product[..., count:, :length]
    sin_sin = product[..., count:, length:]
    return (cos_cos - sin_sin) / length, (sin_cos + cos_sin) / length


def line_allreduce(value, axis, pieces):
    count = lax.axis_size(axis)
    if count == 1:
        return value
    if count % 2:
        return lax.psum(value, axis)
    half = count // 2
    index = lax.axis_index(axis)
    chunks = jnp.split(value, pieces, axis=-2)
    done = []
    for chunk in chunks:
        total = chunk
        for step in range(half - 1):
            pairs = [(step, step + 1), (count - 1 - step, count - 2 - step)]
            total = total + lax.ppermute(total, axis, pairs)
        total = total + lax.ppermute(total, axis, [(half - 1, half), (half, half - 1)])
        for step in range(half - 1):
            pairs = [(half - 1 - step, half - 2 - step), (half + step, half + 1 + step)]
            got = lax.ppermute(total, axis, pairs)
            target = (index == half - 2 - step) | (index == half + 1 + step)
            total = jnp.where(target, got, total)
        done.append(total)
    return jnp.concatenate(done, axis=-2)


def toeplitz_kernel(q_ref, o_ref):
    count = q_ref.shape[0]
    rows, length = o_ref.shape[1], o_ref.shape[2]
    for t in range(count):
        line = jnp.broadcast_to(q_ref[t : t + 1, :], (rows, q_ref.shape[1]))
        rolled = pltpu.roll(line, MARGIN, 1, stride=1, stride_axis=0)
        o_ref[t] = rolled[:, :length]


def toeplitz(h, rows):
    count, length = h.shape
    flipped = jnp.roll(h[:, ::-1], 1, axis=-1)
    width = ((2 * length + 127) // 128) * 128
    reps = -(-width // length)
    doubled = jnp.concatenate([flipped] * reps, axis=-1)[:, :width]
    return pl.pallas_call(
        toeplitz_kernel,
        out_shape=jax.ShapeDtypeStruct((count, rows, length), jnp.float32),
    )(doubled)


def fold_rows(table, core_size):
    inner = table[..., MARGIN : MARGIN + core_size]
    top = table[..., :MARGIN]
    bottom = table[..., MARGIN + core_size :]
    zeros = jnp.zeros(inner.shape[:-1] + (core_size - MARGIN,), inner.dtype)
    return (
        inner
        + jnp.concatenate([zeros, top], axis=-1)
        + jnp.concatenate([bottom, zeros], axis=-1)
    )


def apply_operator(wave, padded_cols, row_table, col_table):
    wave_real = wave[:, 0]
    wave_imag = wave[:, 1]
    row_real = row_table[:, 0]
    row_imag = row_table[:, 1]
    first = contract("ajl,alk->ajk", row_real + row_imag, wave_real)
    second = contract("ajl,alk->ajk", row_real, wave_imag - wave_real)
    third = contract("ajl,alk->ajk", row_imag, wave_real + wave_imag)
    half = jnp.stack([first - third, first + second], axis=1)
    half = padded_cols(half)
    half_real = half[:, 0]
    half_imag = half[:, 1]
    col_real = col_table[:, 0]
    col_imag = col_table[:, 1]
    first = contract("ajk,aik->aji", half_real + half_imag, col_real)
    second = contract("ajk,aik->aji", half_real, col_imag - col_real)
    third = contract("ajk,aik->aji", half_imag, col_real + col_imag)
    return jnp.stack([first - third, first + second], axis=1)


def body(probe, phase, forward_in, adjoint_in, held_waves, measured, tilt_index, positions):
    core_size = phase.shape[-1]
    length = core_size + 2 * MARGIN
    angle_count = forward_in.shape[1]
    section = lax.axis_index("depth")
    sections = lax.axis_size("depth")
    is_first = section == 0
    frequency = signed_freqs(length)
    base_phase = -math.pi * fresnel * frequency * frequency

    tilt_angle = (tilt_index.astype(jnp.float32) - (TILTS - 1) / 2.0) * tilt_step
    lateral_drift = slice_step * jnp.tan(tilt_angle)
    shift_rows = jnp.where(is_first, positions[:, 0].astype(jnp.float32), 0.0)
    shift_cols = lateral_drift + jnp.where(is_first, positions[:, 1].astype(jnp.float32), 0.0)
    row_line = base_phase[None, :] - 2.0 * math.pi * frequency[None, :] * shift_rows[:, None]
    col_line = base_phase[None, :] - 2.0 * math.pi * frequency[None, :] * shift_cols[:, None]
    lines = jnp.stack([row_line, -row_line, col_line, -col_line], axis=1)
    h_real, h_imag = kernel_lines(lines, length)
    h_all = jnp.stack([h_real, h_imag], axis=2).reshape(angle_count * 8, length)
    tables = toeplitz(h_all, core_size).reshape(angle_count, 4, 2, core_size, length)
    rows_fwd = fold_rows(tables[:, 0], core_size)
    rows_back = fold_rows(tables[:, 1], core_size)
    cols_fwd = tables[:, 2]
    cols_back = tables[:, 3]

    cosine = jnp.cos(phase[0, 0])
    sine_part = jnp.sin(phase[0, 0])
    outgoing = jnp.concatenate([adjoint_in, forward_in], axis=0)
    received = padded_2(outgoing, (("depth", 0),), 1, False)
    probe_wave = probe.astype(jnp.float32)[None]
    wavefield = jnp.where(is_first, probe_wave, received[0])
    exit_wave = held_waves[0, 1].astype(jnp.float32)
    intensity = exit_wave[:, 0] * exit_wave[:, 0] + exit_wave[:, 1] * exit_wave[:, 1]
    residual = (intensity - measured)[:, None] * exit_wave
    returning = jnp.where(section == sections - 1, residual, received[3])
    transmitted = jnp.stack(
        [
            cosine * wavefield[:, 0] - sine_part * wavefield[:, 1],
            cosine * wavefield[:, 1] + sine_part * wavefield[:, 0],
        ],
        axis=1,
    )

    def side_halo(field):
        return padded_2(field, (("tile", 3),), MARGIN, True)

    spread = apply_operator(returning, side_halo, rows_back, cols_back)
    held_field = held_waves[0, 0].astype(jnp.float32)
    grad_real = spread[:, 0] * held_field[:, 0] + spread[:, 1] * held_field[:, 1]
    grad_imag = spread[:, 1] * held_field[:, 0] - spread[:, 0] * held_field[:, 1]
    gradient_term = jnp.stack([jnp.sum(grad_real, axis=0), jnp.sum(grad_imag, axis=0)])
    summed = line_allreduce(gradient_term, "angle", 4)
    returning = jnp.stack(
        [
            cosine * spread[:, 0] + sine_part * spread[:, 1],
            cosine * spread[:, 1] - sine_part * spread[:, 0],
        ],
        axis=1,
    )
    wavefield = apply_operator(transmitted, side_halo, rows_fwd, cols_fwd)
    return (wavefield[None], returning[None], summed[None, None])


def solution(mesh):
    in_specs = (
        P(None, "tile", None),
        P("depth", None, "tile", None),
        P("depth", "angle", None, "tile", None),
        P("depth", "angle", None, "tile", None),
        P("depth", None, "angle", None, "tile", None),
        P("angle", "tile", None),
        P("angle"),
        P("angle", None),
    )
    out_specs = (
        P("depth", "angle", None, "tile", None),
        P("depth", "angle", None, "tile", None),
        P("depth", None, None, "tile", None),
    )
    return jax.shard_map(body, mesh=mesh, in_specs=in_specs, out_specs=out_specs, check_vma=False)
```

```python
import math

import jax
import numpy as np
import jax.numpy as jnp
from jax import lax
from jax.experimental import pallas as pl
from jax.experimental.pallas import tpu as pltpu
from jax.sharding import PartitionSpec as P

MARGIN = 32
TILTS = 61


fresnel = 24.0
slice_step = 6.0
tilt_step = math.pi / 90.0
highest = lax.Precision.HIGHEST
wave_precision = lax.Precision.HIGH


def padded_2(block, sides, width, periodic):
    for axis, dim in sides:
        count = lax.axis_size(axis)
        forward = [(i, i + 1) for i in range(count - 1)]
        if periodic:
            forward.append((count - 1, 0))
        backward = [(target, source) for source, target in forward]
        low = lax.ppermute(
            lax.slice_in_dim(block, block.shape[dim] - width, None, axis=dim), axis, forward
        )
        high = lax.ppermute(lax.slice_in_dim(block, 0, width, axis=dim), axis, backward)
        block = jnp.concatenate([low, block, high], axis=dim)
    return block


def contract(form, left, right):
    return jnp.einsum(form, left, right, precision=wave_precision)


def signed_freqs(length):
    ordinal = lax.iota(jnp.int32, length)
    signed = jnp.where(ordinal >= length // 2, ordinal - length, ordinal)
    return signed.astype(jnp.float32) / length


def kernel_lines(lines, length):
    ids = np.arange(length)
    angle = 2.0 * np.pi / length * (ids[None, :] * ids[:, None] % length)
    grids = jnp.asarray(np.concatenate([np.cos(angle), np.sin(angle)], axis=1), jnp.float32)
    both = jnp.concatenate([jnp.cos(lines), jnp.sin(lines)], axis=-2)
    product = jnp.einsum("...f,fn->...n", both, grids, precision=highest)
    count = lines.shape[-2]
    cos_cos = product[..., :count, :length]
    cos_sin = product[..., :count, length:]
    sin_cos = product[..., count:, :length]
    sin_sin = product[..., count:, length:]
    return (cos_cos - sin_sin) / length, (sin_cos + cos_sin) / length


def line_allreduce(value, axis, pieces):
    count = lax.axis_size(axis)
    if count == 1:
        return value
    if count % 2:
        return lax.psum(value, axis)
    half = count // 2
    index = lax.axis_index(axis)
    chunks = jnp.split(value, pieces, axis=-2)
    done = []
    for chunk in chunks:
        total = chunk
        for step in range(half - 1):
            pairs = [(step, step + 1), (count - 1 - step, count - 2 - step)]
            total = total + lax.ppermute(total, axis, pairs)
        total = total + lax.ppermute(total, axis, [(half - 1, half), (half, half - 1)])
        for step in range(half - 1):
            pairs = [(half - 1 - step, half - 2 - step), (half + step, half + 1 + step)]
            got = lax.ppermute(total, axis, pairs)
            target = (index == half - 2 - step) | (index == half + 1 + step)
            total = jnp.where(target, got, total)
        done.append(total)
    return jnp.concatenate(done, axis=-2)


def toeplitz_kernel(q_ref, o_ref):
    count = q_ref.shape[0]
    rows, length = o_ref.shape[1], o_ref.shape[2]
    for t in range(count):
        line = jnp.broadcast_to(q_ref[t : t + 1, :], (rows, q_ref.shape[1]))
        rolled = pltpu.roll(line, MARGIN, 1, stride=1, stride_axis=0)
        o_ref[t] = rolled[:, :length]


def toeplitz(h, rows):
    count, length = h.shape
    flipped = jnp.roll(h[:, ::-1], 1, axis=-1)
    width = ((2 * length + 127) // 128) * 128
    reps = -(-width // length)
    doubled = jnp.concatenate([flipped] * reps, axis=-1)[:, :width]
    return pl.pallas_call(
        toeplitz_kernel,
        out_shape=jax.ShapeDtypeStruct((count, rows, length), jnp.float32),
    )(doubled)


def fold_rows(table, core_size):
    inner = table[..., MARGIN : MARGIN + core_size]
    top = table[..., :MARGIN]
    bottom = table[..., MARGIN + core_size :]
    zeros = jnp.zeros(inner.shape[:-1] + (core_size - MARGIN,), inner.dtype)
    return (
        inner
        + jnp.concatenate([zeros, top], axis=-1)
        + jnp.concatenate([bottom, zeros], axis=-1)
    )


def apply_rows(wave, row_table):
    wave_real = wave[:, 0]
    wave_imag = wave[:, 1]
    row_real = row_table[:, 0]
    row_imag = row_table[:, 1]
    first = contract("ajl,alk->ajk", row_real + row_imag, wave_real)
    second = contract("ajl,alk->ajk", row_real, wave_imag - wave_real)
    third = contract("ajl,alk->ajk", row_imag, wave_real + wave_imag)
    return jnp.stack([first - third, first + second], axis=1)


def apply_cols(half, col_table):
    half_real = half[:, 0]
    half_imag = half[:, 1]
    col_real = col_table[:, 0]
    col_imag = col_table[:, 1]
    first = contract("ajk,aik->aji", half_real + half_imag, col_real)
    second = contract("ajk,aik->aji", half_real, col_imag - col_real)
    third = contract("ajk,aik->aji", half_imag, col_real + col_imag)
    return jnp.stack([first - third, first + second], axis=1)


def side_halo(field, axis, dim):
    count = lax.axis_size(axis)
    if count > 2:
        return padded_2(field, ((axis, dim),), MARGIN, True)
    width = field.shape[dim]
    left = lax.slice_in_dim(field, 0, MARGIN, axis=dim)
    right = lax.slice_in_dim(field, width - MARGIN, None, axis=dim)
    edges = jnp.concatenate([left, right], axis=dim)
    if count == 2:
        edges = lax.ppermute(edges, axis, [(0, 1), (1, 0)])
    low = lax.slice_in_dim(edges, MARGIN, None, axis=dim)
    high = lax.slice_in_dim(edges, 0, MARGIN, axis=dim)
    return jnp.concatenate([low, field, high], axis=dim)


def body(probe, phase, forward_in, adjoint_in, held_waves, measured, tilt_index, positions):
    core_size = phase.shape[-1]
    length = core_size + 2 * MARGIN
    angle_count = forward_in.shape[1]
    section = lax.axis_index("depth")
    sections = lax.axis_size("depth")
    is_first = section == 0
    frequency = signed_freqs(length)
    base_phase = -math.pi * fresnel * frequency * frequency

    tilt_angle = (tilt_index.astype(jnp.float32) - (TILTS - 1) / 2.0) * tilt_step
    lateral_drift = slice_step * jnp.tan(tilt_angle)
    shift_rows = jnp.where(is_first, positions[:, 0].astype(jnp.float32), 0.0)
    shift_cols = lateral_drift + jnp.where(is_first, positions[:, 1].astype(jnp.float32), 0.0)
    row_line = base_phase[None, :] - 2.0 * math.pi * frequency[None, :] * shift_rows[:, None]
    col_line = base_phase[None, :] - 2.0 * math.pi * frequency[None, :] * shift_cols[:, None]
    lines = jnp.stack([row_line, -row_line, col_line, -col_line], axis=1)
    h_real, h_imag = kernel_lines(lines, length)
    h_all = jnp.stack([h_real, h_imag], axis=2).reshape(angle_count * 8, length)
    tables = toeplitz(h_all, core_size).reshape(angle_count, 4, 2, core_size, length)
    rows_fwd = fold_rows(tables[:, 0], core_size)
    rows_back = fold_rows(tables[:, 1], core_size)
    cols_fwd = tables[:, 2]
    cols_back = tables[:, 3]

    cosine = jnp.cos(phase[0, 0])
    sine_part = jnp.sin(phase[0, 0])
    outgoing = jnp.concatenate([adjoint_in, forward_in], axis=0)
    received = padded_2(outgoing, (("depth", 0),), 1, False)
    probe_wave = probe.astype(jnp.float32)[None]
    wavefield = jnp.where(is_first, probe_wave, received[0])
    exit_wave = held_waves[0, 1].astype(jnp.float32)
    intensity = exit_wave[:, 0] * exit_wave[:, 0] + exit_wave[:, 1] * exit_wave[:, 1]
    residual = (intensity - measured)[:, None] * exit_wave
    returning = jnp.where(section == sections - 1, residual, received[3])
    transmitted = jnp.stack(
        [
            cosine * wavefield[:, 0] - sine_part * wavefield[:, 1],
            cosine * wavefield[:, 1] + sine_part * wavefield[:, 0],
        ],
        axis=1,
    )

    halves = jnp.concatenate(
        [apply_rows(returning, rows_back), apply_rows(transmitted, rows_fwd)], axis=1
    )
    halves = side_halo(halves, "tile", 3)
    spread = apply_cols(halves[:, :2], cols_back)
    held_field = held_waves[0, 0].astype(jnp.float32)
    grad_real = spread[:, 0] * held_field[:, 0] + spread[:, 1] * held_field[:, 1]
    grad_imag = spread[:, 1] * held_field[:, 0] - spread[:, 0] * held_field[:, 1]
    gradient_term = jnp.stack([jnp.sum(grad_real, axis=0), jnp.sum(grad_imag, axis=0)])
    summed = line_allreduce(gradient_term, "angle", 2)
    returning = jnp.stack(
        [
            cosine * spread[:, 0] + sine_part * spread[:, 1],
            cosine * spread[:, 1] - sine_part * spread[:, 0],
        ],
        axis=1,
    )
    wavefield = apply_cols(halves[:, 2:], cols_fwd)
    return (wavefield[None], returning[None], summed[None, None])


def solution(mesh):
    in_specs = (
        P(None, "tile", None),
        P("depth", None, "tile", None),
        P("depth", "angle", None, "tile", None),
        P("depth", "angle", None, "tile", None),
        P("depth", None, "angle", None, "tile", None),
        P("angle", "tile", None),
        P("angle"),
        P("angle", None),
    )
    out_specs = (
        P("depth", "angle", None, "tile", None),
        P("depth", "angle", None, "tile", None),
        P("depth", None, None, "tile", None),
    )
    return jax.shard_map(body, mesh=mesh, in_specs=in_specs, out_specs=out_specs, check_vma=False)
```

```python
import math

import jax
import numpy as np
import jax.numpy as jnp
from jax import lax
from jax.experimental import pallas as pl
from jax.experimental.pallas import tpu as pltpu
from jax.sharding import PartitionSpec as P

MARGIN = 32
TILTS = 61


fresnel = 24.0
slice_step = 6.0
tilt_step = math.pi / 90.0
highest = lax.Precision.HIGHEST
wave_precision = lax.Precision.HIGH


def padded_2(block, sides, width, periodic):
    for axis, dim in sides:
        count = lax.axis_size(axis)
        forward = [(i, i + 1) for i in range(count - 1)]
        if periodic:
            forward.append((count - 1, 0))
        backward = [(target, source) for source, target in forward]
        low = lax.ppermute(
            lax.slice_in_dim(block, block.shape[dim] - width, None, axis=dim), axis, forward
        )
        high = lax.ppermute(lax.slice_in_dim(block, 0, width, axis=dim), axis, backward)
        block = jnp.concatenate([low, block, high], axis=dim)
    return block


def contract(form, left, right):
    return jnp.einsum(form, left, right, precision=wave_precision)


def signed_freqs(length):
    ordinal = lax.iota(jnp.int32, length)
    signed = jnp.where(ordinal >= length // 2, ordinal - length, ordinal)
    return signed.astype(jnp.float32) / length


def kernel_lines(lines, length):
    ids = np.arange(length)
    angle = 2.0 * np.pi / length * (ids[None, :] * ids[:, None] % length)
    grids = jnp.asarray(np.concatenate([np.cos(angle), np.sin(angle)], axis=1), jnp.float32)
    both = jnp.concatenate([jnp.cos(lines), jnp.sin(lines)], axis=-2)
    product = jnp.einsum("...f,fn->...n", both, grids, precision=highest)
    count = lines.shape[-2]
    cos_cos = product[..., :count, :length]
    cos_sin = product[..., :count, length:]
    sin_cos = product[..., count:, :length]
    sin_sin = product[..., count:, length:]
    return (cos_cos - sin_sin) / length, (sin_cos + cos_sin) / length


def line_allreduce(value, axis, pieces):
    count = lax.axis_size(axis)
    if count == 1:
        return value
    if count % 2:
        return lax.psum(value, axis)
    half = count // 2
    index = lax.axis_index(axis)
    chunks = jnp.split(value, pieces, axis=-2)
    done = []
    for chunk in chunks:
        total = chunk
        for step in range(half - 1):
            pairs = [(step, step + 1), (count - 1 - step, count - 2 - step)]
            total = total + lax.ppermute(total, axis, pairs)
        total = total + lax.ppermute(total, axis, [(half - 1, half), (half, half - 1)])
        for step in range(half - 1):
            pairs = [(half - 1 - step, half - 2 - step), (half + step, half + 1 + step)]
            got = lax.ppermute(total, axis, pairs)
            target = (index == half - 2 - step) | (index == half + 1 + step)
            total = jnp.where(target, got, total)
        done.append(total)
    return jnp.concatenate(done, axis=-2)


def toeplitz_kernel(q_ref, o_ref):
    count = q_ref.shape[0]
    rows, length = o_ref.shape[1], o_ref.shape[2]
    for t in range(count):
        line = jnp.broadcast_to(q_ref[t : t + 1, :], (rows, q_ref.shape[1]))
        rolled = pltpu.roll(line, MARGIN, 1, stride=1, stride_axis=0)
        o_ref[t] = rolled[:, :length]


def toeplitz(h, rows):
    count, length = h.shape
    flipped = jnp.roll(h[:, ::-1], 1, axis=-1)
    width = ((2 * length + 127) // 128) * 128
    reps = -(-width // length)
    doubled = jnp.concatenate([flipped] * reps, axis=-1)[:, :width]
    return pl.pallas_call(
        toeplitz_kernel,
        out_shape=jax.ShapeDtypeStruct((count, rows, length), jnp.float32),
    )(doubled)


def fold_rows(table, core_size):
    inner = table[..., MARGIN : MARGIN + core_size]
    top = table[..., :MARGIN]
    bottom = table[..., MARGIN + core_size :]
    zeros = jnp.zeros(inner.shape[:-1] + (core_size - MARGIN,), inner.dtype)
    return (
        inner
        + jnp.concatenate([zeros, top], axis=-1)
        + jnp.concatenate([bottom, zeros], axis=-1)
    )


def apply_operator(wave, padded_cols, row_table, col_table):
    wave_real = wave[:, 0]
    wave_imag = wave[:, 1]
    row_real = row_table[:, 0]
    row_imag = row_table[:, 1]
    first = contract("ajl,alk->ajk", row_real + row_imag, wave_real)
    second = contract("ajl,alk->ajk", row_real, wave_imag - wave_real)
    third = contract("ajl,alk->ajk", row_imag, wave_real + wave_imag)
    half = jnp.stack([first - third, first + second], axis=1)
    half = padded_cols(half)
    half_real = half[:, 0]
    half_imag = half[:, 1]
    col_real = col_table[:, 0]
    col_imag = col_table[:, 1]
    first = contract("ajk,aik->aji", half_real + half_imag, col_real)
    second = contract("ajk,aik->aji", half_real, col_imag - col_real)
    third = contract("ajk,aik->aji", half_imag, col_real + col_imag)
    return jnp.stack([first - third, first + second], axis=1)


def body(probe, phase, forward_in, adjoint_in, held_waves, measured, tilt_index, positions):
    core_size = phase.shape[-1]
    length = core_size + 2 * MARGIN
    angle_count = forward_in.shape[1]
    section = lax.axis_index("depth")
    sections = lax.axis_size("depth")
    is_first = section == 0
    frequency = signed_freqs(length)
    base_phase = -math.pi * fresnel * frequency * frequency

    tilt_angle = (tilt_index.astype(jnp.float32) - (TILTS - 1) / 2.0) * tilt_step
    lateral_drift = slice_step * jnp.tan(tilt_angle)
    shift_rows = jnp.where(is_first, positions[:, 0].astype(jnp.float32), 0.0)
    shift_cols = lateral_drift + jnp.where(is_first, positions[:, 1].astype(jnp.float32), 0.0)
    row_line = base_phase[None, :] - 2.0 * math.pi * frequency[None, :] * shift_rows[:, None]
    col_line = base_phase[None, :] - 2.0 * math.pi * frequency[None, :] * shift_cols[:, None]
    lines = jnp.stack([row_line, -row_line, col_line, -col_line], axis=1)
    h_real, h_imag = kernel_lines(lines, length)
    h_all = jnp.stack([h_real, h_imag], axis=2)

    def build(which):
        picked = jnp.stack([h_all[:, i] for i in which], axis=1).reshape(angle_count * 4, length)
        return toeplitz(picked, core_size).reshape(angle_count, 2, 2, core_size, length)

    back_tables = build((1, 3))
    rows_back = fold_rows(back_tables[:, 0], core_size)
    cols_back = back_tables[:, 1]

    cosine = jnp.cos(phase[0, 0])
    sine_part = jnp.sin(phase[0, 0])
    outgoing = jnp.concatenate([adjoint_in, forward_in], axis=0)
    received = padded_2(outgoing, (("depth", 0),), 1, False)
    probe_wave = probe.astype(jnp.float32)[None]
    wavefield = jnp.where(is_first, probe_wave, received[0])
    exit_wave = held_waves[0, 1].astype(jnp.float32)
    intensity = exit_wave[:, 0] * exit_wave[:, 0] + exit_wave[:, 1] * exit_wave[:, 1]
    residual = (intensity - measured)[:, None] * exit_wave
    returning = jnp.where(section == sections - 1, residual, received[3])
    def side_halo(field):
        return padded_2(field, (("tile", 3),), MARGIN, True)

    spread = apply_operator(returning, side_halo, rows_back, cols_back)
    held_field = held_waves[0, 0].astype(jnp.float32)
    grad_real = spread[:, 0] * held_field[:, 0] + spread[:, 1] * held_field[:, 1]
    grad_imag = spread[:, 1] * held_field[:, 0] - spread[:, 0] * held_field[:, 1]
    gradient_term = jnp.stack([jnp.sum(grad_real, axis=0), jnp.sum(grad_imag, axis=0)])
    gradient_term, cosine, sine_part, h_all = lax.optimization_barrier(
        (gradient_term, cosine, sine_part, h_all)
    )
    summed = line_allreduce(gradient_term, "angle", 4)
    returning = jnp.stack(
        [
            cosine * spread[:, 0] + sine_part * spread[:, 1],
            cosine * spread[:, 1] - sine_part * spread[:, 0],
        ],
        axis=1,
    )
    transmitted = jnp.stack(
        [
            cosine * wavefield[:, 0] - sine_part * wavefield[:, 1],
            cosine * wavefield[:, 1] + sine_part * wavefield[:, 0],
        ],
        axis=1,
    )
    fwd_tables = build((0, 2))
    rows_fwd = fold_rows(fwd_tables[:, 0], core_size)
    cols_fwd = fwd_tables[:, 1]
    wavefield = apply_operator(transmitted, side_halo, rows_fwd, cols_fwd)
    return (wavefield[None], returning[None], summed[None, None])


def solution(mesh):
    in_specs = (
        P(None, "tile", None),
        P("depth", None, "tile", None),
        P("depth", "angle", None, "tile", None),
        P("depth", "angle", None, "tile", None),
        P("depth", None, "angle", None, "tile", None),
        P("angle", "tile", None),
        P("angle"),
        P("angle", None),
    )
    out_specs = (
        P("depth", "angle", None, "tile", None),
        P("depth", "angle", None, "tile", None),
        P("depth", None, None, "tile", None),
    )
    return jax.shard_map(body, mesh=mesh, in_specs=in_specs, out_specs=out_specs, check_vma=False)
```

```python
import math

import jax
import numpy as np
import jax.numpy as jnp
from jax import lax
from jax.experimental import pallas as pl
from jax.experimental.pallas import tpu as pltpu
from jax.sharding import PartitionSpec as P

MARGIN = 32
TILTS = 61


fresnel = 24.0
slice_step = 6.0
tilt_step = math.pi / 90.0
highest = lax.Precision.HIGHEST
wave_precision = lax.Precision.HIGH


def padded_2(block, sides, width, periodic):
    for axis, dim in sides:
        count = lax.axis_size(axis)
        forward = [(i, i + 1) for i in range(count - 1)]
        if periodic:
            forward.append((count - 1, 0))
        backward = [(target, source) for source, target in forward]
        low = lax.ppermute(
            lax.slice_in_dim(block, block.shape[dim] - width, None, axis=dim), axis, forward
        )
        high = lax.ppermute(lax.slice_in_dim(block, 0, width, axis=dim), axis, backward)
        block = jnp.concatenate([low, block, high], axis=dim)
    return block


def contract(form, left, right):
    return jnp.einsum(form, left, right, precision=wave_precision)


def signed_freqs(length):
    ordinal = lax.iota(jnp.int32, length)
    signed = jnp.where(ordinal >= length // 2, ordinal - length, ordinal)
    return signed.astype(jnp.float32) / length


def line_allreduce(value, axis, pieces):
    count = lax.axis_size(axis)
    if count == 1:
        return value
    if count % 2:
        return lax.psum(value, axis)
    half = count // 2
    index = lax.axis_index(axis)
    chunks = jnp.split(value, pieces, axis=-2)
    done = []
    for chunk in chunks:
        total = chunk
        for step in range(half - 1):
            pairs = [(step, step + 1), (count - 1 - step, count - 2 - step)]
            total = total + lax.ppermute(total, axis, pairs)
        total = total + lax.ppermute(total, axis, [(half - 1, half), (half, half - 1)])
        for step in range(half - 1):
            pairs = [(half - 1 - step, half - 2 - step), (half + step, half + 1 + step)]
            got = lax.ppermute(total, axis, pairs)
            target = (index == half - 2 - step) | (index == half + 1 + step)
            total = jnp.where(target, got, total)
        done.append(total)
    return jnp.concatenate(done, axis=-2)


def table_kernel(both_ref, grid_ref, rows_ref, cols_ref):
    angle_count, doubled = both_ref.shape[0], both_ref.shape[1]
    count = doubled // 2
    length = both_ref.shape[2]
    core_size = rows_ref.shape[-1]
    width = grid_ref.shape[1] // 2
    column = lax.broadcasted_iota(jnp.int32, (core_size, core_size), 1)
    low_mask = column >= core_size - MARGIN
    high_mask = column < MARGIN
    for a in range(angle_count):
        product = jnp.dot(
            both_ref[a], grid_ref[...], precision=highest, preferred_element_type=jnp.float32
        )
        cos_cos = product[:count, :width]
        cos_sin = product[:count, width:]
        sin_cos = product[count:, :width]
        sin_sin = product[count:, width:]
        q_real = (cos_cos + sin_sin) * (1.0 / length)
        q_imag = (sin_cos - cos_sin) * (1.0 / length)

        def rolled(line, shift):
            wide = jnp.broadcast_to(line, (core_size, width))
            return pltpu.roll(wide, shift, 1, stride=1, stride_axis=0)

        for t in range(count):
            parts = []
            for q in (q_real, q_imag):
                line = q[t : t + 1, :]
                if t < 2:
                    inner = rolled(line, 0)[:, :core_size]
                    low = rolled(line, core_size)[:, :core_size]
                    high = rolled(line, width - core_size)[:, :core_size]
                    folded = inner + jnp.where(low_mask, low, 0.0) + jnp.where(high_mask, high, 0.0)
                    parts.append(folded)
                else:
                    parts.append(rolled(line, MARGIN)[:, :length])
            real, imag = parts
            if t < 2:
                rows_ref[a, t, 0] = real + imag
                rows_ref[a, t, 1] = real
                rows_ref[a, t, 2] = imag
            else:
                cols_ref[a, t - 2, 0] = real
                cols_ref[a, t - 2, 1] = imag - real
                cols_ref[a, t - 2, 2] = real + imag


def build_tables(lines, core_size):
    angle_count, count, length = lines.shape
    width = ((2 * length + 127) // 128) * 128
    ids = np.arange(length)[:, None] * np.arange(width)[None, :] % length
    angle = 2.0 * np.pi / length * ids
    grid = jnp.asarray(np.concatenate([np.cos(angle), np.sin(angle)], axis=1), jnp.float32)
    both = jnp.concatenate([jnp.cos(lines), jnp.sin(lines)], axis=1)
    return pl.pallas_call(
        table_kernel,
        out_shape=(
            jax.ShapeDtypeStruct((angle_count, 2, 3, core_size, core_size), jnp.float32),
            jax.ShapeDtypeStruct((angle_count, 2, 3, core_size, length), jnp.float32),
        ),
    )(both, grid)


def apply_operator(wave, padded_cols, row_table, col_table):
    wave_real = wave[:, 0]
    wave_imag = wave[:, 1]
    first = contract("ajl,alk->ajk", row_table[:, 0], wave_real)
    second = contract("ajl,alk->ajk", row_table[:, 1], wave_imag - wave_real)
    third = contract("ajl,alk->ajk", row_table[:, 2], wave_real + wave_imag)
    half = jnp.stack([first - third, first + second], axis=1)
    half = padded_cols(half)
    half_real = half[:, 0]
    half_imag = half[:, 1]
    first = contract("ajk,aik->aji", half_real + half_imag, col_table[:, 0])
    second = contract("ajk,aik->aji", half_real, col_table[:, 1])
    third = contract("ajk,aik->aji", half_imag, col_table[:, 2])
    return jnp.stack([first - third, first + second], axis=1)


def body(probe, phase, forward_in, adjoint_in, held_waves, measured, tilt_index, positions):
    core_size = phase.shape[-1]
    length = core_size + 2 * MARGIN
    angle_count = forward_in.shape[1]
    section = lax.axis_index("depth")
    sections = lax.axis_size("depth")
    is_first = section == 0
    frequency = signed_freqs(length)
    base_phase = -math.pi * fresnel * frequency * frequency

    tilt_angle = (tilt_index.astype(jnp.float32) - (TILTS - 1) / 2.0) * tilt_step
    lateral_drift = slice_step * jnp.tan(tilt_angle)
    shift_rows = jnp.where(is_first, positions[:, 0].astype(jnp.float32), 0.0)
    shift_cols = lateral_drift + jnp.where(is_first, positions[:, 1].astype(jnp.float32), 0.0)
    row_line = base_phase[None, :] - 2.0 * math.pi * frequency[None, :] * shift_rows[:, None]
    col_line = base_phase[None, :] - 2.0 * math.pi * frequency[None, :] * shift_cols[:, None]
    lines = jnp.stack([row_line, -row_line, col_line, -col_line], axis=1)
    row_tables, col_tables = build_tables(lines, core_size)
    rows_fwd = row_tables[:, 0]
    rows_back = row_tables[:, 1]
    cols_fwd = col_tables[:, 0]
    cols_back = col_tables[:, 1]

    cosine = jnp.cos(phase[0, 0])
    sine_part = jnp.sin(phase[0, 0])
    outgoing = jnp.concatenate([adjoint_in, forward_in], axis=0)
    received = padded_2(outgoing, (("depth", 0),), 1, False)
    probe_wave = probe.astype(jnp.float32)[None]
    wavefield = jnp.where(is_first, probe_wave, received[0])
    exit_wave = held_waves[0, 1].astype(jnp.float32)
    intensity = exit_wave[:, 0] * exit_wave[:, 0] + exit_wave[:, 1] * exit_wave[:, 1]
    residual = (intensity - measured)[:, None] * exit_wave
    returning = jnp.where(section == sections - 1, residual, received[3])
    transmitted = jnp.stack(
        [
            cosine * wavefield[:, 0] - sine_part * wavefield[:, 1],
            cosine * wavefield[:, 1] + sine_part * wavefield[:, 0],
        ],
        axis=1,
    )

    def side_halo(field):
        return padded_2(field, (("tile", 3),), MARGIN, True)

    spread = apply_operator(returning, side_halo, rows_back, cols_back)
    held_field = held_waves[0, 0].astype(jnp.float32)
    grad_real = spread[:, 0] * held_field[:, 0] + spread[:, 1] * held_field[:, 1]
    grad_imag = spread[:, 1] * held_field[:, 0] - spread[:, 0] * held_field[:, 1]
    gradient_term = jnp.stack([jnp.sum(grad_real, axis=0), jnp.sum(grad_imag, axis=0)])
    summed = line_allreduce(gradient_term, "angle", 4)
    returning = jnp.stack(
        [
            cosine * spread[:, 0] + sine_part * spread[:, 1],
            cosine * spread[:, 1] - sine_part * spread[:, 0],
        ],
        axis=1,
    )
    wavefield = apply_operator(transmitted, side_halo, rows_fwd, cols_fwd)
    return (wavefield[None], returning[None], summed[None, None])


def solution(mesh):
    in_specs = (
        P(None, "tile", None),
        P("depth", None, "tile", None),
        P("depth", "angle", None, "tile", None),
        P("depth", "angle", None, "tile", None),
        P("depth", None, "angle", None, "tile", None),
        P("angle", "tile", None),
        P("angle"),
        P("angle", None),
    )
    out_specs = (
        P("depth", "angle", None, "tile", None),
        P("depth", "angle", None, "tile", None),
        P("depth", None, None, "tile", None),
    )
    return jax.shard_map(body, mesh=mesh, in_specs=in_specs, out_specs=out_specs, check_vma=False)
```

```python
import math

import jax
import numpy as np
import jax.numpy as jnp
from jax import lax
from jax.experimental import pallas as pl
from jax.experimental.pallas import tpu as pltpu
from jax.sharding import PartitionSpec as P

MARGIN = 32
TILTS = 61


fresnel = 24.0
slice_step = 6.0
tilt_step = math.pi / 90.0
highest = lax.Precision.HIGHEST
wave_precision = lax.Precision.HIGH


def padded_2(block, sides, width, periodic):
    for axis, dim in sides:
        count = lax.axis_size(axis)
        forward = [(i, i + 1) for i in range(count - 1)]
        if periodic:
            forward.append((count - 1, 0))
        backward = [(target, source) for source, target in forward]
        low = lax.ppermute(
            lax.slice_in_dim(block, block.shape[dim] - width, None, axis=dim), axis, forward
        )
        high = lax.ppermute(lax.slice_in_dim(block, 0, width, axis=dim), axis, backward)
        block = jnp.concatenate([low, block, high], axis=dim)
    return block


def contract(form, left, right):
    return jnp.einsum(form, left, right, precision=wave_precision)


def signed_freqs(length):
    ordinal = lax.iota(jnp.int32, length)
    signed = jnp.where(ordinal >= length // 2, ordinal - length, ordinal)
    return signed.astype(jnp.float32) / length


def line_allreduce(value, axis, pieces):
    count = lax.axis_size(axis)
    if count == 1:
        return value
    if count % 2 or count > 8:
        return lax.psum(value, axis)
    half = count // 2
    index = lax.axis_index(axis)
    chunks = jnp.split(value, pieces, axis=-2)
    zero = jnp.zeros_like(chunks[0])

    def own(c):
        return chunks[c] if 0 <= c < pieces else zero

    def by_role(candidates):
        picked = candidates[-1]
        for role in range(count - 2, -1, -1):
            picked = jnp.where(index == role, candidates[role], picked)
        return picked

    from_left = []
    from_right = []

    def got(buffers, t):
        return buffers[t] if t >= 0 else zero

    right_pairs = [(j, j + 1) for j in range(count - 1)]
    left_pairs = [(j + 1, j) for j in range(count - 1)]
    for t in range(pieces + count - 2):
        rightward = []
        leftward = []
        for role in range(count):
            c = t - role
            if role < half:
                rightward.append(own(c) + got(from_left, t - 1))
            elif role == half:
                rightward.append(got(from_left, t - 1) + (own(c) + got(from_right, t - 2)))
            else:
                rightward.append(got(from_left, t - 1))
            c = t - (count - 1 - role)
            if role >= half:
                leftward.append(own(c) + got(from_right, t - 1))
            elif role == half - 1:
                leftward.append((own(c) + got(from_left, t - 2)) + got(from_right, t - 1))
            else:
                leftward.append(got(from_right, t - 1))
        from_left.append(lax.ppermute(by_role(rightward), axis, right_pairs))
        from_right.append(lax.ppermute(by_role(leftward), axis, left_pairs))
    done = []
    for c in range(pieces):
        finals = []
        for role in range(count):
            if role < half - 1:
                finals.append(got(from_right, c + count - 2 - role))
            elif role == half - 1:
                finals.append(
                    (own(c) + got(from_left, c + half - 2)) + got(from_right, c + half - 1)
                )
            elif role == half:
                finals.append(
                    got(from_left, c + half - 1) + (own(c) + got(from_right, c + half - 2))
                )
            else:
                finals.append(got(from_left, c + role - 1))
        done.append(by_role(finals))
    return jnp.concatenate(done, axis=-2)


def table_kernel(both_ref, grid_ref, rows_ref, cols_ref):
    angle_count, doubled = both_ref.shape[0], both_ref.shape[1]
    count = doubled // 2
    length = both_ref.shape[2]
    core_size = rows_ref.shape[-1]
    width = grid_ref.shape[1] // 2
    column = lax.broadcasted_iota(jnp.int32, (core_size, core_size), 1)
    low_mask = column >= core_size - MARGIN
    high_mask = column < MARGIN
    for a in range(angle_count):
        product = jnp.dot(
            both_ref[a], grid_ref[...], precision=highest, preferred_element_type=jnp.float32
        )
        cos_cos = product[:count, :width]
        cos_sin = product[:count, width:]
        sin_cos = product[count:, :width]
        sin_sin = product[count:, width:]
        q_real = (cos_cos + sin_sin) * (1.0 / length)
        q_imag = (sin_cos - cos_sin) * (1.0 / length)

        def rolled(line, shift):
            wide = jnp.broadcast_to(line, (core_size, width))
            return pltpu.roll(wide, shift, 1, stride=1, stride_axis=0)

        for t in range(count):
            parts = []
            for q in (q_real, q_imag):
                line = q[t : t + 1, :]
                if t < 2:
                    inner = rolled(line, 0)[:, :core_size]
                    low = rolled(line, core_size)[:, :core_size]
                    high = rolled(line, width - core_size)[:, :core_size]
                    folded = inner + jnp.where(low_mask, low, 0.0) + jnp.where(high_mask, high, 0.0)
                    parts.append(folded)
                else:
                    parts.append(rolled(line, MARGIN)[:, :length])
            real, imag = parts
            if t < 2:
                rows_ref[a, t, 0] = real + imag
                rows_ref[a, t, 1] = real
                rows_ref[a, t, 2] = imag
            else:
                cols_ref[a, t - 2, 0] = real
                cols_ref[a, t - 2, 1] = imag - real
                cols_ref[a, t - 2, 2] = real + imag


def build_tables(lines, core_size):
    angle_count, count, length = lines.shape
    width = ((2 * length + 127) // 128) * 128
    ids = np.arange(length)[:, None] * np.arange(width)[None, :] % length
    angle = 2.0 * np.pi / length * ids
    grid = jnp.asarray(np.concatenate([np.cos(angle), np.sin(angle)], axis=1), jnp.float32)
    both = jnp.concatenate([jnp.cos(lines), jnp.sin(lines)], axis=1)
    return pl.pallas_call(
        table_kernel,
        out_shape=(
            jax.ShapeDtypeStruct((angle_count, 2, 3, core_size, core_size), jnp.float32),
            jax.ShapeDtypeStruct((angle_count, 2, 3, core_size, length), jnp.float32),
        ),
    )(both, grid)


def apply_operator(wave, padded_cols, row_table, col_table):
    wave_real = wave[:, 0]
    wave_imag = wave[:, 1]
    first = contract("ajl,alk->ajk", row_table[:, 0], wave_real)
    second = contract("ajl,alk->ajk", row_table[:, 1], wave_imag - wave_real)
    third = contract("ajl,alk->ajk", row_table[:, 2], wave_real + wave_imag)
    half = jnp.stack([first - third, first + second], axis=1)
    half = padded_cols(half)
    half_real = half[:, 0]
    half_imag = half[:, 1]
    first = contract("ajk,aik->aji", half_real + half_imag, col_table[:, 0])
    second = contract("ajk,aik->aji", half_real, col_table[:, 1])
    third = contract("ajk,aik->aji", half_imag, col_table[:, 2])
    return jnp.stack([first - third, first + second], axis=1)


def body(probe, phase, forward_in, adjoint_in, held_waves, measured, tilt_index, positions):
    core_size = phase.shape[-1]
    length = core_size + 2 * MARGIN
    angle_count = forward_in.shape[1]
    section = lax.axis_index("depth")
    sections = lax.axis_size("depth")
    is_first = section == 0
    frequency = signed_freqs(length)
    base_phase = -math.pi * fresnel * frequency * frequency

    tilt_angle = (tilt_index.astype(jnp.float32) - (TILTS - 1) / 2.0) * tilt_step
    lateral_drift = slice_step * jnp.tan(tilt_angle)
    shift_rows = jnp.where(is_first, positions[:, 0].astype(jnp.float32), 0.0)
    shift_cols = lateral_drift + jnp.where(is_first, positions[:, 1].astype(jnp.float32), 0.0)
    row_line = base_phase[None, :] - 2.0 * math.pi * frequency[None, :] * shift_rows[:, None]
    col_line = base_phase[None, :] - 2.0 * math.pi * frequency[None, :] * shift_cols[:, None]
    lines = jnp.stack([row_line, -row_line, col_line, -col_line], axis=1)
    row_tables, col_tables = build_tables(lines, core_size)
    rows_fwd = row_tables[:, 0]
    rows_back = row_tables[:, 1]
    cols_fwd = col_tables[:, 0]
    cols_back = col_tables[:, 1]

    cosine = jnp.cos(phase[0, 0])
    sine_part = jnp.sin(phase[0, 0])
    outgoing = jnp.concatenate([adjoint_in, forward_in], axis=0)
    received = padded_2(outgoing, (("depth", 0),), 1, False)
    probe_wave = probe.astype(jnp.float32)[None]
    wavefield = jnp.where(is_first, probe_wave, received[0])
    exit_wave = held_waves[0, 1].astype(jnp.float32)
    intensity = exit_wave[:, 0] * exit_wave[:, 0] + exit_wave[:, 1] * exit_wave[:, 1]
    residual = (intensity - measured)[:, None] * exit_wave
    returning = jnp.where(section == sections - 1, residual, received[3])
    transmitted = jnp.stack(
        [
            cosine * wavefield[:, 0] - sine_part * wavefield[:, 1],
            cosine * wavefield[:, 1] + sine_part * wavefield[:, 0],
        ],
        axis=1,
    )

    def side_halo(field):
        return padded_2(field, (("tile", 3),), MARGIN, True)

    spread = apply_operator(returning, side_halo, rows_back, cols_back)
    held_field = held_waves[0, 0].astype(jnp.float32)
    grad_real = spread[:, 0] * held_field[:, 0] + spread[:, 1] * held_field[:, 1]
    grad_imag = spread[:, 1] * held_field[:, 0] - spread[:, 0] * held_field[:, 1]
    gradient_term = jnp.stack([jnp.sum(grad_real, axis=0), jnp.sum(grad_imag, axis=0)])
    summed = line_allreduce(gradient_term, "angle", 4)
    returning = jnp.stack(
        [
            cosine * spread[:, 0] + sine_part * spread[:, 1],
            cosine * spread[:, 1] - sine_part * spread[:, 0],
        ],
        axis=1,
    )
    wavefield = apply_operator(transmitted, side_halo, rows_fwd, cols_fwd)
    return (wavefield[None], returning[None], summed[None, None])


def solution(mesh):
    in_specs = (
        P(None, "tile", None),
        P("depth", None, "tile", None),
        P("depth", "angle", None, "tile", None),
        P("depth", "angle", None, "tile", None),
        P("depth", None, "angle", None, "tile", None),
        P("angle", "tile", None),
        P("angle"),
        P("angle", None),
    )
    out_specs = (
        P("depth", "angle", None, "tile", None),
        P("depth", "angle", None, "tile", None),
        P("depth", None, None, "tile", None),
    )
    return jax.shard_map(body, mesh=mesh, in_specs=in_specs, out_specs=out_specs, check_vma=False)
```

```python
import math

import jax
import numpy as np
import jax.numpy as jnp
from jax import lax
from jax.experimental import pallas as pl
from jax.experimental.pallas import tpu as pltpu
from jax.sharding import PartitionSpec as P

MARGIN = 32
TILTS = 61


fresnel = 24.0
slice_step = 6.0
tilt_step = math.pi / 90.0
highest = lax.Precision.HIGHEST
wave_precision = lax.Precision.HIGH


def padded_2(block, sides, width, periodic):
    for axis, dim in sides:
        count = lax.axis_size(axis)
        forward = [(i, i + 1) for i in range(count - 1)]
        if periodic:
            forward.append((count - 1, 0))
        backward = [(target, source) for source, target in forward]
        low = lax.ppermute(
            lax.slice_in_dim(block, block.shape[dim] - width, None, axis=dim), axis, forward
        )
        high = lax.ppermute(lax.slice_in_dim(block, 0, width, axis=dim), axis, backward)
        block = jnp.concatenate([low, block, high], axis=dim)
    return block


def contract(form, left, right):
    return jnp.einsum(form, left, right, precision=wave_precision)


def signed_freqs(length):
    ordinal = lax.iota(jnp.int32, length)
    signed = jnp.where(ordinal >= length // 2, ordinal - length, ordinal)
    return signed.astype(jnp.float32) / length


def halving_allreduce(value, axis):
    count = lax.axis_size(axis)
    if count == 1:
        return value
    if count & (count - 1) or value.shape[-2] % count:
        return lax.psum(value, axis)
    index = lax.axis_index(axis)
    steps = count.bit_length() - 1
    dim = value.ndim - 2
    held = value
    for k in range(steps):
        bit = (index >> k) & 1
        size = held.shape[dim] // 2
        low = lax.slice_in_dim(held, 0, size, axis=dim)
        high = lax.slice_in_dim(held, size, None, axis=dim)
        keep = jnp.where(bit == 0, low, high)
        give = jnp.where(bit == 0, high, low)
        pairs = [(j, j ^ (1 << k)) for j in range(count)]
        held = keep + lax.ppermute(give, axis, pairs)
    for k in reversed(range(steps)):
        bit = (index >> k) & 1
        pairs = [(j, j ^ (1 << k)) for j in range(count)]
        other = lax.ppermute(held, axis, pairs)
        held = jnp.where(
            bit == 0,
            jnp.concatenate([held, other], axis=dim),
            jnp.concatenate([other, held], axis=dim),
        )
    return held


def table_kernel(both_ref, grid_ref, rows_ref, cols_ref):
    angle_count, doubled = both_ref.shape[0], both_ref.shape[1]
    count = doubled // 2
    length = both_ref.shape[2]
    core_size = rows_ref.shape[-1]
    width = grid_ref.shape[1] // 2
    column = lax.broadcasted_iota(jnp.int32, (core_size, core_size), 1)
    low_mask = column >= core_size - MARGIN
    high_mask = column < MARGIN
    for a in range(angle_count):
        product = jnp.dot(
            both_ref[a], grid_ref[...], precision=highest, preferred_element_type=jnp.float32
        )
        cos_cos = product[:count, :width]
        cos_sin = product[:count, width:]
        sin_cos = product[count:, :width]
        sin_sin = product[count:, width:]
        q_real = (cos_cos + sin_sin) * (1.0 / length)
        q_imag = (sin_cos - cos_sin) * (1.0 / length)

        def rolled(line, shift):
            wide = jnp.broadcast_to(line, (core_size, width))
            return pltpu.roll(wide, shift, 1, stride=1, stride_axis=0)

        for t in range(count):
            parts = []
            for q in (q_real, q_imag):
                line = q[t : t + 1, :]
                if t < 2:
                    inner = rolled(line, 0)[:, :core_size]
                    low = rolled(line, core_size)[:, :core_size]
                    high = rolled(line, width - core_size)[:, :core_size]
                    folded = inner + jnp.where(low_mask, low, 0.0) + jnp.where(high_mask, high, 0.0)
                    parts.append(folded)
                else:
                    parts.append(rolled(line, MARGIN)[:, :length])
            real, imag = parts
            if t < 2:
                rows_ref[a, t, 0] = real + imag
                rows_ref[a, t, 1] = real
                rows_ref[a, t, 2] = imag
            else:
                cols_ref[a, t - 2, 0] = real
                cols_ref[a, t - 2, 1] = imag - real
                cols_ref[a, t - 2, 2] = real + imag


def build_tables(lines, core_size):
    angle_count, count, length = lines.shape
    width = ((2 * length + 127) // 128) * 128
    ids = np.arange(length)[:, None] * np.arange(width)[None, :] % length
    angle = 2.0 * np.pi / length * ids
    grid = jnp.asarray(np.concatenate([np.cos(angle), np.sin(angle)], axis=1), jnp.float32)
    both = jnp.concatenate([jnp.cos(lines), jnp.sin(lines)], axis=1)
    return pl.pallas_call(
        table_kernel,
        out_shape=(
            jax.ShapeDtypeStruct((angle_count, 2, 3, core_size, core_size), jnp.float32),
            jax.ShapeDtypeStruct((angle_count, 2, 3, core_size, length), jnp.float32),
        ),
    )(both, grid)


def apply_operator(wave, padded_cols, row_table, col_table):
    wave_real = wave[:, 0]
    wave_imag = wave[:, 1]
    first = contract("ajl,alk->ajk", row_table[:, 0], wave_real)
    second = contract("ajl,alk->ajk", row_table[:, 1], wave_imag - wave_real)
    third = contract("ajl,alk->ajk", row_table[:, 2], wave_real + wave_imag)
    half = jnp.stack([first - third, first + second], axis=1)
    half = padded_cols(half)
    half_real = half[:, 0]
    half_imag = half[:, 1]
    first = contract("ajk,aik->aji", half_real + half_imag, col_table[:, 0])
    second = contract("ajk,aik->aji", half_real, col_table[:, 1])
    third = contract("ajk,aik->aji", half_imag, col_table[:, 2])
    return jnp.stack([first - third, first + second], axis=1)


def body(probe, phase, forward_in, adjoint_in, held_waves, measured, tilt_index, positions):
    core_size = phase.shape[-1]
    length = core_size + 2 * MARGIN
    angle_count = forward_in.shape[1]
    section = lax.axis_index("depth")
    sections = lax.axis_size("depth")
    is_first = section == 0
    frequency = signed_freqs(length)
    base_phase = -math.pi * fresnel * frequency * frequency

    tilt_angle = (tilt_index.astype(jnp.float32) - (TILTS - 1) / 2.0) * tilt_step
    lateral_drift = slice_step * jnp.tan(tilt_angle)
    shift_rows = jnp.where(is_first, positions[:, 0].astype(jnp.float32), 0.0)
    shift_cols = lateral_drift + jnp.where(is_first, positions[:, 1].astype(jnp.float32), 0.0)
    row_line = base_phase[None, :] - 2.0 * math.pi * frequency[None, :] * shift_rows[:, None]
    col_line = base_phase[None, :] - 2.0 * math.pi * frequency[None, :] * shift_cols[:, None]
    lines = jnp.stack([row_line, -row_line, col_line, -col_line], axis=1)
    row_tables, col_tables = build_tables(lines, core_size)
    rows_fwd = row_tables[:, 0]
    rows_back = row_tables[:, 1]
    cols_fwd = col_tables[:, 0]
    cols_back = col_tables[:, 1]

    cosine = jnp.cos(phase[0, 0])
    sine_part = jnp.sin(phase[0, 0])
    outgoing = jnp.concatenate([adjoint_in, forward_in], axis=0)
    received = padded_2(outgoing, (("depth", 0),), 1, False)
    probe_wave = probe.astype(jnp.float32)[None]
    wavefield = jnp.where(is_first, probe_wave, received[0])
    exit_wave = held_waves[0, 1].astype(jnp.float32)
    intensity = exit_wave[:, 0] * exit_wave[:, 0] + exit_wave[:, 1] * exit_wave[:, 1]
    residual = (intensity - measured)[:, None] * exit_wave
    returning = jnp.where(section == sections - 1, residual, received[3])
    transmitted = jnp.stack(
        [
            cosine * wavefield[:, 0] - sine_part * wavefield[:, 1],
            cosine * wavefield[:, 1] + sine_part * wavefield[:, 0],
        ],
        axis=1,
    )

    def side_halo(field):
        return padded_2(field, (("tile", 3),), MARGIN, True)

    spread = apply_operator(returning, side_halo, rows_back, cols_back)
    held_field = held_waves[0, 0].astype(jnp.float32)
    grad_real = spread[:, 0] * held_field[:, 0] + spread[:, 1] * held_field[:, 1]
    grad_imag = spread[:, 1] * held_field[:, 0] - spread[:, 0] * held_field[:, 1]
    gradient_term = jnp.stack([jnp.sum(grad_real, axis=0), jnp.sum(grad_imag, axis=0)])
    summed = halving_allreduce(gradient_term, "angle")
    returning = jnp.stack(
        [
            cosine * spread[:, 0] + sine_part * spread[:, 1],
            cosine * spread[:, 1] - sine_part * spread[:, 0],
        ],
        axis=1,
    )
    wavefield = apply_operator(transmitted, side_halo, rows_fwd, cols_fwd)
    return (wavefield[None], returning[None], summed[None, None])


def solution(mesh):
    in_specs = (
        P(None, "tile", None),
        P("depth", None, "tile", None),
        P("depth", "angle", None, "tile", None),
        P("depth", "angle", None, "tile", None),
        P("depth", None, "angle", None, "tile", None),
        P("angle", "tile", None),
        P("angle"),
        P("angle", None),
    )
    out_specs = (
        P("depth", "angle", None, "tile", None),
        P("depth", "angle", None, "tile", None),
        P("depth", None, None, "tile", None),
    )
    return jax.shard_map(body, mesh=mesh, in_specs=in_specs, out_specs=out_specs, check_vma=False)
```

```python
import math

import jax
import numpy as np
import jax.numpy as jnp
from jax import lax
from jax.experimental import pallas as pl
from jax.experimental.pallas import tpu as pltpu
from jax.sharding import PartitionSpec as P

MARGIN = 32
TILTS = 61


fresnel = 24.0
slice_step = 6.0
tilt_step = math.pi / 90.0
highest = lax.Precision.HIGHEST
wave_precision = lax.Precision.HIGH


def padded_2(block, sides, width, periodic):
    for axis, dim in sides:
        count = lax.axis_size(axis)
        forward = [(i, i + 1) for i in range(count - 1)]
        if periodic:
            forward.append((count - 1, 0))
        backward = [(target, source) for source, target in forward]
        low = lax.ppermute(
            lax.slice_in_dim(block, block.shape[dim] - width, None, axis=dim), axis, forward
        )
        high = lax.ppermute(lax.slice_in_dim(block, 0, width, axis=dim), axis, backward)
        block = jnp.concatenate([low, block, high], axis=dim)
    return block


def contract(form, left, right):
    return jnp.einsum(form, left, right, precision=wave_precision)


def signed_freqs(length):
    ordinal = lax.iota(jnp.int32, length)
    signed = jnp.where(ordinal >= length // 2, ordinal - length, ordinal)
    return signed.astype(jnp.float32) / length


def halving_allreduce(value, axis):
    count = lax.axis_size(axis)
    if count == 1:
        return value
    if count & (count - 1) or value.shape[-2] % count:
        return lax.psum(value, axis)
    index = lax.axis_index(axis)
    steps = count.bit_length() - 1
    dim = value.ndim - 2
    held = value
    for k in range(steps):
        bit = (index >> k) & 1
        size = held.shape[dim] // 2
        low = lax.slice_in_dim(held, 0, size, axis=dim)
        high = lax.slice_in_dim(held, size, None, axis=dim)
        keep = jnp.where(bit == 0, low, high)
        give = jnp.where(bit == 0, high, low)
        pairs = [(j, j ^ (1 << k)) for j in range(count)]
        held = keep + lax.ppermute(give, axis, pairs)
    for k in reversed(range(steps)):
        bit = (index >> k) & 1
        pairs = [(j, j ^ (1 << k)) for j in range(count)]
        other = lax.ppermute(held, axis, pairs)
        held = jnp.where(
            bit == 0,
            jnp.concatenate([held, other], axis=dim),
            jnp.concatenate([other, held], axis=dim),
        )
    return held


def table_kernel(shift_ref, grid_ref, rows_fwd_ref, rows_back_ref, cols_fwd_ref, cols_back_ref):
    angle_count = rows_fwd_ref.shape[0]
    length = grid_ref.shape[0]
    core_size = rows_fwd_ref.shape[-1]
    width = grid_ref.shape[1] // 2
    lane = lax.broadcasted_iota(jnp.int32, (1, length), 1)
    signed = jnp.where(lane >= length // 2, lane - length, lane)
    frequency = signed.astype(jnp.float32) / length
    base_phase = -math.pi * fresnel * frequency * frequency
    column = lax.broadcasted_iota(jnp.int32, (core_size, core_size), 1)
    low_mask = column >= core_size - MARGIN
    high_mask = column < MARGIN
    outputs = (rows_fwd_ref, rows_back_ref, cols_fwd_ref, cols_back_ref)
    for a in range(angle_count):
        row_line = base_phase - 2.0 * math.pi * frequency * shift_ref[2 * a]
        col_line = base_phase - 2.0 * math.pi * frequency * shift_ref[2 * a + 1]
        lines = jnp.concatenate([row_line, -row_line, col_line, -col_line], axis=0)
        both = jnp.concatenate([jnp.cos(lines), jnp.sin(lines)], axis=0)
        product = jnp.dot(both, grid_ref[...], precision=highest, preferred_element_type=jnp.float32)
        count = 4
        cos_cos = product[:count, :width]
        cos_sin = product[:count, width:]
        sin_cos = product[count:, :width]
        sin_sin = product[count:, width:]
        q_real = (cos_cos + sin_sin) * (1.0 / length)
        q_imag = (sin_cos - cos_sin) * (1.0 / length)

        def rolled(line, shift):
            wide = jnp.broadcast_to(line, (core_size, width))
            return pltpu.roll(wide, shift, 1, stride=1, stride_axis=0)

        for t in range(count):
            parts = []
            for q in (q_real, q_imag):
                line = q[t : t + 1, :]
                if t < 2:
                    inner = rolled(line, 0)[:, :core_size]
                    low = rolled(line, core_size)[:, :core_size]
                    high = rolled(line, width - core_size)[:, :core_size]
                    folded = inner + jnp.where(low_mask, low, 0.0) + jnp.where(high_mask, high, 0.0)
                    parts.append(folded)
                else:
                    parts.append(rolled(line, MARGIN)[:, :length])
            real, imag = parts
            out = outputs[t]
            if t < 2:
                out[a, 0] = real + imag
                out[a, 1] = real
                out[a, 2] = imag
            else:
                out[a, 0] = real
                out[a, 1] = imag - real
                out[a, 2] = real + imag


def build_tables(shifts, core_size, length):
    angle_count = shifts.shape[0]
    width = ((2 * length + 127) // 128) * 128
    ids = np.arange(length)[:, None] * np.arange(width)[None, :] % length
    angle = 2.0 * np.pi / length * ids
    grid = jnp.asarray(np.concatenate([np.cos(angle), np.sin(angle)], axis=1), jnp.float32)
    rows = jax.ShapeDtypeStruct((angle_count, 3, core_size, core_size), jnp.float32)
    cols = jax.ShapeDtypeStruct((angle_count, 3, core_size, length), jnp.float32)
    return pl.pallas_call(
        table_kernel,
        out_shape=(rows, rows, cols, cols),
        in_specs=[
            pl.BlockSpec(memory_space=pltpu.SMEM),
            pl.BlockSpec(memory_space=pltpu.VMEM),
        ],
    )(shifts.reshape(-1), grid)


def apply_operator(wave, padded_cols, row_table, col_table):
    wave_real = wave[:, 0]
    wave_imag = wave[:, 1]
    first = contract("ajl,alk->ajk", row_table[:, 0], wave_real)
    second = contract("ajl,alk->ajk", row_table[:, 1], wave_imag - wave_real)
    third = contract("ajl,alk->ajk", row_table[:, 2], wave_real + wave_imag)
    half = jnp.stack([first - third, first + second], axis=1)
    half = padded_cols(half)
    half_real = half[:, 0]
    half_imag = half[:, 1]
    first = contract("ajk,aik->aji", half_real + half_imag, col_table[:, 0])
    second = contract("ajk,aik->aji", half_real, col_table[:, 1])
    third = contract("ajk,aik->aji", half_imag, col_table[:, 2])
    return jnp.stack([first - third, first + second], axis=1)


def body(probe, phase, forward_in, adjoint_in, held_waves, measured, tilt_index, positions):
    core_size = phase.shape[-1]
    length = core_size + 2 * MARGIN
    angle_count = forward_in.shape[1]
    section = lax.axis_index("depth")
    sections = lax.axis_size("depth")
    is_first = section == 0
    tilt_angle = (tilt_index.astype(jnp.float32) - (TILTS - 1) / 2.0) * tilt_step
    lateral_drift = slice_step * jnp.tan(tilt_angle)
    shift_rows = jnp.where(is_first, positions[:, 0].astype(jnp.float32), 0.0)
    shift_cols = lateral_drift + jnp.where(is_first, positions[:, 1].astype(jnp.float32), 0.0)
    shifts = jnp.stack([shift_rows, shift_cols], axis=-1)
    rows_fwd, rows_back, cols_fwd, cols_back = build_tables(shifts, core_size, length)

    cosine = jnp.cos(phase[0, 0])
    sine_part = jnp.sin(phase[0, 0])
    outgoing = jnp.concatenate([adjoint_in, forward_in], axis=0)
    received = padded_2(outgoing, (("depth", 0),), 1, False)
    probe_wave = probe.astype(jnp.float32)[None]
    wavefield = jnp.where(is_first, probe_wave, received[0])
    exit_wave = held_waves[0, 1].astype(jnp.float32)
    intensity = exit_wave[:, 0] * exit_wave[:, 0] + exit_wave[:, 1] * exit_wave[:, 1]
    residual = (intensity - measured)[:, None] * exit_wave
    returning = jnp.where(section == sections - 1, residual, received[3])
    transmitted = jnp.stack(
        [
            cosine * wavefield[:, 0] - sine_part * wavefield[:, 1],
            cosine * wavefield[:, 1] + sine_part * wavefield[:, 0],
        ],
        axis=1,
    )

    def side_halo(field):
        return padded_2(field, (("tile", 3),), MARGIN, True)

    spread = apply_operator(returning, side_halo, rows_back, cols_back)
    held_field = held_waves[0, 0].astype(jnp.float32)
    grad_real = spread[:, 0] * held_field[:, 0] + spread[:, 1] * held_field[:, 1]
    grad_imag = spread[:, 1] * held_field[:, 0] - spread[:, 0] * held_field[:, 1]
    gradient_term = jnp.stack([jnp.sum(grad_real, axis=0), jnp.sum(grad_imag, axis=0)])
    summed = halving_allreduce(gradient_term, "angle")
    returning = jnp.stack(
        [
            cosine * spread[:, 0] + sine_part * spread[:, 1],
            cosine * spread[:, 1] - sine_part * spread[:, 0],
        ],
        axis=1,
    )
    wavefield = apply_operator(transmitted, side_halo, rows_fwd, cols_fwd)
    return (wavefield[None], returning[None], summed[None, None])


def solution(mesh):
    in_specs = (
        P(None, "tile", None),
        P("depth", None, "tile", None),
        P("depth", "angle", None, "tile", None),
        P("depth", "angle", None, "tile", None),
        P("depth", None, "angle", None, "tile", None),
        P("angle", "tile", None),
        P("angle"),
        P("angle", None),
    )
    out_specs = (
        P("depth", "angle", None, "tile", None),
        P("depth", "angle", None, "tile", None),
        P("depth", None, None, "tile", None),
    )
    return jax.shard_map(body, mesh=mesh, in_specs=in_specs, out_specs=out_specs, check_vma=False)
```

```python
import math

import jax
import numpy as np
import jax.numpy as jnp
from jax import lax
from jax.experimental import pallas as pl
from jax.experimental.pallas import tpu as pltpu
from jax.sharding import PartitionSpec as P

MARGIN = 32
TILTS = 61


fresnel = 24.0
slice_step = 6.0
tilt_step = math.pi / 90.0
highest = lax.Precision.HIGHEST
wave_precision = lax.Precision.HIGH


def padded_2(block, sides, width, periodic):
    for axis, dim in sides:
        count = lax.axis_size(axis)
        forward = [(i, i + 1) for i in range(count - 1)]
        if periodic:
            forward.append((count - 1, 0))
        backward = [(target, source) for source, target in forward]
        low = lax.ppermute(
            lax.slice_in_dim(block, block.shape[dim] - width, None, axis=dim), axis, forward
        )
        high = lax.ppermute(lax.slice_in_dim(block, 0, width, axis=dim), axis, backward)
        block = jnp.concatenate([low, block, high], axis=dim)
    return block


def contract(form, left, right):
    return jnp.einsum(form, left, right, precision=wave_precision)


def signed_freqs(length):
    ordinal = lax.iota(jnp.int32, length)
    signed = jnp.where(ordinal >= length // 2, ordinal - length, ordinal)
    return signed.astype(jnp.float32) / length


def halving_allreduce(value, axis):
    count = lax.axis_size(axis)
    if count == 1:
        return value
    if count & (count - 1) or value.shape[-2] % count:
        return lax.psum(value, axis)
    index = lax.axis_index(axis)
    steps = count.bit_length() - 1
    dim = value.ndim - 2
    held = value
    for k in range(steps):
        bit = (index >> k) & 1
        size = held.shape[dim] // 2
        low = lax.slice_in_dim(held, 0, size, axis=dim)
        high = lax.slice_in_dim(held, size, None, axis=dim)
        keep = jnp.where(bit == 0, low, high)
        give = jnp.where(bit == 0, high, low)
        pairs = [(j, j ^ (1 << k)) for j in range(count)]
        held = keep + lax.ppermute(give, axis, pairs)
    for k in reversed(range(steps)):
        bit = (index >> k) & 1
        pairs = [(j, j ^ (1 << k)) for j in range(count)]
        other = lax.ppermute(held, axis, pairs)
        held = jnp.where(
            bit == 0,
            jnp.concatenate([held, other], axis=dim),
            jnp.concatenate([other, held], axis=dim),
        )
    return held


def table_kernel(
    tilt_ref, position_ref, first_ref, grid_ref, rows_fwd_ref, rows_back_ref, cols_fwd_ref, cols_back_ref
):
    angle_count = rows_fwd_ref.shape[0]
    length = grid_ref.shape[0]
    core_size = rows_fwd_ref.shape[-1]
    width = grid_ref.shape[1] // 2
    lane = lax.broadcasted_iota(jnp.int32, (1, length), 1)
    signed = jnp.where(lane >= length // 2, lane - length, lane)
    frequency = signed.astype(jnp.float32) / length
    base_phase = -math.pi * fresnel * frequency * frequency
    column = lax.broadcasted_iota(jnp.int32, (core_size, core_size), 1)
    low_mask = column >= core_size - MARGIN
    high_mask = column < MARGIN
    outputs = (rows_fwd_ref, rows_back_ref, cols_fwd_ref, cols_back_ref)
    first = jnp.full((1, length), first_ref[0], jnp.int32).astype(jnp.float32)
    for a in range(angle_count):
        tilt = jnp.full((1, length), tilt_ref[a], jnp.int32).astype(jnp.float32)
        tilt_angle = (tilt - (TILTS - 1) / 2.0) * tilt_step
        drift = slice_step * (jnp.sin(tilt_angle) / jnp.cos(tilt_angle))
        shift_rows = jnp.full((1, length), position_ref[2 * a], jnp.int32).astype(jnp.float32) * first
        shift_cols = drift + jnp.full((1, length), position_ref[2 * a + 1], jnp.int32).astype(
            jnp.float32
        ) * first
        row_line = base_phase - 2.0 * math.pi * frequency * shift_rows
        col_line = base_phase - 2.0 * math.pi * frequency * shift_cols
        lines = jnp.concatenate([row_line, -row_line, col_line, -col_line], axis=0)
        both = jnp.concatenate([jnp.cos(lines), jnp.sin(lines)], axis=0)
        product = jnp.dot(both, grid_ref[...], precision=highest, preferred_element_type=jnp.float32)
        count = 4
        cos_cos = product[:count, :width]
        cos_sin = product[:count, width:]
        sin_cos = product[count:, :width]
        sin_sin = product[count:, width:]
        q_real = (cos_cos + sin_sin) * (1.0 / length)
        q_imag = (sin_cos - cos_sin) * (1.0 / length)

        def rolled(line, shift):
            wide = jnp.broadcast_to(line, (core_size, width))
            return pltpu.roll(wide, shift, 1, stride=1, stride_axis=0)

        for t in range(count):
            parts = []
            for q in (q_real, q_imag):
                line = q[t : t + 1, :]
                if t < 2:
                    inner = rolled(line, 0)[:, :core_size]
                    low = rolled(line, core_size)[:, :core_size]
                    high = rolled(line, width - core_size)[:, :core_size]
                    folded = inner + jnp.where(low_mask, low, 0.0) + jnp.where(high_mask, high, 0.0)
                    parts.append(folded)
                else:
                    parts.append(rolled(line, MARGIN)[:, :length])
            real, imag = parts
            out = outputs[t]
            if t < 2:
                out[a, 0] = real + imag
                out[a, 1] = real
                out[a, 2] = imag
            else:
                out[a, 0] = real
                out[a, 1] = imag - real
                out[a, 2] = real + imag


def build_tables(tilt_index, positions, is_first, core_size, length):
    angle_count = tilt_index.shape[0]
    width = ((2 * length + 127) // 128) * 128
    ids = np.arange(length)[:, None] * np.arange(width)[None, :] % length
    angle = 2.0 * np.pi / length * ids
    grid = jnp.asarray(np.concatenate([np.cos(angle), np.sin(angle)], axis=1), jnp.float32)
    rows = jax.ShapeDtypeStruct((angle_count, 3, core_size, core_size), jnp.float32)
    cols = jax.ShapeDtypeStruct((angle_count, 3, core_size, length), jnp.float32)
    return pl.pallas_call(
        table_kernel,
        out_shape=(rows, rows, cols, cols),
        in_specs=[
            pl.BlockSpec(memory_space=pltpu.SMEM),
            pl.BlockSpec(memory_space=pltpu.SMEM),
            pl.BlockSpec(memory_space=pltpu.SMEM),
            pl.BlockSpec(memory_space=pltpu.VMEM),
        ],
    )(tilt_index, positions.reshape(-1), is_first.astype(jnp.int32).reshape(1), grid)


def apply_operator(wave, padded_cols, row_table, col_table):
    wave_real = wave[:, 0]
    wave_imag = wave[:, 1]
    first = contract("ajl,alk->ajk", row_table[:, 0], wave_real)
    second = contract("ajl,alk->ajk", row_table[:, 1], wave_imag - wave_real)
    third = contract("ajl,alk->ajk", row_table[:, 2], wave_real + wave_imag)
    half = jnp.stack([first - third, first + second], axis=1)
    half = padded_cols(half)
    half_real = half[:, 0]
    half_imag = half[:, 1]
    first = contract("ajk,aik->aji", half_real + half_imag, col_table[:, 0])
    second = contract("ajk,aik->aji", half_real, col_table[:, 1])
    third = contract("ajk,aik->aji", half_imag, col_table[:, 2])
    return jnp.stack([first - third, first + second], axis=1)


def body(probe, phase, forward_in, adjoint_in, held_waves, measured, tilt_index, positions):
    core_size = phase.shape[-1]
    length = core_size + 2 * MARGIN
    angle_count = forward_in.shape[1]
    section = lax.axis_index("depth")
    sections = lax.axis_size("depth")
    is_first = section == 0
    rows_fwd, rows_back, cols_fwd, cols_back = build_tables(
        tilt_index, positions, is_first, core_size, length
    )

    cosine = jnp.cos(phase[0, 0])
    sine_part = jnp.sin(phase[0, 0])
    outgoing = jnp.concatenate([adjoint_in, forward_in], axis=0)
    received = padded_2(outgoing, (("depth", 0),), 1, False)
    probe_wave = probe.astype(jnp.float32)[None]
    wavefield = jnp.where(is_first, probe_wave, received[0])
    exit_wave = held_waves[0, 1].astype(jnp.float32)
    intensity = exit_wave[:, 0] * exit_wave[:, 0] + exit_wave[:, 1] * exit_wave[:, 1]
    residual = (intensity - measured)[:, None] * exit_wave
    returning = jnp.where(section == sections - 1, residual, received[3])
    transmitted = jnp.stack(
        [
            cosine * wavefield[:, 0] - sine_part * wavefield[:, 1],
            cosine * wavefield[:, 1] + sine_part * wavefield[:, 0],
        ],
        axis=1,
    )

    def side_halo(field):
        return padded_2(field, (("tile", 3),), MARGIN, True)

    spread = apply_operator(returning, side_halo, rows_back, cols_back)
    held_field = held_waves[0, 0].astype(jnp.float32)
    grad_real = spread[:, 0] * held_field[:, 0] + spread[:, 1] * held_field[:, 1]
    grad_imag = spread[:, 1] * held_field[:, 0] - spread[:, 0] * held_field[:, 1]
    gradient_term = jnp.stack([jnp.sum(grad_real, axis=0), jnp.sum(grad_imag, axis=0)])
    summed = halving_allreduce(gradient_term, "angle")
    returning = jnp.stack(
        [
            cosine * spread[:, 0] + sine_part * spread[:, 1],
            cosine * spread[:, 1] - sine_part * spread[:, 0],
        ],
        axis=1,
    )
    wavefield = apply_operator(transmitted, side_halo, rows_fwd, cols_fwd)
    return (wavefield[None], returning[None], summed[None, None])


def solution(mesh):
    in_specs = (
        P(None, "tile", None),
        P("depth", None, "tile", None),
        P("depth", "angle", None, "tile", None),
        P("depth", "angle", None, "tile", None),
        P("depth", None, "angle", None, "tile", None),
        P("angle", "tile", None),
        P("angle"),
        P("angle", None),
    )
    out_specs = (
        P("depth", "angle", None, "tile", None),
        P("depth", "angle", None, "tile", None),
        P("depth", None, None, "tile", None),
    )
    return jax.shard_map(body, mesh=mesh, in_specs=in_specs, out_specs=out_specs, check_vma=False)
```

```python
import math

import jax
import numpy as np
import jax.numpy as jnp
from jax import lax
from jax.experimental import pallas as pl
from jax.experimental.pallas import tpu as pltpu
from jax.sharding import PartitionSpec as P

MARGIN = 32
TILTS = 61


fresnel = 24.0
slice_step = 6.0
tilt_step = math.pi / 90.0
highest = lax.Precision.HIGHEST
wave_precision = lax.Precision.HIGH


def padded_2(block, sides, width, periodic):
    for axis, dim in sides:
        count = lax.axis_size(axis)
        forward = [(i, i + 1) for i in range(count - 1)]
        if periodic:
            forward.append((count - 1, 0))
        backward = [(target, source) for source, target in forward]
        low = lax.ppermute(
            lax.slice_in_dim(block, block.shape[dim] - width, None, axis=dim), axis, forward
        )
        high = lax.ppermute(lax.slice_in_dim(block, 0, width, axis=dim), axis, backward)
        block = jnp.concatenate([low, block, high], axis=dim)
    return block


def contract(form, left, right):
    return jnp.einsum(form, left, right, precision=wave_precision)


def signed_freqs(length):
    ordinal = lax.iota(jnp.int32, length)
    signed = jnp.where(ordinal >= length // 2, ordinal - length, ordinal)
    return signed.astype(jnp.float32) / length


def halving_allreduce(value, axis):
    count = lax.axis_size(axis)
    if count == 1:
        return value
    if count & (count - 1) or value.shape[-2] % count:
        return lax.psum(value, axis)
    index = lax.axis_index(axis)
    steps = count.bit_length() - 1
    dim = value.ndim - 2
    held = value
    for k in range(steps):
        bit = (index >> k) & 1
        size = held.shape[dim] // 2
        low = lax.slice_in_dim(held, 0, size, axis=dim)
        high = lax.slice_in_dim(held, size, None, axis=dim)
        keep = jnp.where(bit == 0, low, high)
        give = jnp.where(bit == 0, high, low)
        pairs = [(j, j ^ (1 << k)) for j in range(count)]
        held = keep + lax.ppermute(give, axis, pairs)
    for k in reversed(range(steps)):
        bit = (index >> k) & 1
        pairs = [(j, j ^ (1 << k)) for j in range(count)]
        other = lax.ppermute(held, axis, pairs)
        held = jnp.where(
            bit == 0,
            jnp.concatenate([held, other], axis=dim),
            jnp.concatenate([other, held], axis=dim),
        )
    return held


def table_kernel(
    tilt_ref, position_ref, first_ref, grid_ref, rows_fwd_ref, rows_back_ref, cols_fwd_ref, cols_back_ref
):
    angle_count = rows_fwd_ref.shape[0]
    length = grid_ref.shape[0]
    core_size = rows_fwd_ref.shape[-1]
    width = grid_ref.shape[1] // 2
    lane = lax.broadcasted_iota(jnp.int32, (1, length), 1)
    signed = jnp.where(lane >= length // 2, lane - length, lane)
    frequency = signed.astype(jnp.float32) / length
    base_phase = -math.pi * fresnel * frequency * frequency
    column = lax.broadcasted_iota(jnp.int32, (core_size, core_size), 1)
    low_mask = column >= core_size - MARGIN
    high_mask = column < MARGIN
    outputs = (rows_fwd_ref, rows_back_ref, cols_fwd_ref, cols_back_ref)
    first = jnp.full((1, length), first_ref[0], jnp.int32).astype(jnp.float32)
    for a in range(angle_count):
        tilt = jnp.full((1, length), tilt_ref[a], jnp.int32).astype(jnp.float32)
        tilt_angle = (tilt - (TILTS - 1) / 2.0) * tilt_step
        drift = slice_step * (jnp.sin(tilt_angle) / jnp.cos(tilt_angle))
        shift_rows = jnp.full((1, length), position_ref[2 * a], jnp.int32).astype(jnp.float32) * first
        shift_cols = drift + jnp.full((1, length), position_ref[2 * a + 1], jnp.int32).astype(
            jnp.float32
        ) * first
        row_line = base_phase - 2.0 * math.pi * frequency * shift_rows
        col_line = base_phase - 2.0 * math.pi * frequency * shift_cols
        lines = jnp.concatenate([row_line, -row_line, col_line, -col_line], axis=0)
        both = jnp.concatenate([jnp.cos(lines), jnp.sin(lines)], axis=0)
        product = jnp.dot(both, grid_ref[...], precision=highest, preferred_element_type=jnp.float32)
        count = 4
        cos_cos = product[:count, :width]
        cos_sin = product[:count, width:]
        sin_cos = product[count:, :width]
        sin_sin = product[count:, width:]
        q_real = (cos_cos + sin_sin) * (1.0 / length)
        q_imag = (sin_cos - cos_sin) * (1.0 / length)

        def rolled(line, shift):
            wide = jnp.broadcast_to(line, (core_size, width))
            return pltpu.roll(wide, shift, 1, stride=1, stride_axis=0)

        for t in range(count):
            parts = []
            for q in (q_real, q_imag):
                line = q[t : t + 1, :]
                if t < 2:
                    inner = rolled(line, 0)[:, :core_size]
                    low = rolled(line, core_size)[:, :core_size]
                    high = rolled(line, width - core_size)[:, :core_size]
                    folded = inner + jnp.where(low_mask, low, 0.0) + jnp.where(high_mask, high, 0.0)
                    parts.append(folded)
                else:
                    parts.append(rolled(line, MARGIN)[:, :length])
            real, imag = parts
            out = outputs[t]
            if t < 2:
                out[a, 0] = real + imag
                out[a, 1] = real
                out[a, 2] = imag
            else:
                out[a, 0] = real
                out[a, 1] = imag - real
                out[a, 2] = real + imag


def build_tables(tilt_index, positions, is_first, core_size, length):
    angle_count = tilt_index.shape[0]
    width = ((2 * length + 127) // 128) * 128
    ids = np.arange(length)[:, None] * np.arange(width)[None, :] % length
    angle = 2.0 * np.pi / length * ids
    grid = jnp.asarray(np.concatenate([np.cos(angle), np.sin(angle)], axis=1), jnp.float32)
    rows = jax.ShapeDtypeStruct((angle_count, 3, core_size, core_size), jnp.float32)
    cols = jax.ShapeDtypeStruct((angle_count, 3, core_size, length), jnp.float32)
    return pl.pallas_call(
        table_kernel,
        out_shape=(rows, rows, cols, cols),
        in_specs=[
            pl.BlockSpec(memory_space=pltpu.SMEM),
            pl.BlockSpec(memory_space=pltpu.SMEM),
            pl.BlockSpec(memory_space=pltpu.SMEM),
            pl.BlockSpec(memory_space=pltpu.VMEM),
        ],
    )(tilt_index, positions.reshape(-1), is_first.astype(jnp.int32).reshape(1), grid)


def apply_operator(wave, padded_cols, row_table, col_table):
    wave_real = wave[:, 0]
    wave_imag = wave[:, 1]
    first = contract("ajl,alk->ajk", row_table[:, 0], wave_real)
    second = contract("ajl,alk->ajk", row_table[:, 1], wave_imag - wave_real)
    third = contract("ajl,alk->ajk", row_table[:, 2], wave_real + wave_imag)
    half = jnp.stack([first - third, first + second], axis=1)
    half = padded_cols(half)
    half_real = half[:, 0]
    half_imag = half[:, 1]
    first = contract("ajk,aik->aji", half_real + half_imag, col_table[:, 0])
    second = contract("ajk,aik->aji", half_real, col_table[:, 1])
    third = contract("ajk,aik->aji", half_imag, col_table[:, 2])
    return jnp.stack([first - third, first + second], axis=1)


def body(probe, phase, forward_in, adjoint_in, held_waves, measured, tilt_index, positions):
    core_size = phase.shape[-1]
    length = core_size + 2 * MARGIN
    angle_count = forward_in.shape[1]
    section = lax.axis_index("depth")
    sections = lax.axis_size("depth")
    is_first = section == 0
    rows_fwd, rows_back, cols_fwd, cols_back = build_tables(
        tilt_index, positions, is_first, core_size, length
    )

    cosine = jnp.cos(phase[0, 0])
    sine_part = jnp.sin(phase[0, 0])
    outgoing = jnp.concatenate([adjoint_in, forward_in], axis=0)
    received = padded_2(outgoing, (("depth", 0),), 1, False)
    probe_wave = probe.astype(jnp.float32)[None]
    wavefield = jnp.where(is_first, probe_wave, received[0])
    exit_wave = held_waves[0, 1].astype(jnp.float32)
    intensity = exit_wave[:, 0] * exit_wave[:, 0] + exit_wave[:, 1] * exit_wave[:, 1]
    residual = (intensity - measured)[:, None] * exit_wave
    returning = jnp.where(section == sections - 1, residual, received[3])
    transmitted = jnp.stack(
        [
            cosine * wavefield[:, 0] - sine_part * wavefield[:, 1],
            cosine * wavefield[:, 1] + sine_part * wavefield[:, 0],
        ],
        axis=1,
    )

    def side_halo(field):
        count = lax.axis_size("tile")
        if count > 2:
            return padded_2(field, (("tile", 3),), MARGIN, True)
        width = field.shape[3]
        edges = jnp.concatenate([field[..., :MARGIN], field[..., width - MARGIN :]], axis=3)
        if count == 2:
            edges = lax.ppermute(edges, "tile", [(0, 1), (1, 0)])
        return jnp.concatenate([edges[..., MARGIN:], field, edges[..., :MARGIN]], axis=3)

    spread = apply_operator(returning, side_halo, rows_back, cols_back)
    held_field = held_waves[0, 0].astype(jnp.float32)
    grad_real = spread[:, 0] * held_field[:, 0] + spread[:, 1] * held_field[:, 1]
    grad_imag = spread[:, 1] * held_field[:, 0] - spread[:, 0] * held_field[:, 1]
    gradient_term = jnp.stack([jnp.sum(grad_real, axis=0), jnp.sum(grad_imag, axis=0)])
    summed = halving_allreduce(gradient_term, "angle")
    returning = jnp.stack(
        [
            cosine * spread[:, 0] + sine_part * spread[:, 1],
            cosine * spread[:, 1] - sine_part * spread[:, 0],
        ],
        axis=1,
    )
    wavefield = apply_operator(transmitted, side_halo, rows_fwd, cols_fwd)
    return (wavefield[None], returning[None], summed[None, None])


def solution(mesh):
    in_specs = (
        P(None, "tile", None),
        P("depth", None, "tile", None),
        P("depth", "angle", None, "tile", None),
        P("depth", "angle", None, "tile", None),
        P("depth", None, "angle", None, "tile", None),
        P("angle", "tile", None),
        P("angle"),
        P("angle", None),
    )
    out_specs = (
        P("depth", "angle", None, "tile", None),
        P("depth", "angle", None, "tile", None),
        P("depth", None, None, "tile", None),
    )
    return jax.shard_map(body, mesh=mesh, in_specs=in_specs, out_specs=out_specs, check_vma=False)
```

```python
import math

import jax
import numpy as np
import jax.numpy as jnp
from jax import lax
from jax.experimental import pallas as pl
from jax.experimental.pallas import tpu as pltpu
from jax.sharding import PartitionSpec as P

MARGIN = 32
TILTS = 61


fresnel = 24.0
slice_step = 6.0
tilt_step = math.pi / 90.0
highest = lax.Precision.HIGHEST
wave_precision = lax.Precision.HIGH


def padded_2(block, sides, width, periodic):
    for axis, dim in sides:
        count = lax.axis_size(axis)
        forward = [(i, i + 1) for i in range(count - 1)]
        if periodic:
            forward.append((count - 1, 0))
        backward = [(target, source) for source, target in forward]
        low = lax.ppermute(
            lax.slice_in_dim(block, block.shape[dim] - width, None, axis=dim), axis, forward
        )
        high = lax.ppermute(lax.slice_in_dim(block, 0, width, axis=dim), axis, backward)
        block = jnp.concatenate([low, block, high], axis=dim)
    return block


def contract(form, left, right):
    return jnp.einsum(form, left, right, precision=wave_precision)


def signed_freqs(length):
    ordinal = lax.iota(jnp.int32, length)
    signed = jnp.where(ordinal >= length // 2, ordinal - length, ordinal)
    return signed.astype(jnp.float32) / length


def halving_allreduce(value, axis, other):
    count = lax.axis_size(axis)
    if count == 1:
        return value
    if count & (count - 1) or value.shape[-2] % count:
        return lax.psum(value, axis)
    groups = lax.axis_size(other)
    index = lax.axis_index(axis)
    odd = lax.axis_index(other) % 2
    steps = count.bit_length() - 1
    dim = value.ndim - 2

    def position(step, parity):
        return step if parity == 0 else steps - 1 - step

    def pairs(step):
        return [
            (g * count + j, g * count + (j ^ (1 << position(step, g % 2))))
            for g in range(groups)
            for j in range(count)
        ]

    def bit_of(step):
        shift = jnp.where(odd == 0, position(step, 0), position(step, 1))
        return (index >> shift) & 1

    held = value
    for k in range(steps):
        bit = bit_of(k)
        size = held.shape[dim] // 2
        low = lax.slice_in_dim(held, 0, size, axis=dim)
        high = lax.slice_in_dim(held, size, None, axis=dim)
        keep = jnp.where(bit == 0, low, high)
        give = jnp.where(bit == 0, high, low)
        held = keep + lax.ppermute(give, (other, axis), pairs(k))
    for k in reversed(range(steps)):
        bit = bit_of(k)
        got = lax.ppermute(held, (other, axis), pairs(k))
        held = jnp.where(
            bit == 0,
            jnp.concatenate([held, got], axis=dim),
            jnp.concatenate([got, held], axis=dim),
        )
    return held


def table_kernel(
    tilt_ref, position_ref, first_ref, grid_ref, rows_fwd_ref, rows_back_ref, cols_fwd_ref, cols_back_ref
):
    angle_count = rows_fwd_ref.shape[0]
    length = grid_ref.shape[0]
    core_size = rows_fwd_ref.shape[-1]
    width = grid_ref.shape[1] // 2
    lane = lax.broadcasted_iota(jnp.int32, (1, length), 1)
    signed = jnp.where(lane >= length // 2, lane - length, lane)
    frequency = signed.astype(jnp.float32) / length
    base_phase = -math.pi * fresnel * frequency * frequency
    column = lax.broadcasted_iota(jnp.int32, (core_size, core_size), 1)
    low_mask = column >= core_size - MARGIN
    high_mask = column < MARGIN
    outputs = (rows_fwd_ref, rows_back_ref, cols_fwd_ref, cols_back_ref)
    first = jnp.full((1, length), first_ref[0], jnp.int32).astype(jnp.float32)
    for a in range(angle_count):
        tilt = jnp.full((1, length), tilt_ref[a], jnp.int32).astype(jnp.float32)
        tilt_angle = (tilt - (TILTS - 1) / 2.0) * tilt_step
        drift = slice_step * (jnp.sin(tilt_angle) / jnp.cos(tilt_angle))
        shift_rows = jnp.full((1, length), position_ref[2 * a], jnp.int32).astype(jnp.float32) * first
        shift_cols = drift + jnp.full((1, length), position_ref[2 * a + 1], jnp.int32).astype(
            jnp.float32
        ) * first
        row_line = base_phase - 2.0 * math.pi * frequency * shift_rows
        col_line = base_phase - 2.0 * math.pi * frequency * shift_cols
        lines = jnp.concatenate([row_line, -row_line, col_line, -col_line], axis=0)
        both = jnp.concatenate([jnp.cos(lines), jnp.sin(lines)], axis=0)
        product = jnp.dot(both, grid_ref[...], precision=highest, preferred_element_type=jnp.float32)
        count = 4
        cos_cos = product[:count, :width]
        cos_sin = product[:count, width:]
        sin_cos = product[count:, :width]
        sin_sin = product[count:, width:]
        q_real = (cos_cos + sin_sin) * (1.0 / length)
        q_imag = (sin_cos - cos_sin) * (1.0 / length)

        def rolled(line, shift):
            wide = jnp.broadcast_to(line, (core_size, width))
            return pltpu.roll(wide, shift, 1, stride=1, stride_axis=0)

        for t in range(count):
            parts = []
            for q in (q_real, q_imag):
                line = q[t : t + 1, :]
                if t < 2:
                    inner = rolled(line, 0)[:, :core_size]
                    low = rolled(line, core_size)[:, :core_size]
                    high = rolled(line, width - core_size)[:, :core_size]
                    folded = inner + jnp.where(low_mask, low, 0.0) + jnp.where(high_mask, high, 0.0)
                    parts.append(folded)
                else:
                    parts.append(rolled(line, MARGIN)[:, :length])
            real, imag = parts
            out = outputs[t]
            if t < 2:
                out[a, 0] = real + imag
                out[a, 1] = real
                out[a, 2] = imag
            else:
                out[a, 0] = real
                out[a, 1] = imag - real
                out[a, 2] = real + imag


def build_tables(tilt_index, positions, is_first, core_size, length):
    angle_count = tilt_index.shape[0]
    width = ((2 * length + 127) // 128) * 128
    ids = np.arange(length)[:, None] * np.arange(width)[None, :] % length
    angle = 2.0 * np.pi / length * ids
    grid = jnp.asarray(np.concatenate([np.cos(angle), np.sin(angle)], axis=1), jnp.float32)
    rows = jax.ShapeDtypeStruct((angle_count, 3, core_size, core_size), jnp.float32)
    cols = jax.ShapeDtypeStruct((angle_count, 3, core_size, length), jnp.float32)
    return pl.pallas_call(
        table_kernel,
        out_shape=(rows, rows, cols, cols),
        in_specs=[
            pl.BlockSpec(memory_space=pltpu.SMEM),
            pl.BlockSpec(memory_space=pltpu.SMEM),
            pl.BlockSpec(memory_space=pltpu.SMEM),
            pl.BlockSpec(memory_space=pltpu.VMEM),
        ],
    )(tilt_index, positions.reshape(-1), is_first.astype(jnp.int32).reshape(1), grid)


def apply_operator(wave, padded_cols, row_table, col_table):
    wave_real = wave[:, 0]
    wave_imag = wave[:, 1]
    first = contract("ajl,alk->ajk", row_table[:, 0], wave_real)
    second = contract("ajl,alk->ajk", row_table[:, 1], wave_imag - wave_real)
    third = contract("ajl,alk->ajk", row_table[:, 2], wave_real + wave_imag)
    half = jnp.stack([first - third, first + second], axis=1)
    half = padded_cols(half)
    half_real = half[:, 0]
    half_imag = half[:, 1]
    first = contract("ajk,aik->aji", half_real + half_imag, col_table[:, 0])
    second = contract("ajk,aik->aji", half_real, col_table[:, 1])
    third = contract("ajk,aik->aji", half_imag, col_table[:, 2])
    return jnp.stack([first - third, first + second], axis=1)


def body(probe, phase, forward_in, adjoint_in, held_waves, measured, tilt_index, positions):
    core_size = phase.shape[-1]
    length = core_size + 2 * MARGIN
    angle_count = forward_in.shape[1]
    section = lax.axis_index("depth")
    sections = lax.axis_size("depth")
    is_first = section == 0
    rows_fwd, rows_back, cols_fwd, cols_back = build_tables(
        tilt_index, positions, is_first, core_size, length
    )

    cosine = jnp.cos(phase[0, 0])
    sine_part = jnp.sin(phase[0, 0])
    outgoing = jnp.concatenate([adjoint_in, forward_in], axis=0)
    received = padded_2(outgoing, (("depth", 0),), 1, False)
    probe_wave = probe.astype(jnp.float32)[None]
    wavefield = jnp.where(is_first, probe_wave, received[0])
    exit_wave = held_waves[0, 1].astype(jnp.float32)
    intensity = exit_wave[:, 0] * exit_wave[:, 0] + exit_wave[:, 1] * exit_wave[:, 1]
    residual = (intensity - measured)[:, None] * exit_wave
    returning = jnp.where(section == sections - 1, residual, received[3])
    transmitted = jnp.stack(
        [
            cosine * wavefield[:, 0] - sine_part * wavefield[:, 1],
            cosine * wavefield[:, 1] + sine_part * wavefield[:, 0],
        ],
        axis=1,
    )

    def side_halo(field):
        count = lax.axis_size("tile")
        if count > 2:
            return padded_2(field, (("tile", 3),), MARGIN, True)
        width = field.shape[3]
        edges = jnp.concatenate([field[..., :MARGIN], field[..., width - MARGIN :]], axis=3)
        if count == 2:
            edges = lax.ppermute(edges, "tile", [(0, 1), (1, 0)])
        return jnp.concatenate([edges[..., MARGIN:], field, edges[..., :MARGIN]], axis=3)

    spread = apply_operator(returning, side_halo, rows_back, cols_back)
    held_field = held_waves[0, 0].astype(jnp.float32)
    grad_real = spread[:, 0] * held_field[:, 0] + spread[:, 1] * held_field[:, 1]
    grad_imag = spread[:, 1] * held_field[:, 0] - spread[:, 0] * held_field[:, 1]
    gradient_term = jnp.stack([jnp.sum(grad_real, axis=0), jnp.sum(grad_imag, axis=0)])
    summed = halving_allreduce(gradient_term, "angle", "depth")
    returning = jnp.stack(
        [
            cosine * spread[:, 0] + sine_part * spread[:, 1],
            cosine * spread[:, 1] - sine_part * spread[:, 0],
        ],
        axis=1,
    )
    wavefield = apply_operator(transmitted, side_halo, rows_fwd, cols_fwd)
    return (wavefield[None], returning[None], summed[None, None])


def solution(mesh):
    in_specs = (
        P(None, "tile", None),
        P("depth", None, "tile", None),
        P("depth", "angle", None, "tile", None),
        P("depth", "angle", None, "tile", None),
        P("depth", None, "angle", None, "tile", None),
        P("angle", "tile", None),
        P("angle"),
        P("angle", None),
    )
    out_specs = (
        P("depth", "angle", None, "tile", None),
        P("depth", "angle", None, "tile", None),
        P("depth", None, None, "tile", None),
    )
    return jax.shard_map(body, mesh=mesh, in_specs=in_specs, out_specs=out_specs, check_vma=False)
```

```python
import math

import jax
import numpy as np
import jax.numpy as jnp
from jax import lax
from jax.experimental import pallas as pl
from jax.experimental.pallas import tpu as pltpu
from jax.sharding import PartitionSpec as P

MARGIN = 32
TILTS = 61


fresnel = 24.0
slice_step = 6.0
tilt_step = math.pi / 90.0
highest = lax.Precision.HIGHEST
wave_precision = lax.Precision.HIGH


def padded_2(block, sides, width, periodic):
    for axis, dim in sides:
        count = lax.axis_size(axis)
        forward = [(i, i + 1) for i in range(count - 1)]
        if periodic:
            forward.append((count - 1, 0))
        backward = [(target, source) for source, target in forward]
        low = lax.ppermute(
            lax.slice_in_dim(block, block.shape[dim] - width, None, axis=dim), axis, forward
        )
        high = lax.ppermute(lax.slice_in_dim(block, 0, width, axis=dim), axis, backward)
        block = jnp.concatenate([low, block, high], axis=dim)
    return block


def contract(form, left, right):
    return jnp.einsum(form, left, right, precision=wave_precision)


def signed_freqs(length):
    ordinal = lax.iota(jnp.int32, length)
    signed = jnp.where(ordinal >= length // 2, ordinal - length, ordinal)
    return signed.astype(jnp.float32) / length


def halving_allreduce(value, axis):
    count = lax.axis_size(axis)
    if count == 1:
        return value
    if count & (count - 1) or value.shape[-2] % count:
        return lax.psum(value, axis)
    index = lax.axis_index(axis)
    steps = count.bit_length() - 1
    dim = value.ndim - 2
    held = value
    for k in range(steps):
        bit = (index >> k) & 1
        size = held.shape[dim] // 2
        low = lax.slice_in_dim(held, 0, size, axis=dim)
        high = lax.slice_in_dim(held, size, None, axis=dim)
        keep = jnp.where(bit == 0, low, high)
        give = jnp.where(bit == 0, high, low)
        pairs = [(j, j ^ (1 << k)) for j in range(count)]
        held = keep + lax.ppermute(give, axis, pairs)
    for k in reversed(range(steps)):
        bit = (index >> k) & 1
        pairs = [(j, j ^ (1 << k)) for j in range(count)]
        other = lax.ppermute(held, axis, pairs)
        held = jnp.where(
            bit == 0,
            jnp.concatenate([held, other], axis=dim),
            jnp.concatenate([other, held], axis=dim),
        )
    return held


def table_kernel(
    tilt_ref,
    position_ref,
    first_ref,
    grid_ref,
    phase_ref,
    rows_fwd_ref,
    rows_back_ref,
    cols_fwd_ref,
    cols_back_ref,
    cosine_ref,
    sine_ref,
):
    cosine_ref[...] = jnp.cos(phase_ref[...])
    sine_ref[...] = jnp.sin(phase_ref[...])
    angle_count = rows_fwd_ref.shape[0]
    length = grid_ref.shape[0]
    core_size = rows_fwd_ref.shape[-1]
    width = grid_ref.shape[1] // 2
    lane = lax.broadcasted_iota(jnp.int32, (1, length), 1)
    signed = jnp.where(lane >= length // 2, lane - length, lane)
    frequency = signed.astype(jnp.float32) / length
    base_phase = -math.pi * fresnel * frequency * frequency
    column = lax.broadcasted_iota(jnp.int32, (core_size, core_size), 1)
    low_mask = column >= core_size - MARGIN
    high_mask = column < MARGIN
    outputs = (rows_fwd_ref, rows_back_ref, cols_fwd_ref, cols_back_ref)
    first = jnp.full((1, length), first_ref[0], jnp.int32).astype(jnp.float32)
    for a in range(angle_count):
        tilt = jnp.full((1, length), tilt_ref[a], jnp.int32).astype(jnp.float32)
        tilt_angle = (tilt - (TILTS - 1) / 2.0) * tilt_step
        drift = slice_step * (jnp.sin(tilt_angle) / jnp.cos(tilt_angle))
        shift_rows = jnp.full((1, length), position_ref[2 * a], jnp.int32).astype(jnp.float32) * first
        shift_cols = drift + jnp.full((1, length), position_ref[2 * a + 1], jnp.int32).astype(
            jnp.float32
        ) * first
        row_line = base_phase - 2.0 * math.pi * frequency * shift_rows
        col_line = base_phase - 2.0 * math.pi * frequency * shift_cols
        lines = jnp.concatenate([row_line, -row_line, col_line, -col_line], axis=0)
        both = jnp.concatenate([jnp.cos(lines), jnp.sin(lines)], axis=0)
        product = jnp.dot(both, grid_ref[...], precision=highest, preferred_element_type=jnp.float32)
        count = 4
        cos_cos = product[:count, :width]
        cos_sin = product[:count, width:]
        sin_cos = product[count:, :width]
        sin_sin = product[count:, width:]
        q_real = (cos_cos + sin_sin) * (1.0 / length)
        q_imag = (sin_cos - cos_sin) * (1.0 / length)

        def rolled(line, shift):
            wide = jnp.broadcast_to(line, (core_size, width))
            return pltpu.roll(wide, shift, 1, stride=1, stride_axis=0)

        for t in range(count):
            parts = []
            for q in (q_real, q_imag):
                line = q[t : t + 1, :]
                if t < 2:
                    inner = rolled(line, 0)[:, :core_size]
                    low = rolled(line, core_size)[:, :core_size]
                    high = rolled(line, width - core_size)[:, :core_size]
                    folded = inner + jnp.where(low_mask, low, 0.0) + jnp.where(high_mask, high, 0.0)
                    parts.append(folded)
                else:
                    parts.append(rolled(line, MARGIN)[:, :length])
            real, imag = parts
            out = outputs[t]
            if t < 2:
                out[a, 0] = real + imag
                out[a, 1] = real
                out[a, 2] = imag
            else:
                out[a, 0] = real
                out[a, 1] = imag - real
                out[a, 2] = real + imag


def build_tables(tilt_index, positions, is_first, phase_plane, core_size, length):
    angle_count = tilt_index.shape[0]
    width = ((2 * length + 127) // 128) * 128
    ids = np.arange(length)[:, None] * np.arange(width)[None, :] % length
    angle = 2.0 * np.pi / length * ids
    grid = jnp.asarray(np.concatenate([np.cos(angle), np.sin(angle)], axis=1), jnp.float32)
    rows = jax.ShapeDtypeStruct((angle_count, 3, core_size, core_size), jnp.float32)
    cols = jax.ShapeDtypeStruct((angle_count, 3, core_size, length), jnp.float32)
    plane = jax.ShapeDtypeStruct(phase_plane.shape, jnp.float32)
    in_vmem = pl.BlockSpec(memory_space=pltpu.VMEM)
    return pl.pallas_call(
        table_kernel,
        out_shape=(rows, rows, cols, cols, plane, plane),
        in_specs=[
            pl.BlockSpec(memory_space=pltpu.SMEM),
            pl.BlockSpec(memory_space=pltpu.SMEM),
            pl.BlockSpec(memory_space=pltpu.SMEM),
            in_vmem,
            in_vmem,
        ],
        out_specs=tuple(pl.BlockSpec(memory_space=pltpu.VMEM) for _ in range(6)),
    )(tilt_index, positions.reshape(-1), is_first.astype(jnp.int32).reshape(1), grid, phase_plane)


def apply_operator(wave, padded_cols, row_table, col_table):
    wave_real = wave[:, 0]
    wave_imag = wave[:, 1]
    first = contract("ajl,alk->ajk", row_table[:, 0], wave_real)
    second = contract("ajl,alk->ajk", row_table[:, 1], wave_imag - wave_real)
    third = contract("ajl,alk->ajk", row_table[:, 2], wave_real + wave_imag)
    half = jnp.stack([first - third, first + second], axis=1)
    half = padded_cols(half)
    half_real = half[:, 0]
    half_imag = half[:, 1]
    first = contract("ajk,aik->aji", half_real + half_imag, col_table[:, 0])
    second = contract("ajk,aik->aji", half_real, col_table[:, 1])
    third = contract("ajk,aik->aji", half_imag, col_table[:, 2])
    return jnp.stack([first - third, first + second], axis=1)


def body(probe, phase, forward_in, adjoint_in, held_waves, measured, tilt_index, positions):
    core_size = phase.shape[-1]
    length = core_size + 2 * MARGIN
    angle_count = forward_in.shape[1]
    section = lax.axis_index("depth")
    sections = lax.axis_size("depth")
    is_first = section == 0
    rows_fwd, rows_back, cols_fwd, cols_back, cosine, sine_part = build_tables(
        tilt_index, positions, is_first, phase[0, 0], core_size, length
    )

    outgoing = jnp.concatenate([adjoint_in, forward_in], axis=0)
    received = padded_2(outgoing, (("depth", 0),), 1, False)
    probe_wave = probe.astype(jnp.float32)[None]
    wavefield = jnp.where(is_first, probe_wave, received[0])
    exit_wave = held_waves[0, 1].astype(jnp.float32)
    intensity = exit_wave[:, 0] * exit_wave[:, 0] + exit_wave[:, 1] * exit_wave[:, 1]
    residual = (intensity - measured)[:, None] * exit_wave
    returning = jnp.where(section == sections - 1, residual, received[3])
    transmitted = jnp.stack(
        [
            cosine * wavefield[:, 0] - sine_part * wavefield[:, 1],
            cosine * wavefield[:, 1] + sine_part * wavefield[:, 0],
        ],
        axis=1,
    )

    def side_halo(field):
        count = lax.axis_size("tile")
        if count > 2:
            return padded_2(field, (("tile", 3),), MARGIN, True)
        width = field.shape[3]
        edges = jnp.concatenate([field[..., :MARGIN], field[..., width - MARGIN :]], axis=3)
        if count == 2:
            edges = lax.ppermute(edges, "tile", [(0, 1), (1, 0)])
        return jnp.concatenate([edges[..., MARGIN:], field, edges[..., :MARGIN]], axis=3)

    spread = apply_operator(returning, side_halo, rows_back, cols_back)
    held_field = held_waves[0, 0].astype(jnp.float32)
    grad_real = spread[:, 0] * held_field[:, 0] + spread[:, 1] * held_field[:, 1]
    grad_imag = spread[:, 1] * held_field[:, 0] - spread[:, 0] * held_field[:, 1]
    gradient_term = jnp.stack([jnp.sum(grad_real, axis=0), jnp.sum(grad_imag, axis=0)])
    summed = halving_allreduce(gradient_term, "angle")
    returning = jnp.stack(
        [
            cosine * spread[:, 0] + sine_part * spread[:, 1],
            cosine * spread[:, 1] - sine_part * spread[:, 0],
        ],
        axis=1,
    )
    wavefield = apply_operator(transmitted, side_halo, rows_fwd, cols_fwd)
    return (wavefield[None], returning[None], summed[None, None])


def solution(mesh):
    in_specs = (
        P(None, "tile", None),
        P("depth", None, "tile", None),
        P("depth", "angle", None, "tile", None),
        P("depth", "angle", None, "tile", None),
        P("depth", None, "angle", None, "tile", None),
        P("angle", "tile", None),
        P("angle"),
        P("angle", None),
    )
    out_specs = (
        P("depth", "angle", None, "tile", None),
        P("depth", "angle", None, "tile", None),
        P("depth", None, None, "tile", None),
    )
    return jax.shard_map(body, mesh=mesh, in_specs=in_specs, out_specs=out_specs, check_vma=False)
```

```python
import math

import jax
import numpy as np
import jax.numpy as jnp
from jax import lax
from jax.experimental import pallas as pl
from jax.experimental.pallas import tpu as pltpu
from jax.sharding import PartitionSpec as P

MARGIN = 32
TILTS = 61


fresnel = 24.0
slice_step = 6.0
tilt_step = math.pi / 90.0
highest = lax.Precision.HIGHEST
wave_precision = lax.Precision.HIGH


def padded_2(block, sides, width, periodic):
    for axis, dim in sides:
        count = lax.axis_size(axis)
        forward = [(i, i + 1) for i in range(count - 1)]
        if periodic:
            forward.append((count - 1, 0))
        backward = [(target, source) for source, target in forward]
        low = lax.ppermute(
            lax.slice_in_dim(block, block.shape[dim] - width, None, axis=dim), axis, forward
        )
        high = lax.ppermute(lax.slice_in_dim(block, 0, width, axis=dim), axis, backward)
        block = jnp.concatenate([low, block, high], axis=dim)
    return block


def contract(form, left, right):
    return jnp.einsum(form, left, right, precision=wave_precision)


def signed_freqs(length):
    ordinal = lax.iota(jnp.int32, length)
    signed = jnp.where(ordinal >= length // 2, ordinal - length, ordinal)
    return signed.astype(jnp.float32) / length


def halving_allreduce(value, axis):
    count = lax.axis_size(axis)
    if count == 1:
        return value
    if count & (count - 1) or value.shape[-2] % count:
        return lax.psum(value, axis)
    index = lax.axis_index(axis)
    steps = count.bit_length() - 1
    dim = value.ndim - 2
    held = value
    for k in range(steps):
        bit = (index >> k) & 1
        size = held.shape[dim] // 2
        low = lax.slice_in_dim(held, 0, size, axis=dim)
        high = lax.slice_in_dim(held, size, None, axis=dim)
        keep = jnp.where(bit == 0, low, high)
        give = jnp.where(bit == 0, high, low)
        pairs = [(j, j ^ (1 << k)) for j in range(count)]
        held = keep + lax.ppermute(give, axis, pairs)
    for k in reversed(range(steps)):
        bit = (index >> k) & 1
        pairs = [(j, j ^ (1 << k)) for j in range(count)]
        other = lax.ppermute(held, axis, pairs)
        held = jnp.where(
            bit == 0,
            jnp.concatenate([held, other], axis=dim),
            jnp.concatenate([other, held], axis=dim),
        )
    return held


def exchange_allreduce(value, axis):
    count = lax.axis_size(axis)
    if count == 1:
        return value
    dim = value.ndim - 2
    rows = value.shape[dim]
    if rows % count:
        return lax.psum(value, axis)
    blocks = jnp.stack(jnp.split(value, count, axis=dim))
    gathered = lax.all_to_all(blocks, axis, 0, 0)
    share = jnp.sum(gathered, axis=0)
    spread = jnp.broadcast_to(share[None], (count,) + share.shape)
    everyone = lax.all_to_all(spread, axis, 0, 0)
    return jnp.concatenate([everyone[j] for j in range(count)], axis=dim)


def table_kernel(
    tilt_ref, position_ref, first_ref, grid_ref, rows_fwd_ref, rows_back_ref, cols_fwd_ref, cols_back_ref
):
    angle_count = rows_fwd_ref.shape[0]
    length = grid_ref.shape[0]
    core_size = rows_fwd_ref.shape[-1]
    width = grid_ref.shape[1] // 2
    lane = lax.broadcasted_iota(jnp.int32, (1, length), 1)
    signed = jnp.where(lane >= length // 2, lane - length, lane)
    frequency = signed.astype(jnp.float32) / length
    base_phase = -math.pi * fresnel * frequency * frequency
    column = lax.broadcasted_iota(jnp.int32, (core_size, core_size), 1)
    low_mask = column >= core_size - MARGIN
    high_mask = column < MARGIN
    outputs = (rows_fwd_ref, rows_back_ref, cols_fwd_ref, cols_back_ref)
    first = jnp.full((1, length), first_ref[0], jnp.int32).astype(jnp.float32)
    for a in range(angle_count):
        tilt = jnp.full((1, length), tilt_ref[a], jnp.int32).astype(jnp.float32)
        tilt_angle = (tilt - (TILTS - 1) / 2.0) * tilt_step
        drift = slice_step * (jnp.sin(tilt_angle) / jnp.cos(tilt_angle))
        shift_rows = jnp.full((1, length), position_ref[2 * a], jnp.int32).astype(jnp.float32) * first
        shift_cols = drift + jnp.full((1, length), position_ref[2 * a + 1], jnp.int32).astype(
            jnp.float32
        ) * first
        row_line = base_phase - 2.0 * math.pi * frequency * shift_rows
        col_line = base_phase - 2.0 * math.pi * frequency * shift_cols
        lines = jnp.concatenate([row_line, -row_line, col_line, -col_line], axis=0)
        both = jnp.concatenate([jnp.cos(lines), jnp.sin(lines)], axis=0)
        product = jnp.dot(both, grid_ref[...], precision=highest, preferred_element_type=jnp.float32)
        count = 4
        cos_cos = product[:count, :width]
        cos_sin = product[:count, width:]
        sin_cos = product[count:, :width]
        sin_sin = product[count:, width:]
        q_real = (cos_cos + sin_sin) * (1.0 / length)
        q_imag = (sin_cos - cos_sin) * (1.0 / length)

        def rolled(line, shift):
            wide = jnp.broadcast_to(line, (core_size, width))
            return pltpu.roll(wide, shift, 1, stride=1, stride_axis=0)

        for t in range(count):
            parts = []
            for q in (q_real, q_imag):
                line = q[t : t + 1, :]
                if t < 2:
                    inner = rolled(line, 0)[:, :core_size]
                    low = rolled(line, core_size)[:, :core_size]
                    high = rolled(line, width - core_size)[:, :core_size]
                    folded = inner + jnp.where(low_mask, low, 0.0) + jnp.where(high_mask, high, 0.0)
                    parts.append(folded)
                else:
                    parts.append(rolled(line, MARGIN)[:, :length])
            real, imag = parts
            out = outputs[t]
            if t < 2:
                out[a, 0] = real + imag
                out[a, 1] = real
                out[a, 2] = imag
            else:
                out[a, 0] = real
                out[a, 1] = imag - real
                out[a, 2] = real + imag


def build_tables(tilt_index, positions, is_first, core_size, length):
    angle_count = tilt_index.shape[0]
    width = ((2 * length + 127) // 128) * 128
    ids = np.arange(length)[:, None] * np.arange(width)[None, :] % length
    angle = 2.0 * np.pi / length * ids
    grid = jnp.asarray(np.concatenate([np.cos(angle), np.sin(angle)], axis=1), jnp.float32)
    rows = jax.ShapeDtypeStruct((angle_count, 3, core_size, core_size), jnp.float32)
    cols = jax.ShapeDtypeStruct((angle_count, 3, core_size, length), jnp.float32)
    return pl.pallas_call(
        table_kernel,
        out_shape=(rows, rows, cols, cols),
        in_specs=[
            pl.BlockSpec(memory_space=pltpu.SMEM),
            pl.BlockSpec(memory_space=pltpu.SMEM),
            pl.BlockSpec(memory_space=pltpu.SMEM),
            pl.BlockSpec(memory_space=pltpu.VMEM),
        ],
    )(tilt_index, positions.reshape(-1), is_first.astype(jnp.int32).reshape(1), grid)


def apply_operator(wave, padded_cols, row_table, col_table):
    wave_real = wave[:, 0]
    wave_imag = wave[:, 1]
    first = contract("ajl,alk->ajk", row_table[:, 0], wave_real)
    second = contract("ajl,alk->ajk", row_table[:, 1], wave_imag - wave_real)
    third = contract("ajl,alk->ajk", row_table[:, 2], wave_real + wave_imag)
    half = jnp.stack([first - third, first + second], axis=1)
    half = padded_cols(half)
    half_real = half[:, 0]
    half_imag = half[:, 1]
    first = contract("ajk,aik->aji", half_real + half_imag, col_table[:, 0])
    second = contract("ajk,aik->aji", half_real, col_table[:, 1])
    third = contract("ajk,aik->aji", half_imag, col_table[:, 2])
    return jnp.stack([first - third, first + second], axis=1)


def body(probe, phase, forward_in, adjoint_in, held_waves, measured, tilt_index, positions):
    core_size = phase.shape[-1]
    length = core_size + 2 * MARGIN
    angle_count = forward_in.shape[1]
    section = lax.axis_index("depth")
    sections = lax.axis_size("depth")
    is_first = section == 0
    rows_fwd, rows_back, cols_fwd, cols_back = build_tables(
        tilt_index, positions, is_first, core_size, length
    )

    cosine = jnp.cos(phase[0, 0])
    sine_part = jnp.sin(phase[0, 0])
    outgoing = jnp.concatenate([adjoint_in, forward_in], axis=0)
    received = padded_2(outgoing, (("depth", 0),), 1, False)
    probe_wave = probe.astype(jnp.float32)[None]
    wavefield = jnp.where(is_first, probe_wave, received[0])
    exit_wave = held_waves[0, 1].astype(jnp.float32)
    intensity = exit_wave[:, 0] * exit_wave[:, 0] + exit_wave[:, 1] * exit_wave[:, 1]
    residual = (intensity - measured)[:, None] * exit_wave
    returning = jnp.where(section == sections - 1, residual, received[3])
    transmitted = jnp.stack(
        [
            cosine * wavefield[:, 0] - sine_part * wavefield[:, 1],
            cosine * wavefield[:, 1] + sine_part * wavefield[:, 0],
        ],
        axis=1,
    )

    def side_halo(field):
        count = lax.axis_size("tile")
        if count > 2:
            return padded_2(field, (("tile", 3),), MARGIN, True)
        width = field.shape[3]
        edges = jnp.concatenate([field[..., :MARGIN], field[..., width - MARGIN :]], axis=3)
        if count == 2:
            edges = lax.ppermute(edges, "tile", [(0, 1), (1, 0)])
        return jnp.concatenate([edges[..., MARGIN:], field, edges[..., :MARGIN]], axis=3)

    spread = apply_operator(returning, side_halo, rows_back, cols_back)
    held_field = held_waves[0, 0].astype(jnp.float32)
    grad_real = spread[:, 0] * held_field[:, 0] + spread[:, 1] * held_field[:, 1]
    grad_imag = spread[:, 1] * held_field[:, 0] - spread[:, 0] * held_field[:, 1]
    gradient_term = jnp.stack([jnp.sum(grad_real, axis=0), jnp.sum(grad_imag, axis=0)])
    summed = exchange_allreduce(gradient_term, "angle")
    returning = jnp.stack(
        [
            cosine * spread[:, 0] + sine_part * spread[:, 1],
            cosine * spread[:, 1] - sine_part * spread[:, 0],
        ],
        axis=1,
    )
    wavefield = apply_operator(transmitted, side_halo, rows_fwd, cols_fwd)
    return (wavefield[None], returning[None], summed[None, None])


def solution(mesh):
    in_specs = (
        P(None, "tile", None),
        P("depth", None, "tile", None),
        P("depth", "angle", None, "tile", None),
        P("depth", "angle", None, "tile", None),
        P("depth", None, "angle", None, "tile", None),
        P("angle", "tile", None),
        P("angle"),
        P("angle", None),
    )
    out_specs = (
        P("depth", "angle", None, "tile", None),
        P("depth", "angle", None, "tile", None),
        P("depth", None, None, "tile", None),
    )
    return jax.shard_map(body, mesh=mesh, in_specs=in_specs, out_specs=out_specs, check_vma=False)
```

```python
import math

import jax
import numpy as np
import jax.numpy as jnp
from jax import lax
from jax.experimental import pallas as pl
from jax.experimental.pallas import tpu as pltpu
from jax.sharding import PartitionSpec as P

MARGIN = 32
TILTS = 61


fresnel = 24.0
slice_step = 6.0
tilt_step = math.pi / 90.0
highest = lax.Precision.HIGHEST
wave_precision = lax.Precision.HIGH


def padded_2(block, sides, width, periodic):
    for axis, dim in sides:
        count = lax.axis_size(axis)
        forward = [(i, i + 1) for i in range(count - 1)]
        if periodic:
            forward.append((count - 1, 0))
        backward = [(target, source) for source, target in forward]
        low = lax.ppermute(
            lax.slice_in_dim(block, block.shape[dim] - width, None, axis=dim), axis, forward
        )
        high = lax.ppermute(lax.slice_in_dim(block, 0, width, axis=dim), axis, backward)
        block = jnp.concatenate([low, block, high], axis=dim)
    return block


def contract(form, left, right):
    return jnp.einsum(form, left, right, precision=wave_precision)


def signed_freqs(length):
    ordinal = lax.iota(jnp.int32, length)
    signed = jnp.where(ordinal >= length // 2, ordinal - length, ordinal)
    return signed.astype(jnp.float32) / length


def halving_allreduce(value, axis):
    count = lax.axis_size(axis)
    if count == 1:
        return value
    if count & (count - 1) or value.shape[-2] % count:
        return lax.psum(value, axis)
    index = lax.axis_index(axis)
    steps = count.bit_length() - 1
    dim = value.ndim - 2
    held = value
    for k in range(steps):
        bit = (index >> k) & 1
        size = held.shape[dim] // 2
        low = lax.slice_in_dim(held, 0, size, axis=dim)
        high = lax.slice_in_dim(held, size, None, axis=dim)
        keep = jnp.where(bit == 0, low, high)
        give = jnp.where(bit == 0, high, low)
        pairs = [(j, j ^ (1 << k)) for j in range(count)]
        held = keep + lax.ppermute(give, axis, pairs)
    for k in reversed(range(steps)):
        bit = (index >> k) & 1
        pairs = [(j, j ^ (1 << k)) for j in range(count)]
        other = lax.ppermute(held, axis, pairs)
        held = jnp.where(
            bit == 0,
            jnp.concatenate([held, other], axis=dim),
            jnp.concatenate([other, held], axis=dim),
        )
    return held


def table_kernel(
    tilt_ref, position_ref, first_ref, grid_ref, rows_fwd_ref, rows_back_ref, cols_fwd_ref, cols_back_ref
):
    angle_count = rows_fwd_ref.shape[0]
    length = grid_ref.shape[0]
    core_size = rows_fwd_ref.shape[-1]
    width = grid_ref.shape[1] // 2
    lane = lax.broadcasted_iota(jnp.int32, (1, length), 1)
    signed = jnp.where(lane >= length // 2, lane - length, lane)
    frequency = signed.astype(jnp.float32) / length
    base_phase = -math.pi * fresnel * frequency * frequency
    column = lax.broadcasted_iota(jnp.int32, (core_size, core_size), 1)
    low_mask = column >= core_size - MARGIN
    high_mask = column < MARGIN
    outputs = (rows_fwd_ref, rows_back_ref, cols_fwd_ref, cols_back_ref)
    first = jnp.full((1, length), first_ref[0], jnp.int32).astype(jnp.float32)
    for a in range(angle_count):
        tilt = jnp.full((1, length), tilt_ref[a], jnp.int32).astype(jnp.float32)
        tilt_angle = (tilt - (TILTS - 1) / 2.0) * tilt_step
        drift = slice_step * (jnp.sin(tilt_angle) / jnp.cos(tilt_angle))
        shift_rows = jnp.full((1, length), position_ref[2 * a], jnp.int32).astype(jnp.float32) * first
        shift_cols = drift + jnp.full((1, length), position_ref[2 * a + 1], jnp.int32).astype(
            jnp.float32
        ) * first
        row_line = base_phase - 2.0 * math.pi * frequency * shift_rows
        col_line = base_phase - 2.0 * math.pi * frequency * shift_cols
        lines = jnp.concatenate([row_line, -row_line, col_line, -col_line], axis=0)
        both = jnp.concatenate([jnp.cos(lines), jnp.sin(lines)], axis=0)
        product = jnp.dot(both, grid_ref[...], precision=highest, preferred_element_type=jnp.float32)
        count = 4
        cos_cos = product[:count, :width]
        cos_sin = product[:count, width:]
        sin_cos = product[count:, :width]
        sin_sin = product[count:, width:]
        q_real = (cos_cos + sin_sin) * (1.0 / length)
        q_imag = (sin_cos - cos_sin) * (1.0 / length)

        def rolled(line, shift):
            wide = jnp.broadcast_to(line, (core_size, width))
            return pltpu.roll(wide, shift, 1, stride=1, stride_axis=0)

        for t in range(count):
            parts = []
            for q in (q_real, q_imag):
                line = q[t : t + 1, :]
                if t < 2:
                    inner = rolled(line, 0)[:, :core_size]
                    low = rolled(line, core_size)[:, :core_size]
                    high = rolled(line, width - core_size)[:, :core_size]
                    folded = inner + jnp.where(low_mask, low, 0.0) + jnp.where(high_mask, high, 0.0)
                    parts.append(folded)
                else:
                    parts.append(rolled(line, MARGIN)[:, :length])
            real, imag = parts
            out = outputs[t]
            if t < 2:
                out[a, 0] = real + imag
                out[a, 1] = real
                out[a, 2] = imag
            else:
                out[a, 0] = real
                out[a, 1] = imag - real
                out[a, 2] = real + imag


def build_tables(tilt_index, positions, is_first, core_size, length):
    angle_count = tilt_index.shape[0]
    width = ((2 * length + 127) // 128) * 128
    ids = np.arange(length)[:, None] * np.arange(width)[None, :] % length
    angle = 2.0 * np.pi / length * ids
    grid = jnp.asarray(np.concatenate([np.cos(angle), np.sin(angle)], axis=1), jnp.float32)
    rows = jax.ShapeDtypeStruct((angle_count, 3, core_size, core_size), jnp.float32)
    cols = jax.ShapeDtypeStruct((angle_count, 3, core_size, length), jnp.float32)
    return pl.pallas_call(
        table_kernel,
        out_shape=(rows, rows, cols, cols),
        in_specs=[
            pl.BlockSpec(memory_space=pltpu.SMEM),
            pl.BlockSpec(memory_space=pltpu.SMEM),
            pl.BlockSpec(memory_space=pltpu.SMEM),
            pl.BlockSpec(memory_space=pltpu.VMEM),
        ],
    )(tilt_index, positions.reshape(-1), is_first.astype(jnp.int32).reshape(1), grid)


def apply_operator(wave, padded_cols, row_table, col_table):
    wave_real = wave[:, 0]
    wave_imag = wave[:, 1]
    first = contract("ajl,alk->ajk", row_table[:, 0], wave_real)
    second = contract("ajl,alk->ajk", row_table[:, 1], wave_imag - wave_real)
    third = contract("ajl,alk->ajk", row_table[:, 2], wave_real + wave_imag)
    half = jnp.stack([first - third, first + second], axis=1)
    half = padded_cols(half)
    half_real = half[:, 0]
    half_imag = half[:, 1]
    first = contract("ajk,aik->aji", half_real + half_imag, col_table[:, 0])
    second = contract("ajk,aik->aji", half_real, col_table[:, 1])
    third = contract("ajk,aik->aji", half_imag, col_table[:, 2])
    return jnp.stack([first - third, first + second], axis=1)


def body(probe, phase, forward_in, adjoint_in, held_waves, measured, tilt_index, positions):
    core_size = phase.shape[-1]
    length = core_size + 2 * MARGIN
    angle_count = forward_in.shape[1]
    section = lax.axis_index("depth")
    sections = lax.axis_size("depth")
    is_first = section == 0
    rows_fwd, rows_back, cols_fwd, cols_back = build_tables(
        tilt_index, positions, is_first, core_size, length
    )

    cosine = jnp.cos(phase[0, 0])
    sine_part = jnp.sin(phase[0, 0])
    down = [(i + 1, i) for i in range(sections - 1)]
    up = [(i, i + 1) for i in range(sections - 1)]
    received_back = lax.ppermute(adjoint_in[0], "depth", down)
    exit_wave = held_waves[0, 1].astype(jnp.float32)
    intensity = exit_wave[:, 0] * exit_wave[:, 0] + exit_wave[:, 1] * exit_wave[:, 1]
    residual = (intensity - measured)[:, None] * exit_wave
    returning = jnp.where(section == sections - 1, residual, received_back)
    def side_halo(field):
        count = lax.axis_size("tile")
        if count > 2:
            return padded_2(field, (("tile", 3),), MARGIN, True)
        width = field.shape[3]
        edges = jnp.concatenate([field[..., :MARGIN], field[..., width - MARGIN :]], axis=3)
        if count == 2:
            edges = lax.ppermute(edges, "tile", [(0, 1), (1, 0)])
        return jnp.concatenate([edges[..., MARGIN:], field, edges[..., :MARGIN]], axis=3)

    spread = apply_operator(returning, side_halo, rows_back, cols_back)
    held_field = held_waves[0, 0].astype(jnp.float32)
    grad_real = spread[:, 0] * held_field[:, 0] + spread[:, 1] * held_field[:, 1]
    grad_imag = spread[:, 1] * held_field[:, 0] - spread[:, 0] * held_field[:, 1]
    gradient_term = jnp.stack([jnp.sum(grad_real, axis=0), jnp.sum(grad_imag, axis=0)])
    gradient_term, forward_in = lax.optimization_barrier((gradient_term, forward_in))
    summed = halving_allreduce(gradient_term, "angle")
    received_fwd = lax.ppermute(forward_in[0], "depth", up)
    probe_wave = probe.astype(jnp.float32)[None]
    wavefield = jnp.where(is_first, probe_wave, received_fwd)
    transmitted = jnp.stack(
        [
            cosine * wavefield[:, 0] - sine_part * wavefield[:, 1],
            cosine * wavefield[:, 1] + sine_part * wavefield[:, 0],
        ],
        axis=1,
    )
    returning = jnp.stack(
        [
            cosine * spread[:, 0] + sine_part * spread[:, 1],
            cosine * spread[:, 1] - sine_part * spread[:, 0],
        ],
        axis=1,
    )
    wavefield = apply_operator(transmitted, side_halo, rows_fwd, cols_fwd)
    return (wavefield[None], returning[None], summed[None, None])


def solution(mesh):
    in_specs = (
        P(None, "tile", None),
        P("depth", None, "tile", None),
        P("depth", "angle", None, "tile", None),
        P("depth", "angle", None, "tile", None),
        P("depth", None, "angle", None, "tile", None),
        P("angle", "tile", None),
        P("angle"),
        P("angle", None),
    )
    out_specs = (
        P("depth", "angle", None, "tile", None),
        P("depth", "angle", None, "tile", None),
        P("depth", None, None, "tile", None),
    )
    return jax.shard_map(body, mesh=mesh, in_specs=in_specs, out_specs=out_specs, check_vma=False)
```

```python
import functools
import math

import jax
import numpy as np
import jax.numpy as jnp
from jax import lax
from jax.experimental import pallas as pl
from jax.experimental.pallas import tpu as pltpu
from jax.sharding import PartitionSpec as P

MARGIN = 32
TILTS = 61


fresnel = 24.0
slice_step = 6.0
tilt_step = math.pi / 90.0
highest = lax.Precision.HIGHEST
wave_precision = lax.Precision.HIGH


def padded_2(block, sides, width, periodic):
    for axis, dim in sides:
        count = lax.axis_size(axis)
        forward = [(i, i + 1) for i in range(count - 1)]
        if periodic:
            forward.append((count - 1, 0))
        backward = [(target, source) for source, target in forward]
        low = lax.ppermute(
            lax.slice_in_dim(block, block.shape[dim] - width, None, axis=dim), axis, forward
        )
        high = lax.ppermute(lax.slice_in_dim(block, 0, width, axis=dim), axis, backward)
        block = jnp.concatenate([low, block, high], axis=dim)
    return block


def contract(form, left, right):
    return jnp.einsum(form, left, right, precision=wave_precision)


def signed_freqs(length):
    ordinal = lax.iota(jnp.int32, length)
    signed = jnp.where(ordinal >= length // 2, ordinal - length, ordinal)
    return signed.astype(jnp.float32) / length


def halving_allreduce(value, axis):
    count = lax.axis_size(axis)
    if count == 1:
        return value
    if count & (count - 1) or value.shape[-2] % count:
        return lax.psum(value, axis)
    index = lax.axis_index(axis)
    steps = count.bit_length() - 1
    dim = value.ndim - 2
    held = value
    for k in range(steps):
        bit = (index >> k) & 1
        size = held.shape[dim] // 2
        low = lax.slice_in_dim(held, 0, size, axis=dim)
        high = lax.slice_in_dim(held, size, None, axis=dim)
        keep = jnp.where(bit == 0, low, high)
        give = jnp.where(bit == 0, high, low)
        pairs = [(j, j ^ (1 << k)) for j in range(count)]
        held = keep + lax.ppermute(give, axis, pairs)
    for k in reversed(range(steps)):
        bit = (index >> k) & 1
        pairs = [(j, j ^ (1 << k)) for j in range(count)]
        other = lax.ppermute(held, axis, pairs)
        held = jnp.where(
            bit == 0,
            jnp.concatenate([held, other], axis=dim),
            jnp.concatenate([other, held], axis=dim),
        )
    return held


def table_kernel(sign, tilt_ref, position_ref, first_ref, grid_ref, rows_ref, cols_ref):
    angle_count = rows_ref.shape[0]
    length = grid_ref.shape[0]
    core_size = rows_ref.shape[-1]
    width = grid_ref.shape[1] // 2
    lane = lax.broadcasted_iota(jnp.int32, (1, length), 1)
    signed = jnp.where(lane >= length // 2, lane - length, lane)
    frequency = signed.astype(jnp.float32) / length
    base_phase = -math.pi * fresnel * frequency * frequency
    column = lax.broadcasted_iota(jnp.int32, (core_size, core_size), 1)
    low_mask = column >= core_size - MARGIN
    high_mask = column < MARGIN
    outputs = (rows_ref, cols_ref)
    first = jnp.full((1, length), first_ref[0], jnp.int32).astype(jnp.float32)
    for a in range(angle_count):
        tilt = jnp.full((1, length), tilt_ref[a], jnp.int32).astype(jnp.float32)
        tilt_angle = (tilt - (TILTS - 1) / 2.0) * tilt_step
        drift = slice_step * (jnp.sin(tilt_angle) / jnp.cos(tilt_angle))
        shift_rows = jnp.full((1, length), position_ref[2 * a], jnp.int32).astype(jnp.float32) * first
        shift_cols = drift + jnp.full((1, length), position_ref[2 * a + 1], jnp.int32).astype(
            jnp.float32
        ) * first
        row_line = base_phase - 2.0 * math.pi * frequency * shift_rows
        col_line = base_phase - 2.0 * math.pi * frequency * shift_cols
        lines = sign * jnp.concatenate([row_line, col_line], axis=0)
        both = jnp.concatenate([jnp.cos(lines), jnp.sin(lines)], axis=0)
        product = jnp.dot(both, grid_ref[...], precision=highest, preferred_element_type=jnp.float32)
        count = 2
        cos_cos = product[:count, :width]
        cos_sin = product[:count, width:]
        sin_cos = product[count:, :width]
        sin_sin = product[count:, width:]
        q_real = (cos_cos + sin_sin) * (1.0 / length)
        q_imag = (sin_cos - cos_sin) * (1.0 / length)

        def rolled(line, shift):
            wide = jnp.broadcast_to(line, (core_size, width))
            return pltpu.roll(wide, shift, 1, stride=1, stride_axis=0)

        for t in range(count):
            parts = []
            for q in (q_real, q_imag):
                line = q[t : t + 1, :]
                if t < 1:
                    inner = rolled(line, 0)[:, :core_size]
                    low = rolled(line, core_size)[:, :core_size]
                    high = rolled(line, width - core_size)[:, :core_size]
                    folded = inner + jnp.where(low_mask, low, 0.0) + jnp.where(high_mask, high, 0.0)
                    parts.append(folded)
                else:
                    parts.append(rolled(line, MARGIN)[:, :length])
            real, imag = parts
            out = outputs[t]
            if t < 1:
                out[a, 0] = real + imag
                out[a, 1] = real
                out[a, 2] = imag
            else:
                out[a, 0] = real
                out[a, 1] = imag - real
                out[a, 2] = real + imag


def build_tables(sign, tilt_index, positions, is_first, core_size, length):
    angle_count = tilt_index.shape[0]
    width = ((2 * length + 127) // 128) * 128
    ids = np.arange(length)[:, None] * np.arange(width)[None, :] % length
    angle = 2.0 * np.pi / length * ids
    grid = jnp.asarray(np.concatenate([np.cos(angle), np.sin(angle)], axis=1), jnp.float32)
    rows = jax.ShapeDtypeStruct((angle_count, 3, core_size, core_size), jnp.float32)
    cols = jax.ShapeDtypeStruct((angle_count, 3, core_size, length), jnp.float32)
    return pl.pallas_call(
        functools.partial(table_kernel, sign),
        out_shape=(rows, cols),
        in_specs=[
            pl.BlockSpec(memory_space=pltpu.SMEM),
            pl.BlockSpec(memory_space=pltpu.SMEM),
            pl.BlockSpec(memory_space=pltpu.SMEM),
            pl.BlockSpec(memory_space=pltpu.VMEM),
        ],
    )(tilt_index, positions.reshape(-1), is_first.astype(jnp.int32).reshape(1), grid)


def apply_operator(wave, padded_cols, row_table, col_table):
    wave_real = wave[:, 0]
    wave_imag = wave[:, 1]
    first = contract("ajl,alk->ajk", row_table[:, 0], wave_real)
    second = contract("ajl,alk->ajk", row_table[:, 1], wave_imag - wave_real)
    third = contract("ajl,alk->ajk", row_table[:, 2], wave_real + wave_imag)
    half = jnp.stack([first - third, first + second], axis=1)
    half = padded_cols(half)
    half_real = half[:, 0]
    half_imag = half[:, 1]
    first = contract("ajk,aik->aji", half_real + half_imag, col_table[:, 0])
    second = contract("ajk,aik->aji", half_real, col_table[:, 1])
    third = contract("ajk,aik->aji", half_imag, col_table[:, 2])
    return jnp.stack([first - third, first + second], axis=1)


def body(probe, phase, forward_in, adjoint_in, held_waves, measured, tilt_index, positions):
    core_size = phase.shape[-1]
    length = core_size + 2 * MARGIN
    angle_count = forward_in.shape[1]
    section = lax.axis_index("depth")
    sections = lax.axis_size("depth")
    is_first = section == 0
    rows_back, cols_back = build_tables(-1.0, tilt_index, positions, is_first, core_size, length)

    cosine = jnp.cos(phase[0, 0])
    sine_part = jnp.sin(phase[0, 0])
    down = [(i + 1, i) for i in range(sections - 1)]
    up = [(i, i + 1) for i in range(sections - 1)]
    received_back = lax.ppermute(adjoint_in[0], "depth", down)
    exit_wave = held_waves[0, 1].astype(jnp.float32)
    intensity = exit_wave[:, 0] * exit_wave[:, 0] + exit_wave[:, 1] * exit_wave[:, 1]
    residual = (intensity - measured)[:, None] * exit_wave
    returning = jnp.where(section == sections - 1, residual, received_back)
    def side_halo(field):
        count = lax.axis_size("tile")
        if count > 2:
            return padded_2(field, (("tile", 3),), MARGIN, True)
        width = field.shape[3]
        edges = jnp.concatenate([field[..., :MARGIN], field[..., width - MARGIN :]], axis=3)
        if count == 2:
            edges = lax.ppermute(edges, "tile", [(0, 1), (1, 0)])
        return jnp.concatenate([edges[..., MARGIN:], field, edges[..., :MARGIN]], axis=3)

    spread = apply_operator(returning, side_halo, rows_back, cols_back)
    held_field = held_waves[0, 0].astype(jnp.float32)
    grad_real = spread[:, 0] * held_field[:, 0] + spread[:, 1] * held_field[:, 1]
    grad_imag = spread[:, 1] * held_field[:, 0] - spread[:, 0] * held_field[:, 1]
    gradient_term = jnp.stack([jnp.sum(grad_real, axis=0), jnp.sum(grad_imag, axis=0)])
    gradient_term, forward_in, tilt_index = lax.optimization_barrier(
        (gradient_term, forward_in, tilt_index)
    )
    rows_fwd, cols_fwd = build_tables(1.0, tilt_index, positions, is_first, core_size, length)
    summed = halving_allreduce(gradient_term, "angle")
    received_fwd = lax.ppermute(forward_in[0], "depth", up)
    probe_wave = probe.astype(jnp.float32)[None]
    wavefield = jnp.where(is_first, probe_wave, received_fwd)
    transmitted = jnp.stack(
        [
            cosine * wavefield[:, 0] - sine_part * wavefield[:, 1],
            cosine * wavefield[:, 1] + sine_part * wavefield[:, 0],
        ],
        axis=1,
    )
    returning = jnp.stack(
        [
            cosine * spread[:, 0] + sine_part * spread[:, 1],
            cosine * spread[:, 1] - sine_part * spread[:, 0],
        ],
        axis=1,
    )
    wavefield = apply_operator(transmitted, side_halo, rows_fwd, cols_fwd)
    return (wavefield[None], returning[None], summed[None, None])


def solution(mesh):
    in_specs = (
        P(None, "tile", None),
        P("depth", None, "tile", None),
        P("depth", "angle", None, "tile", None),
        P("depth", "angle", None, "tile", None),
        P("depth", None, "angle", None, "tile", None),
        P("angle", "tile", None),
        P("angle"),
        P("angle", None),
    )
    out_specs = (
        P("depth", "angle", None, "tile", None),
        P("depth", "angle", None, "tile", None),
        P("depth", None, None, "tile", None),
    )
    return jax.shard_map(body, mesh=mesh, in_specs=in_specs, out_specs=out_specs, check_vma=False)
```

```python
import functools
import math

import jax
import numpy as np
import jax.numpy as jnp
from jax import lax
from jax.experimental import pallas as pl
from jax.experimental.pallas import tpu as pltpu
from jax.sharding import PartitionSpec as P

MARGIN = 32
TILTS = 61


fresnel = 24.0
slice_step = 6.0
tilt_step = math.pi / 90.0
highest = lax.Precision.HIGHEST
wave_precision = lax.Precision.HIGH


def padded_2(block, sides, width, periodic):
    for axis, dim in sides:
        count = lax.axis_size(axis)
        forward = [(i, i + 1) for i in range(count - 1)]
        if periodic:
            forward.append((count - 1, 0))
        backward = [(target, source) for source, target in forward]
        low = lax.ppermute(
            lax.slice_in_dim(block, block.shape[dim] - width, None, axis=dim), axis, forward
        )
        high = lax.ppermute(lax.slice_in_dim(block, 0, width, axis=dim), axis, backward)
        block = jnp.concatenate([low, block, high], axis=dim)
    return block


def contract(form, left, right):
    return jnp.einsum(form, left, right, precision=wave_precision)


def signed_freqs(length):
    ordinal = lax.iota(jnp.int32, length)
    signed = jnp.where(ordinal >= length // 2, ordinal - length, ordinal)
    return signed.astype(jnp.float32) / length


def halving_allreduce(value, axis):
    count = lax.axis_size(axis)
    if count == 1:
        return value
    if count & (count - 1) or value.shape[-2] % count:
        return lax.psum(value, axis)
    index = lax.axis_index(axis)
    steps = count.bit_length() - 1
    dim = value.ndim - 2
    held = value
    for k in range(steps):
        bit = (index >> k) & 1
        size = held.shape[dim] // 2
        low = lax.slice_in_dim(held, 0, size, axis=dim)
        high = lax.slice_in_dim(held, size, None, axis=dim)
        keep = jnp.where(bit == 0, low, high)
        give = jnp.where(bit == 0, high, low)
        pairs = [(j, j ^ (1 << k)) for j in range(count)]
        held = keep + lax.ppermute(give, axis, pairs)
    for k in reversed(range(steps)):
        bit = (index >> k) & 1
        pairs = [(j, j ^ (1 << k)) for j in range(count)]
        other = lax.ppermute(held, axis, pairs)
        held = jnp.where(
            bit == 0,
            jnp.concatenate([held, other], axis=dim),
            jnp.concatenate([other, held], axis=dim),
        )
    return held


def table_kernel(sign, tilt_ref, position_ref, first_ref, grid_ref, rows_ref, cols_ref):
    angle_count = rows_ref.shape[0]
    length = grid_ref.shape[0]
    core_size = rows_ref.shape[-1]
    period = grid_ref.shape[1] // 2
    width = 2 * period
    lane = lax.broadcasted_iota(jnp.int32, (1, length), 1)
    signed = jnp.where(lane >= length // 2, lane - length, lane)
    frequency = signed.astype(jnp.float32) / length
    base_phase = -math.pi * fresnel * frequency * frequency
    column = lax.broadcasted_iota(jnp.int32, (core_size, core_size), 1)
    low_mask = column >= core_size - MARGIN
    high_mask = column < MARGIN
    outputs = (rows_ref, cols_ref)
    first = jnp.full((1, length), first_ref[0], jnp.int32).astype(jnp.float32)
    for a in range(angle_count):
        tilt = jnp.full((1, length), tilt_ref[a], jnp.int32).astype(jnp.float32)
        tilt_angle = (tilt - (TILTS - 1) / 2.0) * tilt_step
        drift = slice_step * (jnp.sin(tilt_angle) / jnp.cos(tilt_angle))
        shift_rows = jnp.full((1, length), position_ref[2 * a], jnp.int32).astype(jnp.float32) * first
        shift_cols = drift + jnp.full((1, length), position_ref[2 * a + 1], jnp.int32).astype(
            jnp.float32
        ) * first
        row_line = base_phase - 2.0 * math.pi * frequency * shift_rows
        col_line = base_phase - 2.0 * math.pi * frequency * shift_cols
        lines = sign * jnp.concatenate([row_line, col_line], axis=0)
        both = jnp.concatenate([jnp.cos(lines), jnp.sin(lines)], axis=0)
        product = jnp.dot(
            both, grid_ref[...], precision=lax.Precision.HIGH, preferred_element_type=jnp.float32
        )
        count = 2
        cos_cos = product[:count, :period]
        cos_sin = product[:count, period:]
        sin_cos = product[count:, :period]
        sin_sin = product[count:, period:]
        q_real = (cos_cos + sin_sin) * (1.0 / length)
        q_imag = (sin_cos - cos_sin) * (1.0 / length)
        q_real = jnp.concatenate([q_real, q_real], axis=1)
        q_imag = jnp.concatenate([q_imag, q_imag], axis=1)

        def rolled(line, shift):
            wide = jnp.broadcast_to(line, (core_size, width))
            return pltpu.roll(wide, shift, 1, stride=1, stride_axis=0)

        for t in range(count):
            parts = []
            for q in (q_real, q_imag):
                line = q[t : t + 1, :]
                if t < 1:
                    inner = rolled(line, 0)[:, :core_size]
                    low = rolled(line, core_size)[:, :core_size]
                    high = rolled(line, width - core_size)[:, :core_size]
                    folded = inner + jnp.where(low_mask, low, 0.0) + jnp.where(high_mask, high, 0.0)
                    parts.append(folded)
                else:
                    parts.append(rolled(line, MARGIN)[:, :length])
            real, imag = parts
            out = outputs[t]
            if t < 1:
                out[a, 0] = real + imag
                out[a, 1] = real
                out[a, 2] = imag
            else:
                out[a, 0] = real
                out[a, 1] = imag - real
                out[a, 2] = real + imag


def build_tables(sign, tilt_index, positions, is_first, core_size, length):
    angle_count = tilt_index.shape[0]
    ids = np.arange(length)[:, None] * np.arange(length)[None, :] % length
    angle = 2.0 * np.pi / length * ids
    grid = jnp.asarray(np.concatenate([np.cos(angle), np.sin(angle)], axis=1), jnp.float32)
    rows = jax.ShapeDtypeStruct((angle_count, 3, core_size, core_size), jnp.float32)
    cols = jax.ShapeDtypeStruct((angle_count, 3, core_size, length), jnp.float32)
    return pl.pallas_call(
        functools.partial(table_kernel, sign),
        out_shape=(rows, cols),
        in_specs=[
            pl.BlockSpec(memory_space=pltpu.SMEM),
            pl.BlockSpec(memory_space=pltpu.SMEM),
            pl.BlockSpec(memory_space=pltpu.SMEM),
            pl.BlockSpec(memory_space=pltpu.VMEM),
        ],
    )(tilt_index, positions.reshape(-1), is_first.astype(jnp.int32).reshape(1), grid)


def apply_operator(wave, padded_cols, row_table, col_table):
    wave_real = wave[:, 0]
    wave_imag = wave[:, 1]
    first = contract("ajl,alk->ajk", row_table[:, 0], wave_real)
    second = contract("ajl,alk->ajk", row_table[:, 1], wave_imag - wave_real)
    third = contract("ajl,alk->ajk", row_table[:, 2], wave_real + wave_imag)
    half = jnp.stack([first - third, first + second], axis=1)
    half = padded_cols(half)
    half_real = half[:, 0]
    half_imag = half[:, 1]
    first = contract("ajk,aik->aji", half_real + half_imag, col_table[:, 0])
    second = contract("ajk,aik->aji", half_real, col_table[:, 1])
    third = contract("ajk,aik->aji", half_imag, col_table[:, 2])
    return jnp.stack([first - third, first + second], axis=1)


def body(probe, phase, forward_in, adjoint_in, held_waves, measured, tilt_index, positions):
    core_size = phase.shape[-1]
    length = core_size + 2 * MARGIN
    angle_count = forward_in.shape[1]
    section = lax.axis_index("depth")
    sections = lax.axis_size("depth")
    is_first = section == 0
    rows_back, cols_back = build_tables(-1.0, tilt_index, positions, is_first, core_size, length)

    cosine = jnp.cos(phase[0, 0])
    sine_part = jnp.sin(phase[0, 0])
    down = [(i + 1, i) for i in range(sections - 1)]
    up = [(i, i + 1) for i in range(sections - 1)]
    received_back = lax.ppermute(adjoint_in[0], "depth", down)
    exit_wave = held_waves[0, 1].astype(jnp.float32)
    intensity = exit_wave[:, 0] * exit_wave[:, 0] + exit_wave[:, 1] * exit_wave[:, 1]
    residual = (intensity - measured)[:, None] * exit_wave
    returning = jnp.where(section == sections - 1, residual, received_back)
    def side_halo(field):
        count = lax.axis_size("tile")
        if count > 2:
            return padded_2(field, (("tile", 3),), MARGIN, True)
        width = field.shape[3]
        edges = jnp.concatenate([field[..., :MARGIN], field[..., width - MARGIN :]], axis=3)
        if count == 2:
            edges = lax.ppermute(edges, "tile", [(0, 1), (1, 0)])
        return jnp.concatenate([edges[..., MARGIN:], field, edges[..., :MARGIN]], axis=3)

    spread = apply_operator(returning, side_halo, rows_back, cols_back)
    held_field = held_waves[0, 0].astype(jnp.float32)
    grad_real = spread[:, 0] * held_field[:, 0] + spread[:, 1] * held_field[:, 1]
    grad_imag = spread[:, 1] * held_field[:, 0] - spread[:, 0] * held_field[:, 1]
    gradient_term = jnp.stack([jnp.sum(grad_real, axis=0), jnp.sum(grad_imag, axis=0)])
    gradient_term, forward_in, tilt_index = lax.optimization_barrier(
        (gradient_term, forward_in, tilt_index)
    )
    rows_fwd, cols_fwd = build_tables(1.0, tilt_index, positions, is_first, core_size, length)
    summed = halving_allreduce(gradient_term, "angle")
    received_fwd = lax.ppermute(forward_in[0], "depth", up)
    probe_wave = probe.astype(jnp.float32)[None]
    wavefield = jnp.where(is_first, probe_wave, received_fwd)
    transmitted = jnp.stack(
        [
            cosine * wavefield[:, 0] - sine_part * wavefield[:, 1],
            cosine * wavefield[:, 1] + sine_part * wavefield[:, 0],
        ],
        axis=1,
    )
    returning = jnp.stack(
        [
            cosine * spread[:, 0] + sine_part * spread[:, 1],
            cosine * spread[:, 1] - sine_part * spread[:, 0],
        ],
        axis=1,
    )
    wavefield = apply_operator(transmitted, side_halo, rows_fwd, cols_fwd)
    return (wavefield[None], returning[None], summed[None, None])


def solution(mesh):
    in_specs = (
        P(None, "tile", None),
        P("depth", None, "tile", None),
        P("depth", "angle", None, "tile", None),
        P("depth", "angle", None, "tile", None),
        P("depth", None, "angle", None, "tile", None),
        P("angle", "tile", None),
        P("angle"),
        P("angle", None),
    )
    out_specs = (
        P("depth", "angle", None, "tile", None),
        P("depth", "angle", None, "tile", None),
        P("depth", None, None, "tile", None),
    )
    return jax.shard_map(body, mesh=mesh, in_specs=in_specs, out_specs=out_specs, check_vma=False)
```

```python
import functools
import math

import jax
import numpy as np
import jax.numpy as jnp
from jax import lax
from jax.experimental import pallas as pl
from jax.experimental.pallas import tpu as pltpu
from jax.sharding import PartitionSpec as P

MARGIN = 32
TILTS = 61


fresnel = 24.0
slice_step = 6.0
tilt_step = math.pi / 90.0
highest = lax.Precision.HIGHEST
wave_precision = lax.Precision.HIGH


def padded_2(block, sides, width, periodic):
    for axis, dim in sides:
        count = lax.axis_size(axis)
        forward = [(i, i + 1) for i in range(count - 1)]
        if periodic:
            forward.append((count - 1, 0))
        backward = [(target, source) for source, target in forward]
        low = lax.ppermute(
            lax.slice_in_dim(block, block.shape[dim] - width, None, axis=dim), axis, forward
        )
        high = lax.ppermute(lax.slice_in_dim(block, 0, width, axis=dim), axis, backward)
        block = jnp.concatenate([low, block, high], axis=dim)
    return block


def contract(form, left, right):
    return jnp.einsum(form, left, right, precision=wave_precision)


def signed_freqs(length):
    ordinal = lax.iota(jnp.int32, length)
    signed = jnp.where(ordinal >= length // 2, ordinal - length, ordinal)
    return signed.astype(jnp.float32) / length


def halving_allreduce(value, axis):
    count = lax.axis_size(axis)
    if count == 1:
        return value
    if count & (count - 1) or value.shape[-2] % count:
        return lax.psum(value, axis)
    index = lax.axis_index(axis)
    steps = count.bit_length() - 1
    dim = value.ndim - 2
    held = value
    for k in range(steps):
        bit = (index >> k) & 1
        size = held.shape[dim] // 2
        low = lax.slice_in_dim(held, 0, size, axis=dim)
        high = lax.slice_in_dim(held, size, None, axis=dim)
        keep = jnp.where(bit == 0, low, high)
        give = jnp.where(bit == 0, high, low)
        pairs = [(j, j ^ (1 << k)) for j in range(count)]
        held = keep + lax.ppermute(give, axis, pairs)
    for k in reversed(range(steps)):
        bit = (index >> k) & 1
        pairs = [(j, j ^ (1 << k)) for j in range(count)]
        other = lax.ppermute(held, axis, pairs)
        size = held.shape[dim]
        blank = jnp.zeros_like(held)
        placed = jnp.where(
            bit == 0,
            jnp.concatenate([held, blank], axis=dim),
            jnp.concatenate([blank, held], axis=dim),
        )
        held = lax.dynamic_update_slice_in_dim(placed, other, (1 - bit) * size, axis=dim)
    return held


def table_kernel(sign, tilt_ref, position_ref, first_ref, grid_ref, rows_ref, cols_ref):
    angle_count = rows_ref.shape[0]
    length = grid_ref.shape[0]
    core_size = rows_ref.shape[-1]
    period = grid_ref.shape[1] // 2
    width = 2 * period
    lane = lax.broadcasted_iota(jnp.int32, (1, length), 1)
    signed = jnp.where(lane >= length // 2, lane - length, lane)
    frequency = signed.astype(jnp.float32) / length
    base_phase = -math.pi * fresnel * frequency * frequency
    column = lax.broadcasted_iota(jnp.int32, (core_size, core_size), 1)
    low_mask = column >= core_size - MARGIN
    high_mask = column < MARGIN
    outputs = (rows_ref, cols_ref)
    first = jnp.full((1, length), first_ref[0], jnp.int32).astype(jnp.float32)
    for a in range(angle_count):
        tilt = jnp.full((1, length), tilt_ref[a], jnp.int32).astype(jnp.float32)
        tilt_angle = (tilt - (TILTS - 1) / 2.0) * tilt_step
        drift = slice_step * (jnp.sin(tilt_angle) / jnp.cos(tilt_angle))
        shift_rows = jnp.full((1, length), position_ref[2 * a], jnp.int32).astype(jnp.float32) * first
        shift_cols = drift + jnp.full((1, length), position_ref[2 * a + 1], jnp.int32).astype(
            jnp.float32
        ) * first
        row_line = base_phase - 2.0 * math.pi * frequency * shift_rows
        col_line = base_phase - 2.0 * math.pi * frequency * shift_cols
        lines = sign * jnp.concatenate([row_line, col_line], axis=0)
        both = jnp.concatenate([jnp.cos(lines), jnp.sin(lines)], axis=0)
        product = jnp.dot(
            both, grid_ref[...], precision=lax.Precision.HIGH, preferred_element_type=jnp.float32
        )
        count = 2
        cos_cos = product[:count, :period]
        cos_sin = product[:count, period:]
        sin_cos = product[count:, :period]
        sin_sin = product[count:, period:]
        q_real = (cos_cos + sin_sin) * (1.0 / length)
        q_imag = (sin_cos - cos_sin) * (1.0 / length)
        q_real = jnp.concatenate([q_real, q_real], axis=1)
        q_imag = jnp.concatenate([q_imag, q_imag], axis=1)

        def rolled(line, shift):
            wide = jnp.broadcast_to(line, (core_size, width))
            return pltpu.roll(wide, shift, 1, stride=1, stride_axis=0)

        for t in range(count):
            parts = []
            for q in (q_real, q_imag):
                line = q[t : t + 1, :]
                if t < 1:
                    inner = rolled(line, 0)[:, :core_size]
                    low = rolled(line, core_size)[:, :core_size]
                    high = rolled(line, width - core_size)[:, :core_size]
                    folded = inner + jnp.where(low_mask, low, 0.0) + jnp.where(high_mask, high, 0.0)
                    parts.append(folded)
                else:
                    parts.append(rolled(line, MARGIN)[:, :length])
            real, imag = parts
            out = outputs[t]
            if t < 1:
                out[a, 0] = real + imag
                out[a, 1] = real
                out[a, 2] = imag
            else:
                out[a, 0] = real
                out[a, 1] = imag - real
                out[a, 2] = real + imag


def build_tables(sign, tilt_index, positions, is_first, core_size, length):
    angle_count = tilt_index.shape[0]
    ids = np.arange(length)[:, None] * np.arange(length)[None, :] % length
    angle = 2.0 * np.pi / length * ids
    grid = jnp.asarray(np.concatenate([np.cos(angle), np.sin(angle)], axis=1), jnp.float32)
    rows = jax.ShapeDtypeStruct((angle_count, 3, core_size, core_size), jnp.float32)
    cols = jax.ShapeDtypeStruct((angle_count, 3, core_size, length), jnp.float32)
    return pl.pallas_call(
        functools.partial(table_kernel, sign),
        out_shape=(rows, cols),
        in_specs=[
            pl.BlockSpec(memory_space=pltpu.SMEM),
            pl.BlockSpec(memory_space=pltpu.SMEM),
            pl.BlockSpec(memory_space=pltpu.SMEM),
            pl.BlockSpec(memory_space=pltpu.VMEM),
        ],
    )(tilt_index, positions.reshape(-1), is_first.astype(jnp.int32).reshape(1), grid)


def apply_operator(wave, padded_cols, row_table, col_table):
    wave_real = wave[:, 0]
    wave_imag = wave[:, 1]
    first = contract("ajl,alk->ajk", row_table[:, 0], wave_real)
    second = contract("ajl,alk->ajk", row_table[:, 1], wave_imag - wave_real)
    third = contract("ajl,alk->ajk", row_table[:, 2], wave_real + wave_imag)
    half = jnp.stack([first - third, first + second], axis=1)
    half = padded_cols(half)
    half_real = half[:, 0]
    half_imag = half[:, 1]
    first = contract("ajk,aik->aji", half_real + half_imag, col_table[:, 0])
    second = contract("ajk,aik->aji", half_real, col_table[:, 1])
    third = contract("ajk,aik->aji", half_imag, col_table[:, 2])
    return jnp.stack([first - third, first + second], axis=1)


def body(probe, phase, forward_in, adjoint_in, held_waves, measured, tilt_index, positions):
    core_size = phase.shape[-1]
    length = core_size + 2 * MARGIN
    angle_count = forward_in.shape[1]
    section = lax.axis_index("depth")
    sections = lax.axis_size("depth")
    is_first = section == 0
    rows_back, cols_back = build_tables(-1.0, tilt_index, positions, is_first, core_size, length)

    cosine = jnp.cos(phase[0, 0])
    sine_part = jnp.sin(phase[0, 0])
    down = [(i + 1, i) for i in range(sections - 1)]
    up = [(i, i + 1) for i in range(sections - 1)]
    received_back = lax.ppermute(adjoint_in[0], "depth", down)
    exit_wave = held_waves[0, 1].astype(jnp.float32)
    intensity = exit_wave[:, 0] * exit_wave[:, 0] + exit_wave[:, 1] * exit_wave[:, 1]
    residual = (intensity - measured)[:, None] * exit_wave
    returning = jnp.where(section == sections - 1, residual, received_back)
    def side_halo(field):
        count = lax.axis_size("tile")
        if count > 2:
            return padded_2(field, (("tile", 3),), MARGIN, True)
        width = field.shape[3]
        edges = jnp.concatenate([field[..., :MARGIN], field[..., width - MARGIN :]], axis=3)
        if count == 2:
            edges = lax.ppermute(edges, "tile", [(0, 1), (1, 0)])
        return jnp.concatenate([edges[..., MARGIN:], field, edges[..., :MARGIN]], axis=3)

    spread = apply_operator(returning, side_halo, rows_back, cols_back)
    held_field = held_waves[0, 0].astype(jnp.float32)
    grad_real = spread[:, 0] * held_field[:, 0] + spread[:, 1] * held_field[:, 1]
    grad_imag = spread[:, 1] * held_field[:, 0] - spread[:, 0] * held_field[:, 1]
    gradient_term = jnp.stack([jnp.sum(grad_real, axis=0), jnp.sum(grad_imag, axis=0)])
    gradient_term, forward_in, tilt_index = lax.optimization_barrier(
        (gradient_term, forward_in, tilt_index)
    )
    rows_fwd, cols_fwd = build_tables(1.0, tilt_index, positions, is_first, core_size, length)
    summed = halving_allreduce(gradient_term, "angle")
    received_fwd = lax.ppermute(forward_in[0], "depth", up)
    probe_wave = probe.astype(jnp.float32)[None]
    wavefield = jnp.where(is_first, probe_wave, received_fwd)
    transmitted = jnp.stack(
        [
            cosine * wavefield[:, 0] - sine_part * wavefield[:, 1],
            cosine * wavefield[:, 1] + sine_part * wavefield[:, 0],
        ],
        axis=1,
    )
    returning = jnp.stack(
        [
            cosine * spread[:, 0] + sine_part * spread[:, 1],
            cosine * spread[:, 1] - sine_part * spread[:, 0],
        ],
        axis=1,
    )
    wavefield = apply_operator(transmitted, side_halo, rows_fwd, cols_fwd)
    return (wavefield[None], returning[None], summed[None, None])


def solution(mesh):
    in_specs = (
        P(None, "tile", None),
        P("depth", None, "tile", None),
        P("depth", "angle", None, "tile", None),
        P("depth", "angle", None, "tile", None),
        P("depth", None, "angle", None, "tile", None),
        P("angle", "tile", None),
        P("angle"),
        P("angle", None),
    )
    out_specs = (
        P("depth", "angle", None, "tile", None),
        P("depth", "angle", None, "tile", None),
        P("depth", None, None, "tile", None),
    )
    return jax.shard_map(body, mesh=mesh, in_specs=in_specs, out_specs=out_specs, check_vma=False)
```

```python
import functools
import math

import jax
import numpy as np
import jax.numpy as jnp
from jax import lax
from jax.experimental import pallas as pl
from jax.experimental.pallas import tpu as pltpu
from jax.sharding import PartitionSpec as P

MARGIN = 32
TILTS = 61


fresnel = 24.0
slice_step = 6.0
tilt_step = math.pi / 90.0
highest = lax.Precision.HIGHEST
wave_precision = lax.Precision.HIGH


def padded_2(block, sides, width, periodic):
    for axis, dim in sides:
        count = lax.axis_size(axis)
        forward = [(i, i + 1) for i in range(count - 1)]
        if periodic:
            forward.append((count - 1, 0))
        backward = [(target, source) for source, target in forward]
        low = lax.ppermute(
            lax.slice_in_dim(block, block.shape[dim] - width, None, axis=dim), axis, forward
        )
        high = lax.ppermute(lax.slice_in_dim(block, 0, width, axis=dim), axis, backward)
        block = jnp.concatenate([low, block, high], axis=dim)
    return block


def contract(form, left, right):
    return jnp.einsum(form, left, right, precision=wave_precision)


def signed_freqs(length):
    ordinal = lax.iota(jnp.int32, length)
    signed = jnp.where(ordinal >= length // 2, ordinal - length, ordinal)
    return signed.astype(jnp.float32) / length


def halving_allreduce(value, axis):
    count = lax.axis_size(axis)
    if count == 1:
        return value
    if count & (count - 1) or value.shape[-2] % count:
        return lax.psum(value, axis)
    index = lax.axis_index(axis)
    steps = count.bit_length() - 1
    dim = value.ndim - 2
    held = value
    for k in range(steps):
        bit = (index >> k) & 1
        size = held.shape[dim] // 2
        low = lax.slice_in_dim(held, 0, size, axis=dim)
        high = lax.slice_in_dim(held, size, None, axis=dim)
        keep = jnp.where(bit == 0, low, high)
        give = jnp.where(bit == 0, high, low)
        pairs = [(j, j ^ (1 << k)) for j in range(count)]
        held = keep + lax.ppermute(give, axis, pairs)
    for k in reversed(range(steps)):
        bit = (index >> k) & 1
        pairs = [(j, j ^ (1 << k)) for j in range(count)]
        other = lax.ppermute(held, axis, pairs)
        held = jnp.where(
            bit == 0,
            jnp.concatenate([held, other], axis=dim),
            jnp.concatenate([other, held], axis=dim),
        )
    return held


def table_kernel(sign, tilt_ref, position_ref, first_ref, grid_ref, rows_ref, cols_ref):
    angle_count = rows_ref.shape[0]
    length = grid_ref.shape[0]
    core_size = rows_ref.shape[-1]
    period = grid_ref.shape[1] // 2
    width = 2 * period
    lane = lax.broadcasted_iota(jnp.int32, (1, length), 1)
    signed = jnp.where(lane >= length // 2, lane - length, lane)
    frequency = signed.astype(jnp.float32) / length
    base_phase = -math.pi * fresnel * frequency * frequency
    column = lax.broadcasted_iota(jnp.int32, (core_size, core_size), 1)
    low_mask = column >= core_size - MARGIN
    high_mask = column < MARGIN
    outputs = (rows_ref, cols_ref)
    first = jnp.full((1, length), first_ref[0], jnp.int32).astype(jnp.float32)
    for a in range(angle_count):
        tilt = jnp.full((1, length), tilt_ref[a], jnp.int32).astype(jnp.float32)
        tilt_angle = (tilt - (TILTS - 1) / 2.0) * tilt_step
        drift = slice_step * (jnp.sin(tilt_angle) / jnp.cos(tilt_angle))
        shift_rows = jnp.full((1, length), position_ref[2 * a], jnp.int32).astype(jnp.float32) * first
        shift_cols = drift + jnp.full((1, length), position_ref[2 * a + 1], jnp.int32).astype(
            jnp.float32
        ) * first
        row_line = base_phase - 2.0 * math.pi * frequency * shift_rows
        col_line = base_phase - 2.0 * math.pi * frequency * shift_cols
        lines = sign * jnp.concatenate([row_line, col_line], axis=0)
        both = jnp.concatenate([jnp.cos(lines), jnp.sin(lines)], axis=0)
        product = jnp.dot(
            both, grid_ref[...], precision=lax.Precision.HIGH, preferred_element_type=jnp.float32
        )
        count = 2
        cos_cos = product[:count, :period]
        cos_sin = product[:count, period:]
        sin_cos = product[count:, :period]
        sin_sin = product[count:, period:]
        q_real = (cos_cos + sin_sin) * (1.0 / length)
        q_imag = (sin_cos - cos_sin) * (1.0 / length)
        q_real = jnp.concatenate([q_real, q_real], axis=1)
        q_imag = jnp.concatenate([q_imag, q_imag], axis=1)

        def rolled(line, shift):
            wide = jnp.broadcast_to(line, (core_size, width))
            return pltpu.roll(wide, shift, 1, stride=1, stride_axis=0)

        for t in range(count):
            parts = []
            for q in (q_real, q_imag):
                line = q[t : t + 1, :]
                if t < 1:
                    inner = rolled(line, 0)[:, :core_size]
                    low = rolled(line, core_size)[:, :core_size]
                    high = rolled(line, width - core_size)[:, :core_size]
                    folded = inner + jnp.where(low_mask, low, 0.0) + jnp.where(high_mask, high, 0.0)
                    parts.append(folded)
                else:
                    parts.append(rolled(line, MARGIN)[:, :length])
            real, imag = parts
            out = outputs[t]
            if t < 1:
                out[a, 0] = real + imag
                out[a, 1] = real
                out[a, 2] = imag
            else:
                out[a, 0] = real
                out[a, 1] = imag - real
                out[a, 2] = real + imag


def build_tables(sign, tilt_index, positions, is_first, core_size, length):
    angle_count = tilt_index.shape[0]
    ids = np.arange(length)[:, None] * np.arange(length)[None, :] % length
    angle = 2.0 * np.pi / length * ids
    grid = jnp.asarray(np.concatenate([np.cos(angle), np.sin(angle)], axis=1), jnp.float32)
    rows = jax.ShapeDtypeStruct((angle_count, 3, core_size, core_size), jnp.float32)
    cols = jax.ShapeDtypeStruct((angle_count, 3, core_size, length), jnp.float32)
    return pl.pallas_call(
        functools.partial(table_kernel, sign),
        out_shape=(rows, cols),
        in_specs=[
            pl.BlockSpec(memory_space=pltpu.SMEM),
            pl.BlockSpec(memory_space=pltpu.SMEM),
            pl.BlockSpec(memory_space=pltpu.SMEM),
            pl.BlockSpec(memory_space=pltpu.VMEM),
        ],
    )(tilt_index, positions.reshape(-1), is_first.astype(jnp.int32).reshape(1), grid)


def apply_rows(wave, row_table):
    wave_real = wave[:, 0]
    wave_imag = wave[:, 1]
    first = contract("ajl,alk->ajk", row_table[:, 0], wave_real)
    second = contract("ajl,alk->ajk", row_table[:, 1], wave_imag - wave_real)
    third = contract("ajl,alk->ajk", row_table[:, 2], wave_real + wave_imag)
    return jnp.stack([first - third, first + second], axis=1)


def apply_operator(wave, padded_cols, row_table, col_table):
    if lax.axis_size("tile") == 2:
        width = wave.shape[-1]
        edges = jnp.concatenate([wave[..., :MARGIN], wave[..., width - MARGIN :]], axis=-1)
        edges = lax.ppermute(apply_rows(edges, row_table), "tile", [(0, 1), (1, 0)])
        half = apply_rows(wave, row_table)
        half = jnp.concatenate([edges[..., MARGIN:], half, edges[..., :MARGIN]], axis=-1)
    else:
        half = padded_cols(apply_rows(wave, row_table))
    half_real = half[:, 0]
    half_imag = half[:, 1]
    first = contract("ajk,aik->aji", half_real + half_imag, col_table[:, 0])
    second = contract("ajk,aik->aji", half_real, col_table[:, 1])
    third = contract("ajk,aik->aji", half_imag, col_table[:, 2])
    return jnp.stack([first - third, first + second], axis=1)


def body(probe, phase, forward_in, adjoint_in, held_waves, measured, tilt_index, positions):
    core_size = phase.shape[-1]
    length = core_size + 2 * MARGIN
    angle_count = forward_in.shape[1]
    section = lax.axis_index("depth")
    sections = lax.axis_size("depth")
    is_first = section == 0
    rows_back, cols_back = build_tables(-1.0, tilt_index, positions, is_first, core_size, length)

    cosine = jnp.cos(phase[0, 0])
    sine_part = jnp.sin(phase[0, 0])
    down = [(i + 1, i) for i in range(sections - 1)]
    up = [(i, i + 1) for i in range(sections - 1)]
    received_back = lax.ppermute(adjoint_in[0], "depth", down)
    exit_wave = held_waves[0, 1].astype(jnp.float32)
    intensity = exit_wave[:, 0] * exit_wave[:, 0] + exit_wave[:, 1] * exit_wave[:, 1]
    residual = (intensity - measured)[:, None] * exit_wave
    returning = jnp.where(section == sections - 1, residual, received_back)
    def side_halo(field):
        count = lax.axis_size("tile")
        if count > 2:
            return padded_2(field, (("tile", 3),), MARGIN, True)
        width = field.shape[3]
        edges = jnp.concatenate([field[..., :MARGIN], field[..., width - MARGIN :]], axis=3)
        if count == 2:
            edges = lax.ppermute(edges, "tile", [(0, 1), (1, 0)])
        return jnp.concatenate([edges[..., MARGIN:], field, edges[..., :MARGIN]], axis=3)

    spread = apply_operator(returning, side_halo, rows_back, cols_back)
    held_field = held_waves[0, 0].astype(jnp.float32)
    grad_real = spread[:, 0] * held_field[:, 0] + spread[:, 1] * held_field[:, 1]
    grad_imag = spread[:, 1] * held_field[:, 0] - spread[:, 0] * held_field[:, 1]
    gradient_term = jnp.stack([jnp.sum(grad_real, axis=0), jnp.sum(grad_imag, axis=0)])
    gradient_term, forward_in, tilt_index = lax.optimization_barrier(
        (gradient_term, forward_in, tilt_index)
    )
    rows_fwd, cols_fwd = build_tables(1.0, tilt_index, positions, is_first, core_size, length)
    summed = halving_allreduce(gradient_term, "angle")
    received_fwd = lax.ppermute(forward_in[0], "depth", up)
    probe_wave = probe.astype(jnp.float32)[None]
    wavefield = jnp.where(is_first, probe_wave, received_fwd)
    transmitted = jnp.stack(
        [
            cosine * wavefield[:, 0] - sine_part * wavefield[:, 1],
            cosine * wavefield[:, 1] + sine_part * wavefield[:, 0],
        ],
        axis=1,
    )
    returning = jnp.stack(
        [
            cosine * spread[:, 0] + sine_part * spread[:, 1],
            cosine * spread[:, 1] - sine_part * spread[:, 0],
        ],
        axis=1,
    )
    wavefield = apply_operator(transmitted, side_halo, rows_fwd, cols_fwd)
    return (wavefield[None], returning[None], summed[None, None])


def solution(mesh):
    in_specs = (
        P(None, "tile", None),
        P("depth", None, "tile", None),
        P("depth", "angle", None, "tile", None),
        P("depth", "angle", None, "tile", None),
        P("depth", None, "angle", None, "tile", None),
        P("angle", "tile", None),
        P("angle"),
        P("angle", None),
    )
    out_specs = (
        P("depth", "angle", None, "tile", None),
        P("depth", "angle", None, "tile", None),
        P("depth", None, None, "tile", None),
    )
    return jax.shard_map(body, mesh=mesh, in_specs=in_specs, out_specs=out_specs, check_vma=False)
```

```python
import functools
import math

import jax
import numpy as np
import jax.numpy as jnp
from jax import lax
from jax.experimental import pallas as pl
from jax.experimental.pallas import tpu as pltpu
from jax.sharding import PartitionSpec as P

MARGIN = 32
TILTS = 61


fresnel = 24.0
slice_step = 6.0
tilt_step = math.pi / 90.0
highest = lax.Precision.HIGHEST
wave_precision = lax.Precision.HIGH


def padded_2(block, sides, width, periodic):
    for axis, dim in sides:
        count = lax.axis_size(axis)
        forward = [(i, i + 1) for i in range(count - 1)]
        if periodic:
            forward.append((count - 1, 0))
        backward = [(target, source) for source, target in forward]
        low = lax.ppermute(
            lax.slice_in_dim(block, block.shape[dim] - width, None, axis=dim), axis, forward
        )
        high = lax.ppermute(lax.slice_in_dim(block, 0, width, axis=dim), axis, backward)
        block = jnp.concatenate([low, block, high], axis=dim)
    return block


def contract(form, left, right):
    return jnp.einsum(form, left, right, precision=wave_precision)


def signed_freqs(length):
    ordinal = lax.iota(jnp.int32, length)
    signed = jnp.where(ordinal >= length // 2, ordinal - length, ordinal)
    return signed.astype(jnp.float32) / length


def halving_allreduce(value, axis):
    count = lax.axis_size(axis)
    if count == 1:
        return value
    if count & (count - 1) or value.shape[-2] % count:
        return lax.psum(value, axis)
    index = lax.axis_index(axis)
    steps = count.bit_length() - 1
    dim = value.ndim - 2
    held = value
    for k in range(steps):
        bit = (index >> k) & 1
        size = held.shape[dim] // 2
        low = lax.slice_in_dim(held, 0, size, axis=dim)
        high = lax.slice_in_dim(held, size, None, axis=dim)
        keep = jnp.where(bit == 0, low, high)
        give = jnp.where(bit == 0, high, low)
        pairs = [(j, j ^ (1 << k)) for j in range(count)]
        held = keep + lax.ppermute(give, axis, pairs)
    for k in reversed(range(steps)):
        bit = (index >> k) & 1
        pairs = [(j, j ^ (1 << k)) for j in range(count)]
        other = lax.ppermute(held, axis, pairs)
        held = jnp.where(
            bit == 0,
            jnp.concatenate([held, other], axis=dim),
            jnp.concatenate([other, held], axis=dim),
        )
    return held


def table_kernel(sign, tilt_ref, position_ref, first_ref, grid_ref, rows_ref, cols_ref):
    angle_count = rows_ref.shape[0]
    length = grid_ref.shape[0]
    core_size = rows_ref.shape[-1]
    period = grid_ref.shape[1] // 2
    width = 2 * period
    lane = lax.broadcasted_iota(jnp.int32, (1, length), 1)
    signed = jnp.where(lane >= length // 2, lane - length, lane)
    frequency = signed.astype(jnp.float32) / length
    base_phase = -math.pi * fresnel * frequency * frequency
    column = lax.broadcasted_iota(jnp.int32, (core_size, core_size), 1)
    low_mask = column >= core_size - MARGIN
    high_mask = column < MARGIN
    outputs = (rows_ref, cols_ref)
    first = jnp.full((1, length), first_ref[0], jnp.int32).astype(jnp.float32)
    for a in range(angle_count):
        tilt = jnp.full((1, length), tilt_ref[a], jnp.int32).astype(jnp.float32)
        tilt_angle = (tilt - (TILTS - 1) / 2.0) * tilt_step
        drift = slice_step * (jnp.sin(tilt_angle) / jnp.cos(tilt_angle))
        shift_rows = jnp.full((1, length), position_ref[2 * a], jnp.int32).astype(jnp.float32) * first
        shift_cols = drift + jnp.full((1, length), position_ref[2 * a + 1], jnp.int32).astype(
            jnp.float32
        ) * first
        row_line = base_phase - 2.0 * math.pi * frequency * shift_rows
        col_line = base_phase - 2.0 * math.pi * frequency * shift_cols
        lines = sign * jnp.concatenate([row_line, col_line], axis=0)
        both = jnp.concatenate([jnp.cos(lines), jnp.sin(lines)], axis=0)
        product = jnp.dot(
            both, grid_ref[...], precision=lax.Precision.HIGH, preferred_element_type=jnp.float32
        )
        count = 2
        cos_cos = product[:count, :period]
        cos_sin = product[:count, period:]
        sin_cos = product[count:, :period]
        sin_sin = product[count:, period:]
        q_real = (cos_cos + sin_sin) * (1.0 / length)
        q_imag = (sin_cos - cos_sin) * (1.0 / length)
        q_real = jnp.concatenate([q_real, q_real], axis=1)
        q_imag = jnp.concatenate([q_imag, q_imag], axis=1)

        def rolled(line, shift):
            wide = jnp.broadcast_to(line, (core_size, width))
            return pltpu.roll(wide, shift, 1, stride=1, stride_axis=0)

        for t in range(count):
            parts = []
            for q in (q_real, q_imag):
                line = q[t : t + 1, :]
                if t < 1:
                    inner = rolled(line, 0)[:, :core_size]
                    low = rolled(line, core_size)[:, :core_size]
                    high = rolled(line, width - core_size)[:, :core_size]
                    folded = inner + jnp.where(low_mask, low, 0.0) + jnp.where(high_mask, high, 0.0)
                    parts.append(folded)
                else:
                    parts.append(rolled(line, MARGIN)[:, :length])
            real, imag = parts
            out = outputs[t]
            if t < 1:
                out[a, 0] = real + imag
                out[a, 1] = real
                out[a, 2] = imag
            else:
                out[a, 0] = real
                out[a, 1] = imag - real
                out[a, 2] = real + imag


def build_tables(sign, tilt_index, positions, is_first, core_size, length):
    angle_count = tilt_index.shape[0]
    ids = np.arange(length)[:, None] * np.arange(length)[None, :] % length
    angle = 2.0 * np.pi / length * ids
    grid = jnp.asarray(np.concatenate([np.cos(angle), np.sin(angle)], axis=1), jnp.float32)
    rows = jax.ShapeDtypeStruct((angle_count, 3, core_size, core_size), jnp.float32)
    cols = jax.ShapeDtypeStruct((angle_count, 3, core_size, length), jnp.float32)
    return pl.pallas_call(
        functools.partial(table_kernel, sign),
        out_shape=(rows, cols),
        in_specs=[
            pl.BlockSpec(memory_space=pltpu.SMEM),
            pl.BlockSpec(memory_space=pltpu.SMEM),
            pl.BlockSpec(memory_space=pltpu.SMEM),
            pl.BlockSpec(memory_space=pltpu.VMEM),
        ],
    )(tilt_index, positions.reshape(-1), is_first.astype(jnp.int32).reshape(1), grid)


def apply_operator(wave, padded_cols, row_table, col_table):
    wave_real = wave[:, 0]
    wave_imag = wave[:, 1]
    first = contract("ajl,alk->ajk", row_table[:, 0], wave_real)
    second = contract("ajl,alk->ajk", row_table[:, 1], wave_imag - wave_real)
    third = contract("ajl,alk->ajk", row_table[:, 2], wave_real + wave_imag)
    half = jnp.stack([first - third, first + second], axis=1)
    half = padded_cols(half)
    half_real = half[:, 0]
    half_imag = half[:, 1]
    first = contract("ajk,aik->aji", half_real + half_imag, col_table[:, 0])
    second = contract("ajk,aik->aji", half_real, col_table[:, 1])
    third = contract("ajk,aik->aji", half_imag, col_table[:, 2])
    return jnp.stack([first - third, first + second], axis=1)


def body(probe, phase, forward_in, adjoint_in, held_waves, measured, tilt_index, positions):
    core_size = phase.shape[-1]
    length = core_size + 2 * MARGIN
    angle_count = forward_in.shape[1]
    section = lax.axis_index("depth")
    sections = lax.axis_size("depth")
    is_first = section == 0
    rows_back, cols_back = build_tables(-1.0, tilt_index, positions, is_first, core_size, length)

    cosine = jnp.cos(phase[0, 0])
    sine_part = jnp.sin(phase[0, 0])
    down = [(i + 1, i) for i in range(sections - 1)]
    up = [(i, i + 1) for i in range(sections - 1)]
    rows_back, cols_back, adjoint_in = lax.optimization_barrier((rows_back, cols_back, adjoint_in))
    received_back = lax.ppermute(adjoint_in[0], "depth", down)
    exit_wave = held_waves[0, 1].astype(jnp.float32)
    intensity = exit_wave[:, 0] * exit_wave[:, 0] + exit_wave[:, 1] * exit_wave[:, 1]
    residual = (intensity - measured)[:, None] * exit_wave
    returning = jnp.where(section == sections - 1, residual, received_back)
    def side_halo(field):
        count = lax.axis_size("tile")
        if count > 2:
            return padded_2(field, (("tile", 3),), MARGIN, True)
        width = field.shape[3]
        edges = jnp.concatenate([field[..., :MARGIN], field[..., width - MARGIN :]], axis=3)
        if count == 2:
            edges = lax.ppermute(edges, "tile", [(0, 1), (1, 0)])
        return jnp.concatenate([edges[..., MARGIN:], field, edges[..., :MARGIN]], axis=3)

    spread = apply_operator(returning, side_halo, rows_back, cols_back)
    held_field = held_waves[0, 0].astype(jnp.float32)
    grad_real = spread[:, 0] * held_field[:, 0] + spread[:, 1] * held_field[:, 1]
    grad_imag = spread[:, 1] * held_field[:, 0] - spread[:, 0] * held_field[:, 1]
    gradient_term = jnp.stack([jnp.sum(grad_real, axis=0), jnp.sum(grad_imag, axis=0)])
    gradient_term, forward_in, tilt_index = lax.optimization_barrier(
        (gradient_term, forward_in, tilt_index)
    )
    rows_fwd, cols_fwd = build_tables(1.0, tilt_index, positions, is_first, core_size, length)
    summed = halving_allreduce(gradient_term, "angle")
    received_fwd = lax.ppermute(forward_in[0], "depth", up)
    probe_wave = probe.astype(jnp.float32)[None]
    wavefield = jnp.where(is_first, probe_wave, received_fwd)
    transmitted = jnp.stack(
        [
            cosine * wavefield[:, 0] - sine_part * wavefield[:, 1],
            cosine * wavefield[:, 1] + sine_part * wavefield[:, 0],
        ],
        axis=1,
    )
    returning = jnp.stack(
        [
            cosine * spread[:, 0] + sine_part * spread[:, 1],
            cosine * spread[:, 1] - sine_part * spread[:, 0],
        ],
        axis=1,
    )
    wavefield = apply_operator(transmitted, side_halo, rows_fwd, cols_fwd)
    return (wavefield[None], returning[None], summed[None, None])


def solution(mesh):
    in_specs = (
        P(None, "tile", None),
        P("depth", None, "tile", None),
        P("depth", "angle", None, "tile", None),
        P("depth", "angle", None, "tile", None),
        P("depth", None, "angle", None, "tile", None),
        P("angle", "tile", None),
        P("angle"),
        P("angle", None),
    )
    out_specs = (
        P("depth", "angle", None, "tile", None),
        P("depth", "angle", None, "tile", None),
        P("depth", None, None, "tile", None),
    )
    return jax.shard_map(body, mesh=mesh, in_specs=in_specs, out_specs=out_specs, check_vma=False)
```
